128 devices in a mesh: gx: 16 (over y, z), gy: 8 (over x, core).
Axes of the slice: x: 4, y: 4, z: 4, core: 2. Of those that a mesh axis runs over, the one named last changes fastest.
Arguments:
- point_feats: bfloat16 [393216, 64], P(('gx', 'gy')), may hold values from -6 to 6
- point_dest: int32 [393216, 1], P(('gx', 'gy')), may hold values from 0 to 127; in each aligned block of 3072 rows (0 to 3071, 3072 to 6143, ...) at most 48 rows name the same one
- point_voxel: int32 [393216], P(('gx', 'gy')), may hold values from 0 to 767
- kernel_map: int32 [27, 98304], P(None, ('gx', 'gy')), may hold values from 0 to 1152, as said below
- border_list: int32 [32, 16, 24], P('gx', 'gy'), may hold values from 0 to 767, as said below
- conv_one: bfloat16 [27, 64, 64], replicated, may hold values from -0.15625 to 0.15625
- conv_two: bfloat16 [27, 64, 64], replicated, may hold values from -0.15625 to 0.15625
- gain_one: float32 [64], replicated, may hold values from 0.25 to 1.75
- gain_two: float32 [64], replicated, may hold values from 0.25 to 1.75
- decoder_in: bfloat16 [64, 128], replicated, may hold values from -0.75 to 0.75
- decoder_bias: float32 [128], replicated, may hold values from -3 to 3
- decoder_out: float32 [128], replicated, may hold values from -0.5 to 0.5
- target: float32 [98304], P(('gx', 'gy')), may hold values from -6 to 6
Outputs:
- sdf_values: float32 [98304], P(('gx', 'gy'))
- loss_value: float32 [], replicated
- grad_conv_one: float32 [27, 64, 64], replicated
- grad_conv_two: float32 [27, 64, 64], replicated
- grad_decoder_in: float32 [64, 128], replicated
- grad_decoder_bias: float32 [128], replicated
- grad_decoder_out: float32 [128], replicated
- grad_points: bfloat16 [393216, 64], P(('gx', 'gy'))
The draws below stay inside these ranges and needn't reach their ends.
Inputs may be any that keep to these rules, and one draw needn't show every extreme that they name: point_dest names the device gx index * 8 + gy index. Among the rows of one device no device is named by more than 48 rows, and some device is named by exactly 48. `kernel_map`: row k gives each voxel's neighbour at offset k as a row of its device's table: below 768 a local voxel, then 16 * 24 boundary rows, and 1152 the zero row. Offset k is the step (k // 9 - 1, k // 3 % 3 - 1, k % 3 - 1) along the first lateral direction, the second lateral direction and height; row (26) // 2 names the voxel itself. The maps are symmetric: where row k names local voxel u for voxel v, row 26 - k names v for u. Only a voxel listed at slot m of its brick's cell c in border_list names boundary rows, and then only slot m of the cell beside c in the step's lateral direction; the voxel at slot m of that cell names, in row 26 - k, slot m of cell c. A step with no lateral part names only local voxels or the zero row. `border_list`: local voxel rows of the owning device, distinct within a brick; the voxels listed for a brick's cell (2a + i, 2b + j) lie in its rows (2i + j) * 192 to (2i + j + 1) * 192 - 1.
All inputs are finite; a program needn't handle non-finite values.
Results may differ from the reference program's by a relative error of at most 0.011.
Values may be sent and summed in bfloat16 or wider, within the bound.
No kernel may reach another device: no remote copies, remote signals or barrier semaphores. Data moves between devices by JAX's collectives and lax.ppermute only.
A program may use at most 64 MiB of HBM per device.

```python
import math
import jax
import jax.numpy as jnp
import numpy as np
from jax import lax

C = 64
HID = 128
K = 27
V_DEV = 768
P_DEV = 3072
BND = 24
CAP = 48
V_TOTAL = 98304
P_TOTAL = 393216
N_GX = 16
N_GY = 8


def quadrant_rows(key):
    quarter = V_DEV // 4
    base_rows = jnp.broadcast_to(jnp.arange(quarter, dtype=jnp.int32), (N_GX * N_GY * 4, quarter))
    shuffled = jax.random.permutation(jax.random.fold_in(key, 11), base_rows, axis=1, independent=True)
    chosen = shuffled[:, :BND].reshape(N_GX, N_GY, 2, 2, BND)
    quadrant = (2 * jnp.arange(2, dtype=jnp.int32))[:, None] + jnp.arange(2, dtype=jnp.int32)[None, :]
    return (chosen + (quadrant * quarter)[None, None, :, :, None]).astype(jnp.int32)


def draw_border_list(key, part):
    listed = quadrant_rows(key)
    return listed.transpose(0, 2, 1, 3, 4).reshape(2 * N_GX, 2 * N_GY, BND)


def draw_kernel_map(key, part):
    devices = N_GX * N_GY
    zero_row = V_DEV + 16 * BND
    flat_rows = quadrant_rows(key).reshape(devices, 4 * BND)
    device_ids = jnp.arange(devices, dtype=jnp.int32)[:, None]
    quad_row = jnp.repeat(jnp.array([0, 0, 1, 1], jnp.int32), BND)
    quad_col = jnp.repeat(jnp.array([0, 1, 0, 1], jnp.int32), BND)
    slot_index = jnp.tile(jnp.arange(BND, dtype=jnp.int32), 4)
    identity = jnp.broadcast_to(jnp.arange(V_DEV, dtype=jnp.int32), (devices, V_DEV))
    empty_map = jnp.full((devices, V_DEV), zero_row, jnp.int32)
    offset_maps = [identity for _ in range(27)]
    for low_offset in range(13):
        high_offset = 26 - low_offset
        step_x = low_offset // 9 - 1
        step_y = low_offset // 3 % 3 - 1
        pair_key = jax.random.fold_in(key, 100 + low_offset)
        sequence = jax.random.permutation(jax.random.fold_in(pair_key, 1), identity, axis=1, independent=True)
        breaks = jax.random.randint(jax.random.fold_in(pair_key, 2), (devices, V_DEV - 1), 0, 3) == 0
        lateral = step_x != 0 or step_y != 0
        if lateral:
            active_slots = jax.random.randint(jax.random.fold_in(pair_key, 3), (BND,), 0, 2)
            slot_flags = jnp.broadcast_to(jnp.tile(active_slots, 4), (devices, 4 * BND)).astype(jnp.int32)
            marked = jnp.zeros((devices, V_DEV), jnp.int32).at[device_ids, flat_rows].set(slot_flags)
            remote_low = V_DEV + ((quad_row + step_x + 1) * 4 + quad_col + step_y + 1) * BND + slot_index
            remote_high = V_DEV + ((quad_row - step_x + 1) * 4 + quad_col - step_y + 1) * BND + slot_index
            target_low = empty_map.at[device_ids, flat_rows].set(jnp.broadcast_to(remote_low, (devices, 4 * BND)).astype(jnp.int32))
            target_high = empty_map.at[device_ids, flat_rows].set(jnp.broadcast_to(remote_high, (devices, 4 * BND)).astype(jnp.int32))
            in_set = jnp.take_along_axis(marked, sequence, axis=1)
            breaks = breaks | (in_set[:, :-1] == 1) | (in_set[:, 1:] == 1)
        linked = jnp.logical_not(breaks)
        forward_map = empty_map.at[device_ids, sequence[:, :-1]].set(jnp.where(linked, sequence[:, 1:], zero_row).astype(jnp.int32))
        backward_map = empty_map.at[device_ids, sequence[:, 1:]].set(jnp.where(linked, sequence[:, :-1], zero_row).astype(jnp.int32))
        if lateral:
            forward_map = jnp.where(marked == 1, target_low, forward_map)
            backward_map = jnp.where(marked == 1, target_high, backward_map)
        offset_maps[low_offset] = forward_map
        offset_maps[high_offset] = backward_map
    return jnp.stack(offset_maps, axis=0).reshape(27, devices * V_DEV).astype(jnp.int32)


def with_ends(drawn, own_key, least, top_value):
    longest = drawn.shape.index(max(drawn.shape))
    spots = []
    for shift in (0, 1):
        where = [jax.random.randint(jax.random.fold_in(own_key, axis), (), 0, length) for axis, length in enumerate(drawn.shape)]
        where[longest] = (where[longest] + shift) % drawn.shape[longest]
        spots.append(tuple(where))
    return drawn.at[spots[0]].set(least).at[spots[1]].set(top_value)


def steps_of(key, dims, pieces, smallest, largest):
    factor_of, own = 1.0, jax.random.fold_in(key, 6)
    for position, parts in pieces:
        steps = jnp.exp(jax.random.uniform(jax.random.fold_in(own, position), (parts,), jnp.float32, smallest / len(pieces), largest / len(pieces)))
        factor_of = factor_of * jnp.repeat(steps, dims[position] // parts).reshape([-1 if axis == position else 1 for axis in range(len(dims))])
    return factor_of


def routed_block(own_key, own, number, rows, count, top, bound, skew):
    order = jax.random.permutation(own_key, count)
    heavy_load, usual = load_shares(count, rows * top, bound, skew, True), load_shares(count, rows * top, bound, skew, False)
    places = jnp.arange(count)

    def named(lengths, rotation):
        used = int((lengths > 0).sum())
        fixed = max(1, used // 4)
        shifted = fixed + (places - fixed + rotation * (used - fixed)) % max(1, count - fixed)
        return jnp.zeros((count,), jnp.int32).at[order[jnp.where(places < fixed, places, shifted)]].set(jnp.asarray(lengths, jnp.int32))

    lengths = jnp.where(number % 4 == 0, named(heavy_load, number // 4), named(usual, number - number // 4 - 1))
    mixed = jax.random.permutation(jax.random.fold_in(own, 3), count)
    giver, taker = mixed[0:count // 2 * 2:2], mixed[1:count // 2 * 2:2]
    room = jnp.minimum(lengths[giver] - 1, bound - lengths[taker]) // 2
    room = jnp.where((giver == order[0]) | (taker == order[0]) | (lengths[taker] == 0), 0, jnp.maximum(room, 0))
    shifted = jax.random.randint(jax.random.fold_in(own, 4), (count // 2,), 0, 1 << 20) % (room + 1)
    lengths = lengths.at[giver].add(-shifted).at[taker].add(shifted)
    items = jnp.searchsorted(jnp.cumsum(lengths), jnp.arange(rows * top), side="right").astype(jnp.int32)
    listing = items.reshape(top, rows).T
    listing = listing[jax.random.permutation(jax.random.fold_in(own, 1), rows)]
    rotation = jax.random.randint(jax.random.fold_in(own, 2), (rows, 1), 0, top)
    return jnp.take_along_axis(listing, (jnp.arange(top)[None, :] + rotation) % top, axis=1)


def load_shares(count, total, bound, lean, full):
    weights = [(1 << 20) // math.isqrt(rank ** lean) + 1 for rank in range(1, count + 1)]
    largest = bound if full else min(bound, max(-(-total // count), total * weights[0] // sum(weights)))
    least = 1 if total - largest >= count - 1 else 0
    given, rest = [largest] + [least] * (count - 1), total - largest - least * (count - 1)
    while rest > 0:
        free = [i for i in range(1, count) if given[i] < largest] or [i for i in range(1, count) if given[i] < bound]
        whole, left = sum([weights[i] for i in free]), rest
        for i in free:
            more = min(bound - given[i], max(1, left * weights[i] // whole), rest)
            given[i] = given[i] + more
            rest = rest - more
    return np.array(given)


def noise(key, extent, deviation, bound, shards=(), held_as=jnp.bfloat16):
    loudness = steps_of(key, extent, shards, -0.22, 0.18) if shards else 1.0
    drawn = jax.random.normal(key, extent, jnp.float32) * deviation * loudness
    return jnp.minimum(jnp.maximum(drawn, -bound), bound).astype(held_as)


def setup_inputs(seed: int = 0) -> dict:
    streams_of = jax.random.split(jax.random.key(seed), 14)
    point_feats = noise(streams_of[0], (P_TOTAL, C), 1.0, 6.0, ((0, 128),))
    point_dest_keys = jax.random.split(jax.random.fold_in(streams_of[1], 1), P_TOTAL // P_DEV)
    point_dest_turns = jax.random.permutation(jax.random.fold_in(streams_of[1], 3), P_TOTAL // P_DEV)
    point_dest = jax.vmap(lambda own, number: routed_block(jax.random.fold_in(streams_of[1], 2), own, number, P_DEV, N_GX * N_GY, 1, CAP, 2))(point_dest_keys, point_dest_turns).reshape((P_TOTAL, 1))
    point_voxel = with_ends(jax.random.randint(streams_of[2], (P_TOTAL,), 0, V_DEV), jax.random.fold_in(streams_of[2], 1), 0, V_DEV - 1).astype(jnp.int32)
    kernel_map = draw_kernel_map(jax.random.fold_in(streams_of[13], 71), 0)
    border_list = draw_border_list(jax.random.fold_in(streams_of[13], 71), 0)
    conv_one = noise(streams_of[5], (K, C, C), (K * C) ** -0.5, 0.15625)
    conv_two = noise(streams_of[6], (K, C, C), (K * C) ** -0.5, 0.15625)
    gain_one = jnp.clip(1.0 + 0.15 * jax.random.normal(streams_of[7], (C,), jnp.float32), 0.25, 1.75)
    gain_two = jnp.clip(1.0 + 0.15 * jax.random.normal(streams_of[8], (C,), jnp.float32), 0.25, 1.75)
    decoder_in = noise(streams_of[9], (C, HID), C ** -0.5, 0.75)
    decoder_bias = noise(streams_of[10], (HID,), 0.5, 3.0, (), jnp.float32)
    decoder_out = noise(streams_of[11], (HID,), HID ** -0.5, 0.5, (), jnp.float32)
    target = noise(streams_of[12], (V_TOTAL,), 1.0, 6.0, ((0, 128),), jnp.float32)
    return {"point_feats": point_feats, "point_dest": point_dest, "point_voxel": point_voxel, "kernel_map": kernel_map, "border_list": border_list, "conv_one": conv_one, "conv_two": conv_two, "gain_one": gain_one, "gain_two": gain_two, "decoder_in": decoder_in, "decoder_bias": decoder_bias, "decoder_out": decoder_out, "target": target}


EPS = 1e-05

def activate(hidden, gain_vec):
    inverse_rms = lax.rsqrt(lax.optimization_barrier(jnp.mean(hidden * hidden, axis=-1, keepdims=True)) + EPS)
    return jax.nn.silu(hidden * inverse_rms * gain_vec)

def window_index():
    row_index = (2 * jnp.arange(N_GX))[:, None, None, None] + jnp.arange(4)[None, None, :, None]
    col_index = (2 * jnp.arange(N_GY))[None, :, None, None] + jnp.arange(4)[None, None, None, :]
    return (row_index, col_index)

def build_tables(features, borders):
    per_device = features.reshape(N_GX, N_GY, V_DEV, C)
    edge_rows = jax.vmap(jax.vmap(lambda source, chosen: source[chosen]))(per_device, borders)
    brick_grid = edge_rows.transpose(0, 2, 1, 3, 4, 5).reshape(2 * N_GX, 2 * N_GY, BND, C)
    padded = jnp.pad(brick_grid, ((1, 1), (1, 1), (0, 0), (0, 0)))
    row_index, col_index = window_index()
    windows = padded[row_index, col_index].reshape(N_GX, N_GY, 16 * BND, C)
    zero_row = jnp.zeros((N_GX, N_GY, 1, C), features.dtype)
    tables = jnp.concatenate([per_device, windows, zero_row], axis=2)
    return tables.reshape(N_GX * N_GY, V_DEV + 16 * BND + 1, C)

def conv_forward(tables, offset_maps, weight):
    weight_full = weight.astype(jnp.float32)

    def one_device(pair_in):
        one_table, index_rows = pair_in
        gathered = one_table[index_rows].astype(jnp.float32)
        return jnp.einsum('knc,kcd->nd', gathered, weight_full, precision=lax.Precision.HIGHEST)
    return lax.map(one_device, (tables, offset_maps)).reshape(-1, C)

def conv_backward(tables, offset_maps, weight, grad_rows):
    weight_full = weight.astype(jnp.float32)
    grad_dev = grad_rows.reshape(N_GX * N_GY, V_DEV, C)

    def one_device(triple):
        one_table, index_rows, grad_part = triple
        gathered = one_table[index_rows].astype(jnp.float32)
        grad_full = grad_part.astype(jnp.float32)
        weight_grad = jnp.einsum('knc,nd->kcd', gathered, grad_full, precision=lax.Precision.HIGHEST)
        contribution = jnp.einsum('nd,kcd->knc', grad_full, weight_full, precision=lax.Precision.HIGHEST)
        table_grad = jnp.zeros((V_DEV + 16 * BND + 1, C), jnp.float32).at[index_rows].add(contribution)
        return (weight_grad, table_grad)
    weight_grads, table_grads = lax.map(one_device, (tables, offset_maps, grad_dev))
    return (lax.optimization_barrier(jnp.sum(weight_grads, axis=0)), table_grads)

def input_grad(table_grads, borders):
    local_part = table_grads[:, :V_DEV].reshape(N_GX, N_GY, V_DEV, C)
    halo_part = table_grads[:, V_DEV:V_DEV + 16 * BND].reshape(N_GX, N_GY, 4, 4, BND, C)
    row_index, col_index = window_index()
    padded = jnp.zeros((2 * N_GX + 2, 2 * N_GY + 2, BND, C), jnp.float32).at[row_index, col_index].add(halo_part)
    per_device = padded[1:-1, 1:-1].reshape(N_GX, 2, N_GY, 2, BND, C).transpose(0, 2, 1, 3, 4, 5)

    def scatter_one(target_rows, chosen, values):
        return target_rows.at[chosen.reshape(-1)].add(values.reshape(-1, C))
    summed = jax.vmap(jax.vmap(scatter_one))(local_part, borders, per_device)
    return summed.reshape(-1, C)

def reference(point_feats, point_dest, point_voxel, kernel_map, border_list, conv_one, conv_two, gain_one, gain_two, decoder_in, decoder_bias, decoder_out, target):
    voxel_of = (point_dest[:, 0] * V_DEV + point_voxel).astype(jnp.int32)
    pooled_sum = jax.ops.segment_sum(point_feats.astype(jnp.float32), voxel_of, num_segments=V_TOTAL)
    counts = jax.ops.segment_sum(jnp.ones(voxel_of.shape, jnp.float32), voxel_of, num_segments=V_TOTAL)
    inverse = 1.0 / jnp.maximum(counts, 1.0)
    x_zero = (pooled_sum * inverse[:, None]).astype(jnp.bfloat16)
    offset_maps = kernel_map.reshape(K, N_GX * N_GY, V_DEV).transpose(1, 0, 2)
    borders = border_list.reshape(N_GX, 2, N_GY, 2, BND).transpose(0, 2, 1, 3, 4)
    table_one = build_tables(x_zero, borders)
    hidden_one = conv_forward(table_one, offset_maps, conv_one)
    act_one = activate(hidden_one, gain_one).astype(jnp.bfloat16)
    table_two = build_tables(act_one, borders)
    hidden_two = conv_forward(table_two, offset_maps, conv_two)
    block_out = (x_zero.astype(jnp.float32) + activate(hidden_two, gain_two)).astype(jnp.bfloat16)
    pre_dec = jnp.dot(block_out, decoder_in, preferred_element_type=jnp.float32) + decoder_bias
    dec_hidden = jax.nn.silu(pre_dec)
    sdf_values = lax.optimization_barrier(jnp.sum(dec_hidden * decoder_out, axis=-1))
    error_sdf = sdf_values - target
    loss_value = jnp.sum(error_sdf * error_sdf) / (2.0 * V_TOTAL)
    grad_sdf = error_sdf / V_TOTAL
    grad_decoder_out = lax.optimization_barrier(jnp.sum(dec_hidden * grad_sdf[:, None], axis=0))
    _, pull_silu = jax.vjp(jax.nn.silu, pre_dec)
    grad_pre = pull_silu(grad_sdf[:, None] * decoder_out)[0]
    grad_decoder_bias = lax.optimization_barrier(jnp.sum(grad_pre, axis=0))
    grad_pre_low = grad_pre.astype(jnp.bfloat16)
    grad_decoder_in = lax.dot_general(block_out, grad_pre_low, (((0,), (0,)), ((), ())), preferred_element_type=jnp.float32)
    grad_block = lax.dot_general(grad_pre_low, decoder_in, (((1,), (1,)), ((), ())), preferred_element_type=jnp.float32)
    _, pull_two = jax.vjp(lambda hidden: activate(hidden, gain_two), hidden_two)
    grad_hidden_two = pull_two(grad_block)[0].astype(jnp.bfloat16)
    grad_conv_two, table_grads_two = conv_backward(table_two, offset_maps, conv_two, grad_hidden_two)
    grad_act_one = input_grad(table_grads_two, borders)
    _, pull_one = jax.vjp(lambda hidden: activate(hidden, gain_one), hidden_one)
    grad_hidden_one = pull_one(grad_act_one)[0].astype(jnp.bfloat16)
    grad_conv_one, table_grads_one = conv_backward(table_one, offset_maps, conv_one, grad_hidden_one)
    grad_x_zero = grad_block + input_grad(table_grads_one, borders)
    grad_points = (grad_x_zero[voxel_of] * inverse[voxel_of][:, None]).astype(jnp.bfloat16)
    return (sdf_values, loss_value, grad_conv_one, grad_conv_two, grad_decoder_in, grad_decoder_bias, grad_decoder_out, grad_points)
```

```python
import math

import jax
import jax.numpy as jnp
from jax import lax
from jax.sharding import PartitionSpec as P

EPS = 1e-05


def with_halo(array, sides, width):
    for axis, dim in sides:
        peers, length = (lax.axis_size(axis), array.shape[dim])
        up = [(i, (i + 1) % peers) for i in range(peers - 1)]
        down = [(j, i) for i, j in up]
        last = lax.slice_in_dim(array, length - width, length, axis=dim)
        leading = lax.slice_in_dim(array, 0, width, axis=dim)
        before = lax.ppermute(last, axis, up)
        after = lax.ppermute(leading, axis, down)
        array = jnp.concatenate([before, array, after], axis=dim)
    return array


def activate(hidden, gain_vec):
    inverse_rms = lax.rsqrt(jnp.mean(hidden * hidden, axis=-1, keepdims=True) + EPS)
    return jax.nn.silu(hidden * inverse_rms * gain_vec)


def build_table(features, border_list):
    channels = features.shape[1]
    edge_rows = features[border_list]
    neighbour_rows = with_halo(edge_rows, (("gx", 0), ("gy", 1)), 1)
    zero_row = jnp.zeros((1, channels), features.dtype)
    return jnp.concatenate([features, neighbour_rows.reshape(-1, channels), zero_row], axis=0)


def split_blocks(kernel_map):
    offsets, voxels = kernel_map.shape
    block_size = math.gcd(voxels, 256)
    return kernel_map.reshape(offsets, voxels // block_size, block_size).transpose(1, 0, 2)


def select_rows(table, index_rows):
    table_rows = jnp.arange(table.shape[0], dtype=jnp.int32)
    selector = (index_rows[:, :, None] == table_rows[None, None, :]).astype(table.dtype)
    picked = jnp.einsum("knr,rc->knc", selector, table, preferred_element_type=jnp.float32)
    return picked.astype(table.dtype)


def conv_forward(table, kernel_map, weight):
    map_blocks = split_blocks(kernel_map)

    def conv_one_block(index_rows):
        return jnp.einsum(
            "knc,kcd->nd",
            select_rows(table, index_rows),
            weight,
            preferred_element_type=jnp.float32,
        )

    result = lax.map(conv_one_block, map_blocks)
    return result.reshape(-1, weight.shape[2])


def weight_grad_only(table, kernel_map, weight, grad_rows):
    map_blocks = split_blocks(kernel_map)
    grad_blocks = grad_rows.reshape(map_blocks.shape[0], map_blocks.shape[2], grad_rows.shape[1])

    def weight_one_block(running, block_item):
        index_rows, block_grad = block_item
        return (
            running
            + jnp.einsum(
                "knc,nd->kcd",
                select_rows(table, index_rows),
                block_grad,
                preferred_element_type=jnp.float32,
            ),
            None,
        )

    total, _ = lax.scan(
        weight_one_block, jnp.zeros(weight.shape, jnp.float32), (map_blocks, grad_blocks)
    )
    return total


def backward_conv(table, kernel_map, weight, grad_rows, border_list):
    voxels = kernel_map.shape[1]
    channels = grad_rows.shape[1]
    boundary = border_list.shape[2]
    weight_grad = weight_grad_only(table, kernel_map, weight, grad_rows)
    flipped_map = kernel_map[::-1]
    flipped_weight = jnp.swapaxes(weight, 1, 2)
    empty_rows = jnp.zeros((16 * boundary + 1, channels), grad_rows.dtype)
    local_part = conv_forward(
        jnp.concatenate([grad_rows, empty_rows], axis=0), flipped_map, flipped_weight
    )
    border_flat = border_list.reshape(-1)
    border_targets = kernel_map[:, border_flat]
    border_terms = jnp.einsum(
        "bd,kcd->kbc", grad_rows[border_flat], weight, preferred_element_type=jnp.float32
    )
    halo_rows = voxels + jnp.arange(16 * boundary, dtype=jnp.int32)
    selector = (border_targets[:, :, None] == halo_rows[None, None, :]).astype(jnp.float32)
    halo_flat = jnp.einsum("kbr,kbc->rc", selector, border_terms, precision=lax.Precision.HIGHEST)
    halo_grad = halo_flat.reshape(4, 4, boundary, channels)
    rows_end = jnp.stack([halo_grad[0], halo_grad[3]], axis=0)
    cols_end = jnp.stack([halo_grad[:, 0], halo_grad[:, 3]], axis=1)
    corner_end = jnp.stack([rows_end[:, 0], rows_end[:, 3]], axis=1)
    payload = jnp.stack([rows_end[:, 1:3], cols_end[1:3], corner_end], axis=2)
    received = with_halo(payload.astype(jnp.bfloat16), (("gx", 0), ("gy", 1)), 1).astype(
        payload.dtype
    )
    from_rows = jnp.stack([received[0, 1:3, 0], received[3, 1:3, 0]], axis=0)
    from_cols = jnp.stack([received[1:3, 0, 1], received[1:3, 3, 1]], axis=1)
    corner_low = jnp.stack([received[0, 0, 2], received[0, 3, 2]], axis=0)
    corner_high = jnp.stack([received[3, 0, 2], received[3, 3, 2]], axis=0)
    from_corner = jnp.stack([corner_low, corner_high], axis=0)
    folded = halo_grad[1:3, 1:3] + from_rows + from_cols + from_corner
    result = local_part.at[border_list.reshape(-1)].add(folded.reshape(-1, channels))
    return (result, weight_grad)


HALVING_STEPS = (("gy", 1), ("gy", 2), ("gx", 1), ("gx", 4), ("gy", 4), ("gx", 2), ("gx", 8))


def tree_psum(parts):
    flat = jnp.concatenate([jnp.ravel(p).astype(jnp.float32) for p in parts])
    lanes = 128
    rows = -(-flat.shape[0] // lanes)
    rows = -(-rows // (8 * 2 ** len(HALVING_STEPS))) * (8 * 2 ** len(HALVING_STEPS))
    x = jnp.pad(flat, (0, rows * lanes - flat.shape[0])).reshape(rows, lanes)
    bits = []
    for axis, mask in HALVING_STEPS:
        peers = lax.axis_size(axis)
        bit = (lax.axis_index(axis) // mask) % 2
        bits.append(bit)
        half = x.shape[0] // 2
        low, high = x[:half], x[half:]
        send = jnp.where(bit == 1, low, high)
        keep = jnp.where(bit == 1, high, low)
        x = keep + lax.ppermute(send, axis, [(i, i ^ mask) for i in range(peers)])
    for (axis, mask), bit in reversed(list(zip(HALVING_STEPS, bits))):
        peers = lax.axis_size(axis)
        other = lax.ppermute(x, axis, [(i, i ^ mask) for i in range(peers)])
        x = jnp.where(bit == 1, jnp.concatenate([other, x]), jnp.concatenate([x, other]))
    flat = x.reshape(-1)
    out, start = [], 0
    for p in parts:
        size = math.prod(p.shape)
        out.append(flat[start:start + size].reshape(p.shape))
        start += size
    return tuple(out)


def send_points(send_feats, send_ids):
    got_feats, got_ids = (
        lax.all_to_all(send_feats, ("gx", "gy"), split_axis=0, concat_axis=0, tiled=True),
        lax.all_to_all(send_ids, ("gx", "gy"), split_axis=0, concat_axis=0, tiled=True),
    )
    return (got_feats, got_ids)


def return_grads(slot_grads):
    returned = lax.all_to_all(slot_grads, ("gx", "gy"), split_axis=0, concat_axis=0, tiled=True)
    return returned


def local(
    point_feats,
    point_dest,
    point_voxel,
    kernel_map,
    border_list,
    conv_one,
    conv_two,
    gain_one,
    gain_two,
    decoder_in,
    decoder_bias,
    decoder_out,
    target,
):
    devices = lax.axis_size("gx") * lax.axis_size("gy")
    voxels = kernel_map.shape[1]
    points, channels = point_feats.shape
    capacity = 2 * points // devices
    destination = point_dest[:, 0]
    order = jnp.argsort(destination, stable=True)
    sorted_dest = destination[order]
    starts = jnp.searchsorted(sorted_dest, jnp.arange(devices, dtype=jnp.int32))
    slot_rank = jnp.arange(points, dtype=jnp.int32) - starts[sorted_dest]
    position = sorted_dest * capacity + slot_rank
    send_feats = (
        jnp.zeros((devices * capacity, channels), point_feats.dtype)
        .at[position]
        .set(point_feats[order])
    )
    send_ids = jnp.full((devices * capacity,), -1, jnp.int32).at[position].set(point_voxel[order])
    got_feats, got_ids = send_points(
        send_feats.reshape(devices, capacity, channels), send_ids.reshape(devices, capacity)
    )
    flat_ids = got_ids.reshape(-1)
    voxel_rows = jnp.arange(voxels, dtype=jnp.int32)
    slot_match = flat_ids[:, None] == voxel_rows[None, :]
    pooled_sum = jnp.einsum(
        "sv,sc->vc",
        slot_match.astype(jnp.bfloat16),
        got_feats.reshape(-1, channels),
        preferred_element_type=jnp.float32,
    )
    counts = jnp.sum(slot_match.astype(jnp.float32), axis=0)
    inverse = 1.0 / jnp.maximum(counts, 1.0)
    x_zero = (pooled_sum * inverse[:, None]).astype(jnp.bfloat16)
    table_one = build_table(x_zero, border_list)
    hidden_one = conv_forward(table_one, kernel_map, conv_one)
    act_one = activate(hidden_one, gain_one).astype(jnp.bfloat16)
    table_two = build_table(act_one, border_list)
    hidden_two = conv_forward(table_two, kernel_map, conv_two)
    block_out = (x_zero.astype(jnp.float32) + activate(hidden_two, gain_two)).astype(jnp.bfloat16)
    pre_dec = jnp.dot(block_out, decoder_in, preferred_element_type=jnp.float32) + decoder_bias
    dec_hidden = jax.nn.silu(pre_dec)
    sdf_values = jnp.sum(dec_hidden * decoder_out, axis=-1)
    whole_count = voxels * devices
    error_sdf = sdf_values - target
    loss_part = jnp.sum(error_sdf * error_sdf) / (2.0 * whole_count)
    grad_sdf = error_sdf / whole_count
    grad_out_part = jnp.sum(dec_hidden * grad_sdf[:, None], axis=0)
    _, pull_silu = jax.vjp(jax.nn.silu, pre_dec)
    grad_pre = pull_silu(grad_sdf[:, None] * decoder_out)[0]
    grad_bias_part = jnp.sum(grad_pre, axis=0)
    grad_pre_low = grad_pre.astype(jnp.bfloat16)
    grad_in_part = lax.dot_general(
        block_out, grad_pre_low, (((0,), (0,)), ((), ())), preferred_element_type=jnp.float32
    )
    grad_block = lax.dot_general(
        grad_pre_low, decoder_in, (((1,), (1,)), ((), ())), preferred_element_type=jnp.float32
    )
    _, pull_two = jax.vjp(lambda hidden: activate(hidden, gain_two), hidden_two)
    grad_hidden_two = pull_two(grad_block)[0].astype(jnp.bfloat16)
    grad_act_one, weight_grad_two = backward_conv(
        table_two, kernel_map, conv_two, grad_hidden_two, border_list
    )
    _, pull_one = jax.vjp(lambda hidden: activate(hidden, gain_one), hidden_one)
    grad_hidden_one = pull_one(grad_act_one)[0].astype(jnp.bfloat16)
    input_part, weight_grad_one = backward_conv(
        table_one, kernel_map, conv_one, grad_hidden_one, border_list
    )
    grad_x_zero = grad_block + input_part
    scaled = grad_x_zero * inverse[:, None]
    slot_values = jnp.einsum(
        "sv,vc->sc", slot_match.astype(jnp.float32), scaled, precision=lax.Precision.HIGHEST
    )
    slot_grads = slot_values.astype(jnp.bfloat16).reshape(devices, capacity, channels)
    returned = return_grads(slot_grads).reshape(-1, channels)
    grad_points = jnp.zeros((points, channels), jnp.bfloat16).at[order].set(returned[position])
    parts = (weight_grad_one, weight_grad_two, grad_in_part, grad_bias_part, grad_out_part, loss_part)
    summed = tree_psum(parts)
    (
        grad_conv_one,
        grad_conv_two,
        grad_decoder_in,
        grad_decoder_bias,
        grad_decoder_out,
        loss_value,
    ) = summed
    return (
        sdf_values,
        loss_value,
        grad_conv_one,
        grad_conv_two,
        grad_decoder_in,
        grad_decoder_bias,
        grad_decoder_out,
        grad_points,
    )


def solution(mesh):
    in_specs = (
        P(("gx", "gy"), None),
        P(("gx", "gy"), None),
        P(("gx", "gy")),
        P(None, ("gx", "gy")),
        P("gx", "gy", None),
        P(),
        P(),
        P(),
        P(),
        P(),
        P(),
        P(),
        P(("gx", "gy")),
    )
    out_specs = (P(("gx", "gy")), P(), P(), P(), P(), P(), P(), P(("gx", "gy"), None))
    return jax.shard_map(local, mesh=mesh, in_specs=in_specs, out_specs=out_specs, check_vma=False)
```

```python
import math

import jax
import numpy as np
import jax.numpy as jnp
from jax import lax
from jax.sharding import PartitionSpec as P

EPS = 1e-05


def with_halo(array, sides, width):
    for axis, dim in sides:
        peers, length = (lax.axis_size(axis), array.shape[dim])
        up = [(i, (i + 1) % peers) for i in range(peers - 1)]
        down = [(j, i) for i, j in up]
        last = lax.slice_in_dim(array, length - width, length, axis=dim)
        leading = lax.slice_in_dim(array, 0, width, axis=dim)
        before = lax.ppermute(last, axis, up)
        after = lax.ppermute(leading, axis, down)
        array = jnp.concatenate([before, array, after], axis=dim)
    return array


def activate(hidden, gain_vec):
    inverse_rms = lax.rsqrt(jnp.mean(hidden * hidden, axis=-1, keepdims=True) + EPS)
    return jax.nn.silu(hidden * inverse_rms * gain_vec)


def build_table(features, border_list):
    channels = features.shape[1]
    edge_rows = features[border_list]
    neighbour_rows = with_halo(edge_rows, (("gx", 0), ("gy", 1)), 1)
    zero_row = jnp.zeros((1, channels), features.dtype)
    return jnp.concatenate([features, neighbour_rows.reshape(-1, channels), zero_row], axis=0)


def gather_local(rows, kernel_map):
    voxels = rows.shape[0]
    local_rows = jnp.arange(voxels, dtype=jnp.int32)
    selector = (kernel_map[:, :, None] == local_rows[None, None, :]).astype(rows.dtype)
    picked = jnp.einsum("kvu,uc->kvc", selector, rows, preferred_element_type=jnp.float32)
    return picked.astype(rows.dtype)


def halo_layout(kernel_map, border_list):
    voxels = kernel_map.shape[1]
    boundary = border_list.shape[2]
    border_flat = border_list.reshape(-1)
    border_hot = (jnp.arange(voxels, dtype=jnp.int32)[:, None] == border_flat[None, :])
    named = jnp.einsum(
        "kv,vb->kb",
        kernel_map.astype(jnp.float32),
        border_hot.astype(jnp.float32),
        precision=lax.Precision.HIGHEST,
    )
    expected = np.zeros((27, 2, 2, boundary), np.float32)
    for k in range(27):
        step_x, step_y = k // 9 - 1, k // 3 % 3 - 1
        for i in range(2):
            for j in range(2):
                cell = (i + 1 + step_x) * 4 + (j + 1 + step_y)
                expected[k, i, j] = voxels + cell * boundary + np.arange(boundary)
    flag = named == jnp.asarray(expected.reshape(27, -1))
    return border_hot, flag


def halo_pick(halo, flag):
    channels = halo.shape[-1]
    pieces = []
    for k in range(27):
        step_x, step_y = k // 9 - 1, k // 3 % 3 - 1
        pieces.append(halo[1 + step_x:3 + step_x, 1 + step_y:3 + step_y].reshape(-1, channels))
    picked = jnp.stack(pieces, axis=0)
    return jnp.where(flag[:, :, None], picked, jnp.zeros_like(picked))


def halo_spread(terms):
    channels = terms.shape[-1]
    boundary = terms.shape[1] // 4
    total = jnp.zeros((4, 4, boundary, channels), terms.dtype)
    for k in range(27):
        step_x, step_y = k // 9 - 1, k // 3 % 3 - 1
        piece = terms[k].reshape(2, 2, boundary, channels)
        total = total + jnp.pad(
            piece, ((1 + step_x, 1 - step_x), (1 + step_y, 1 - step_y), (0, 0), (0, 0))
        )
    return total


def edge_halo(features, border_hot, border_list):
    channels = features.shape[1]
    edge_rows = jnp.einsum(
        "vb,vc->bc", border_hot.astype(features.dtype), features, preferred_element_type=jnp.float32
    ).astype(features.dtype)
    edge_rows = edge_rows.reshape(border_list.shape + (channels,))
    return with_halo(edge_rows, (("gx", 0), ("gy", 1)), 1)


def conv_forward(features, kernel_map, border_list, border_hot, flag, weight):
    gathered = gather_local(features, kernel_map)
    halo_rows = halo_pick(edge_halo(features, border_hot, border_list), flag)
    local_out = jnp.einsum("kvc,kcd->vd", gathered, weight, preferred_element_type=jnp.float32)
    border_out = jnp.einsum("kbc,kcd->bd", halo_rows, weight, preferred_element_type=jnp.float32)
    placed = jnp.einsum(
        "vb,bd->vd", border_hot.astype(jnp.float32), border_out, precision=lax.Precision.HIGHEST
    )
    return local_out + placed, gathered, halo_rows


def backward_conv(gathered, halo_rows, kernel_map, weight, grad_rows, border_hot, flag, border_list):
    grad_border = jnp.einsum(
        "vb,vd->bd", border_hot.astype(grad_rows.dtype), grad_rows, preferred_element_type=jnp.float32
    ).astype(grad_rows.dtype)
    weight_grad = jnp.einsum(
        "kvc,vd->kcd", gathered, grad_rows, preferred_element_type=jnp.float32
    ) + jnp.einsum("kbc,bd->kcd", halo_rows, grad_border, preferred_element_type=jnp.float32)
    flipped_weight = jnp.swapaxes(weight[::-1], 1, 2)
    grad_gathered = gather_local(grad_rows, kernel_map)
    local_part = jnp.einsum(
        "kvc,kcd->vd", grad_gathered, flipped_weight, preferred_element_type=jnp.float32
    )
    border_terms = jnp.einsum("bd,kcd->kbc", grad_border, weight, preferred_element_type=jnp.float32)
    border_terms = jnp.where(flag[:, :, None], border_terms, jnp.zeros_like(border_terms))
    halo_grad = halo_spread(border_terms)
    rows_end = jnp.stack([halo_grad[0], halo_grad[3]], axis=0)
    cols_end = jnp.stack([halo_grad[:, 0], halo_grad[:, 3]], axis=1)
    corner_end = jnp.stack([rows_end[:, 0], rows_end[:, 3]], axis=1)
    payload = jnp.stack([rows_end[:, 1:3], cols_end[1:3], corner_end], axis=2)
    received = with_halo(payload.astype(jnp.bfloat16), (("gx", 0), ("gy", 1)), 1).astype(
        payload.dtype
    )
    from_rows = jnp.stack([received[0, 1:3, 0], received[3, 1:3, 0]], axis=0)
    from_cols = jnp.stack([received[1:3, 0, 1], received[1:3, 3, 1]], axis=1)
    corner_low = jnp.stack([received[0, 0, 2], received[0, 3, 2]], axis=0)
    corner_high = jnp.stack([received[3, 0, 2], received[3, 3, 2]], axis=0)
    from_corner = jnp.stack([corner_low, corner_high], axis=0)
    folded = halo_grad[1:3, 1:3] + from_rows + from_cols + from_corner
    channels = grad_rows.shape[1]
    result = local_part + jnp.einsum(
        "vb,bd->vd",
        border_hot.astype(jnp.float32),
        folded.reshape(-1, channels),
        precision=lax.Precision.HIGHEST,
    )
    return (result, weight_grad)


HALVING_STEPS = (("gy", 1), ("gy", 2), ("gx", 1), ("gx", 4), ("gy", 4), ("gx", 2), ("gx", 8))


def tree_psum(parts):
    flat = jnp.concatenate([jnp.ravel(p).astype(jnp.float32) for p in parts])
    lanes = 128
    rows = -(-flat.shape[0] // lanes)
    rows = -(-rows // (8 * 2 ** len(HALVING_STEPS))) * (8 * 2 ** len(HALVING_STEPS))
    x = jnp.pad(flat, (0, rows * lanes - flat.shape[0])).reshape(rows, lanes)
    bits = []
    for axis, mask in HALVING_STEPS:
        peers = lax.axis_size(axis)
        bit = (lax.axis_index(axis) // mask) % 2
        bits.append(bit)
        half = x.shape[0] // 2
        low, high = x[:half], x[half:]
        send = jnp.where(bit == 1, low, high)
        keep = jnp.where(bit == 1, high, low)
        x = keep + lax.ppermute(send, axis, [(i, i ^ mask) for i in range(peers)])
    for (axis, mask), bit in reversed(list(zip(HALVING_STEPS, bits))):
        peers = lax.axis_size(axis)
        other = lax.ppermute(x, axis, [(i, i ^ mask) for i in range(peers)])
        x = jnp.where(bit == 1, jnp.concatenate([other, x]), jnp.concatenate([x, other]))
    flat = x.reshape(-1)
    out, start = [], 0
    for p in parts:
        size = math.prod(p.shape)
        out.append(flat[start:start + size].reshape(p.shape))
        start += size
    return tuple(out)


def send_points(send_feats, send_ids):
    got_feats, got_ids = (
        lax.all_to_all(send_feats, ("gx", "gy"), split_axis=0, concat_axis=0, tiled=True),
        lax.all_to_all(send_ids, ("gx", "gy"), split_axis=0, concat_axis=0, tiled=True),
    )
    return (got_feats, got_ids)


def return_grads(slot_grads):
    returned = lax.all_to_all(slot_grads, ("gx", "gy"), split_axis=0, concat_axis=0, tiled=True)
    return returned


def local(
    point_feats,
    point_dest,
    point_voxel,
    kernel_map,
    border_list,
    conv_one,
    conv_two,
    gain_one,
    gain_two,
    decoder_in,
    decoder_bias,
    decoder_out,
    target,
):
    devices = lax.axis_size("gx") * lax.axis_size("gy")
    voxels = kernel_map.shape[1]
    points, channels = point_feats.shape
    capacity = 2 * points // devices
    destination = point_dest[:, 0]
    order = jnp.argsort(destination, stable=True)
    sorted_dest = destination[order]
    starts = jnp.searchsorted(sorted_dest, jnp.arange(devices, dtype=jnp.int32))
    slot_rank = jnp.arange(points, dtype=jnp.int32) - starts[sorted_dest]
    position = sorted_dest * capacity + slot_rank
    send_feats = (
        jnp.zeros((devices * capacity, channels), point_feats.dtype)
        .at[position]
        .set(point_feats[order])
    )
    send_ids = jnp.full((devices * capacity,), -1, jnp.int32).at[position].set(point_voxel[order])
    got_feats, got_ids = send_points(
        send_feats.reshape(devices, capacity, channels), send_ids.reshape(devices, capacity)
    )
    flat_ids = got_ids.reshape(-1)
    voxel_rows = jnp.arange(voxels, dtype=jnp.int32)
    slot_match = flat_ids[:, None] == voxel_rows[None, :]
    pooled_sum = jnp.einsum(
        "sv,sc->vc",
        slot_match.astype(jnp.bfloat16),
        got_feats.reshape(-1, channels),
        preferred_element_type=jnp.float32,
    )
    counts = jnp.sum(slot_match.astype(jnp.float32), axis=0)
    inverse = 1.0 / jnp.maximum(counts, 1.0)
    x_zero = (pooled_sum * inverse[:, None]).astype(jnp.bfloat16)
    border_hot, flag = halo_layout(kernel_map, border_list)
    hidden_one, gathered_one, halo_one = conv_forward(
        x_zero, kernel_map, border_list, border_hot, flag, conv_one
    )
    act_one = activate(hidden_one, gain_one).astype(jnp.bfloat16)
    hidden_two, gathered_two, halo_two = conv_forward(
        act_one, kernel_map, border_list, border_hot, flag, conv_two
    )
    block_out = (x_zero.astype(jnp.float32) + activate(hidden_two, gain_two)).astype(jnp.bfloat16)
    pre_dec = jnp.dot(block_out, decoder_in, preferred_element_type=jnp.float32) + decoder_bias
    dec_hidden = jax.nn.silu(pre_dec)
    sdf_values = jnp.sum(dec_hidden * decoder_out, axis=-1)
    whole_count = voxels * devices
    error_sdf = sdf_values - target
    loss_part = jnp.sum(error_sdf * error_sdf) / (2.0 * whole_count)
    grad_sdf = error_sdf / whole_count
    grad_out_part = jnp.sum(dec_hidden * grad_sdf[:, None], axis=0)
    _, pull_silu = jax.vjp(jax.nn.silu, pre_dec)
    grad_pre = pull_silu(grad_sdf[:, None] * decoder_out)[0]
    grad_bias_part = jnp.sum(grad_pre, axis=0)
    grad_pre_low = grad_pre.astype(jnp.bfloat16)
    grad_in_part = lax.dot_general(
        block_out, grad_pre_low, (((0,), (0,)), ((), ())), preferred_element_type=jnp.float32
    )
    grad_block = lax.dot_general(
        grad_pre_low, decoder_in, (((1,), (1,)), ((), ())), preferred_element_type=jnp.float32
    )
    _, pull_two = jax.vjp(lambda hidden: activate(hidden, gain_two), hidden_two)
    grad_hidden_two = pull_two(grad_block)[0].astype(jnp.bfloat16)
    grad_act_one, weight_grad_two = backward_conv(
        gathered_two, halo_two, kernel_map, conv_two, grad_hidden_two, border_hot, flag, border_list
    )
    _, pull_one = jax.vjp(lambda hidden: activate(hidden, gain_one), hidden_one)
    grad_hidden_one = pull_one(grad_act_one)[0].astype(jnp.bfloat16)
    input_part, weight_grad_one = backward_conv(
        gathered_one, halo_one, kernel_map, conv_one, grad_hidden_one, border_hot, flag, border_list
    )
    grad_x_zero = grad_block + input_part
    scaled = grad_x_zero * inverse[:, None]
    slot_values = jnp.einsum(
        "sv,vc->sc", slot_match.astype(jnp.float32), scaled, precision=lax.Precision.HIGHEST
    )
    slot_grads = slot_values.astype(jnp.bfloat16).reshape(devices, capacity, channels)
    returned = return_grads(slot_grads).reshape(-1, channels)
    grad_points = jnp.zeros((points, channels), jnp.bfloat16).at[order].set(returned[position])
    parts = (weight_grad_one, weight_grad_two, grad_in_part, grad_bias_part, grad_out_part, loss_part)
    summed = tree_psum(parts)
    (
        grad_conv_one,
        grad_conv_two,
        grad_decoder_in,
        grad_decoder_bias,
        grad_decoder_out,
        loss_value,
    ) = summed
    return (
        sdf_values,
        loss_value,
        grad_conv_one,
        grad_conv_two,
        grad_decoder_in,
        grad_decoder_bias,
        grad_decoder_out,
        grad_points,
    )


def solution(mesh):
    in_specs = (
        P(("gx", "gy"), None),
        P(("gx", "gy"), None),
        P(("gx", "gy")),
        P(None, ("gx", "gy")),
        P("gx", "gy", None),
        P(),
        P(),
        P(),
        P(),
        P(),
        P(),
        P(),
        P(("gx", "gy")),
    )
    out_specs = (P(("gx", "gy")), P(), P(), P(), P(), P(), P(), P(("gx", "gy"), None))
    return jax.shard_map(local, mesh=mesh, in_specs=in_specs, out_specs=out_specs, check_vma=False)
```

```python
import math

import jax
import numpy as np
import jax.numpy as jnp
from jax import lax
from jax.sharding import PartitionSpec as P

EPS = 1e-05


def with_halo(array, sides, width):
    for axis, dim in sides:
        peers, length = (lax.axis_size(axis), array.shape[dim])
        up = [(i, (i + 1) % peers) for i in range(peers - 1)]
        down = [(j, i) for i, j in up]
        last = lax.slice_in_dim(array, length - width, length, axis=dim)
        leading = lax.slice_in_dim(array, 0, width, axis=dim)
        before = lax.ppermute(last, axis, up)
        after = lax.ppermute(leading, axis, down)
        array = jnp.concatenate([before, array, after], axis=dim)
    return array


def activate(hidden, gain_vec):
    inverse_rms = lax.rsqrt(jnp.mean(hidden * hidden, axis=-1, keepdims=True) + EPS)
    return jax.nn.silu(hidden * inverse_rms * gain_vec)


def build_table(features, border_list):
    channels = features.shape[1]
    edge_rows = features[border_list]
    neighbour_rows = with_halo(edge_rows, (("gx", 0), ("gy", 1)), 1)
    zero_row = jnp.zeros((1, channels), features.dtype)
    return jnp.concatenate([features, neighbour_rows.reshape(-1, channels), zero_row], axis=0)


def gather_local(rows, kernel_map):
    voxels = rows.shape[0]
    local_rows = jnp.arange(voxels, dtype=jnp.int32)
    selector = (kernel_map[:, :, None] == local_rows[None, None, :]).astype(rows.dtype)
    picked = jnp.einsum("kvu,uc->kvc", selector, rows, preferred_element_type=jnp.float32)
    return picked.astype(rows.dtype)


def halo_layout(kernel_map, border_list):
    voxels = kernel_map.shape[1]
    boundary = border_list.shape[2]
    border_flat = border_list.reshape(-1)
    border_hot = (jnp.arange(voxels, dtype=jnp.int32)[:, None] == border_flat[None, :])
    named = jnp.einsum(
        "kv,vb->kb",
        kernel_map.astype(jnp.float32),
        border_hot.astype(jnp.float32),
        precision=lax.Precision.HIGHEST,
    )
    expected = np.zeros((27, 2, 2, boundary), np.int32)
    for k in range(27):
        step_x, step_y = k // 9 - 1, k // 3 % 3 - 1
        for i in range(2):
            for j in range(2):
                cell = (i + 1 + step_x) * 4 + (j + 1 + step_y)
                expected[k, i, j] = cell * boundary + np.arange(boundary)
    expected = jnp.asarray(expected.reshape(27, -1))
    flag = named == (expected + voxels).astype(jnp.float32)
    target = jnp.where(flag, expected, -1)
    return border_hot, target


def halo_hot(target, halo_count):
    return target[:, :, None] == jnp.arange(halo_count, dtype=jnp.int32)[None, None, :]


def halo_pick(halo, target):
    channels = halo.shape[-1]
    flat = halo.reshape(-1, channels)
    picked = jnp.einsum(
        "kbr,rc->kbc",
        halo_hot(target, flat.shape[0]).astype(flat.dtype),
        flat,
        preferred_element_type=jnp.float32,
    )
    return picked.astype(halo.dtype)


def edge_halo(features, border_hot, border_list):
    channels = features.shape[1]
    edge_rows = jnp.einsum(
        "vb,vc->bc", border_hot.astype(features.dtype), features, preferred_element_type=jnp.float32
    ).astype(features.dtype)
    edge_rows = edge_rows.reshape(border_list.shape + (channels,))
    return with_halo(edge_rows, (("gx", 0), ("gy", 1)), 1)


def conv_forward(features, kernel_map, border_list, border_hot, target, weight):
    gathered = gather_local(features, kernel_map)
    halo_rows = halo_pick(edge_halo(features, border_hot, border_list), target)
    local_out = jnp.einsum("kvc,kcd->vd", gathered, weight, preferred_element_type=jnp.float32)
    border_out = jnp.einsum("kbc,kcd->bd", halo_rows, weight, preferred_element_type=jnp.float32)
    placed = jnp.einsum(
        "vb,bd->vd", border_hot.astype(jnp.float32), border_out, precision=lax.Precision.HIGHEST
    )
    return local_out + placed, gathered, halo_rows


def backward_conv(gathered, halo_rows, kernel_map, weight, grad_rows, border_hot, target, border_list):
    grad_border = jnp.einsum(
        "vb,vd->bd", border_hot.astype(grad_rows.dtype), grad_rows, preferred_element_type=jnp.float32
    ).astype(grad_rows.dtype)
    weight_grad = jnp.einsum(
        "kvc,vd->kcd", gathered, grad_rows, preferred_element_type=jnp.float32
    ) + jnp.einsum("kbc,bd->kcd", halo_rows, grad_border, preferred_element_type=jnp.float32)
    flipped_weight = jnp.swapaxes(weight[::-1], 1, 2)
    grad_gathered = gather_local(grad_rows, kernel_map)
    local_part = jnp.einsum(
        "kvc,kcd->vd", grad_gathered, flipped_weight, preferred_element_type=jnp.float32
    )
    channels = grad_rows.shape[1]
    boundary = border_list.shape[2]
    spread = jnp.einsum(
        "kbr,bd->rkd",
        halo_hot(target, 16 * boundary).astype(grad_border.dtype),
        grad_border,
        preferred_element_type=jnp.float32,
    ).astype(grad_border.dtype)
    halo_grad = jnp.einsum(
        "rkd,kcd->rc", spread, weight, preferred_element_type=jnp.float32
    ).reshape(4, 4, boundary, channels)
    rows_end = jnp.stack([halo_grad[0], halo_grad[3]], axis=0)
    cols_end = jnp.stack([halo_grad[:, 0], halo_grad[:, 3]], axis=1)
    corner_end = jnp.stack([rows_end[:, 0], rows_end[:, 3]], axis=1)
    payload = jnp.stack([rows_end[:, 1:3], cols_end[1:3], corner_end], axis=2)
    received = with_halo(payload.astype(jnp.bfloat16), (("gx", 0), ("gy", 1)), 1).astype(
        payload.dtype
    )
    from_rows = jnp.stack([received[0, 1:3, 0], received[3, 1:3, 0]], axis=0)
    from_cols = jnp.stack([received[1:3, 0, 1], received[1:3, 3, 1]], axis=1)
    corner_low = jnp.stack([received[0, 0, 2], received[0, 3, 2]], axis=0)
    corner_high = jnp.stack([received[3, 0, 2], received[3, 3, 2]], axis=0)
    from_corner = jnp.stack([corner_low, corner_high], axis=0)
    folded = halo_grad[1:3, 1:3] + from_rows + from_cols + from_corner
    result = local_part + jnp.einsum(
        "vb,bd->vd",
        border_hot.astype(jnp.float32),
        folded.reshape(-1, channels),
        precision=lax.Precision.HIGHEST,
    )
    return (result, weight_grad)


HALVING_STEPS = (("gy", 1), ("gy", 2), ("gx", 1), ("gx", 4), ("gy", 4), ("gx", 2), ("gx", 8))


def tree_psum(parts):
    flat = jnp.concatenate([jnp.ravel(p).astype(jnp.float32) for p in parts])
    lanes = 128
    rows = -(-flat.shape[0] // lanes)
    rows = -(-rows // (8 * 2 ** len(HALVING_STEPS))) * (8 * 2 ** len(HALVING_STEPS))
    x = jnp.pad(flat, (0, rows * lanes - flat.shape[0])).reshape(rows, lanes)
    bits = []
    for axis, mask in HALVING_STEPS:
        peers = lax.axis_size(axis)
        bit = (lax.axis_index(axis) // mask) % 2
        bits.append(bit)
        half = x.shape[0] // 2
        low, high = x[:half], x[half:]
        send = jnp.where(bit == 1, low, high)
        keep = jnp.where(bit == 1, high, low)
        x = keep + lax.ppermute(send, axis, [(i, i ^ mask) for i in range(peers)])
    for (axis, mask), bit in reversed(list(zip(HALVING_STEPS, bits))):
        peers = lax.axis_size(axis)
        other = lax.ppermute(x, axis, [(i, i ^ mask) for i in range(peers)])
        x = jnp.where(bit == 1, jnp.concatenate([other, x]), jnp.concatenate([x, other]))
    flat = x.reshape(-1)
    out, start = [], 0
    for p in parts:
        size = math.prod(p.shape)
        out.append(flat[start:start + size].reshape(p.shape))
        start += size
    return tuple(out)


def send_points(send_feats, send_ids):
    got_feats, got_ids = (
        lax.all_to_all(send_feats, ("gx", "gy"), split_axis=0, concat_axis=0, tiled=True),
        lax.all_to_all(send_ids, ("gx", "gy"), split_axis=0, concat_axis=0, tiled=True),
    )
    return (got_feats, got_ids)


def return_grads(slot_grads):
    returned = lax.all_to_all(slot_grads, ("gx", "gy"), split_axis=0, concat_axis=0, tiled=True)
    return returned


def local(
    point_feats,
    point_dest,
    point_voxel,
    kernel_map,
    border_list,
    conv_one,
    conv_two,
    gain_one,
    gain_two,
    decoder_in,
    decoder_bias,
    decoder_out,
    target,
):
    devices = lax.axis_size("gx") * lax.axis_size("gy")
    voxels = kernel_map.shape[1]
    points, channels = point_feats.shape
    capacity = 2 * points // devices
    destination = point_dest[:, 0]
    order = jnp.argsort(destination, stable=True)
    sorted_dest = destination[order]
    starts = jnp.searchsorted(sorted_dest, jnp.arange(devices, dtype=jnp.int32))
    slot_rank = jnp.arange(points, dtype=jnp.int32) - starts[sorted_dest]
    position = sorted_dest * capacity + slot_rank
    send_feats = (
        jnp.zeros((devices * capacity, channels), point_feats.dtype)
        .at[position]
        .set(point_feats[order])
    )
    send_ids = jnp.full((devices * capacity,), -1, jnp.int32).at[position].set(point_voxel[order])
    got_feats, got_ids = send_points(
        send_feats.reshape(devices, capacity, channels), send_ids.reshape(devices, capacity)
    )
    flat_ids = got_ids.reshape(-1)
    voxel_rows = jnp.arange(voxels, dtype=jnp.int32)
    slot_match = flat_ids[:, None] == voxel_rows[None, :]
    pooled_sum = jnp.einsum(
        "sv,sc->vc",
        slot_match.astype(jnp.bfloat16),
        got_feats.reshape(-1, channels),
        preferred_element_type=jnp.float32,
    )
    counts = jnp.sum(slot_match.astype(jnp.float32), axis=0)
    inverse = 1.0 / jnp.maximum(counts, 1.0)
    x_zero = (pooled_sum * inverse[:, None]).astype(jnp.bfloat16)
    border_hot, halo_target = halo_layout(kernel_map, border_list)
    hidden_one, gathered_one, halo_one = conv_forward(
        x_zero, kernel_map, border_list, border_hot, halo_target, conv_one
    )
    act_one = activate(hidden_one, gain_one).astype(jnp.bfloat16)
    hidden_two, gathered_two, halo_two = conv_forward(
        act_one, kernel_map, border_list, border_hot, halo_target, conv_two
    )
    block_out = (x_zero.astype(jnp.float32) + activate(hidden_two, gain_two)).astype(jnp.bfloat16)
    pre_dec = jnp.dot(block_out, decoder_in, preferred_element_type=jnp.float32) + decoder_bias
    dec_hidden = jax.nn.silu(pre_dec)
    sdf_values = jnp.sum(dec_hidden * decoder_out, axis=-1)
    whole_count = voxels * devices
    error_sdf = sdf_values - target
    loss_part = jnp.sum(error_sdf * error_sdf) / (2.0 * whole_count)
    grad_sdf = error_sdf / whole_count
    grad_out_part = jnp.sum(dec_hidden * grad_sdf[:, None], axis=0)
    _, pull_silu = jax.vjp(jax.nn.silu, pre_dec)
    grad_pre = pull_silu(grad_sdf[:, None] * decoder_out)[0]
    grad_bias_part = jnp.sum(grad_pre, axis=0)
    grad_pre_low = grad_pre.astype(jnp.bfloat16)
    grad_in_part = lax.dot_general(
        block_out, grad_pre_low, (((0,), (0,)), ((), ())), preferred_element_type=jnp.float32
    )
    grad_block = lax.dot_general(
        grad_pre_low, decoder_in, (((1,), (1,)), ((), ())), preferred_element_type=jnp.float32
    )
    _, pull_two = jax.vjp(lambda hidden: activate(hidden, gain_two), hidden_two)
    grad_hidden_two = pull_two(grad_block)[0].astype(jnp.bfloat16)
    grad_act_one, weight_grad_two = backward_conv(
        gathered_two, halo_two, kernel_map, conv_two, grad_hidden_two, border_hot, halo_target, border_list
    )
    _, pull_one = jax.vjp(lambda hidden: activate(hidden, gain_one), hidden_one)
    grad_hidden_one = pull_one(grad_act_one)[0].astype(jnp.bfloat16)
    input_part, weight_grad_one = backward_conv(
        gathered_one, halo_one, kernel_map, conv_one, grad_hidden_one, border_hot, halo_target, border_list
    )
    grad_x_zero = grad_block + input_part
    scaled = grad_x_zero * inverse[:, None]
    slot_values = jnp.einsum(
        "sv,vc->sc", slot_match.astype(jnp.float32), scaled, precision=lax.Precision.HIGHEST
    )
    slot_grads = slot_values.astype(jnp.bfloat16).reshape(devices, capacity, channels)
    returned = return_grads(slot_grads).reshape(-1, channels)
    grad_points = jnp.zeros((points, channels), jnp.bfloat16).at[order].set(returned[position])
    parts = (weight_grad_one, weight_grad_two, grad_in_part, grad_bias_part, grad_out_part, loss_part)
    summed = tree_psum(parts)
    (
        grad_conv_one,
        grad_conv_two,
        grad_decoder_in,
        grad_decoder_bias,
        grad_decoder_out,
        loss_value,
    ) = summed
    return (
        sdf_values,
        loss_value,
        grad_conv_one,
        grad_conv_two,
        grad_decoder_in,
        grad_decoder_bias,
        grad_decoder_out,
        grad_points,
    )


def solution(mesh):
    in_specs = (
        P(("gx", "gy"), None),
        P(("gx", "gy"), None),
        P(("gx", "gy")),
        P(None, ("gx", "gy")),
        P("gx", "gy", None),
        P(),
        P(),
        P(),
        P(),
        P(),
        P(),
        P(),
        P(("gx", "gy")),
    )
    out_specs = (P(("gx", "gy")), P(), P(), P(), P(), P(), P(), P(("gx", "gy"), None))
    return jax.shard_map(local, mesh=mesh, in_specs=in_specs, out_specs=out_specs, check_vma=False)
```

```python
import math

import jax
import numpy as np
import jax.numpy as jnp
from jax import lax
from jax.sharding import PartitionSpec as P

EPS = 1e-05


def with_halo(array, sides, width):
    for axis, dim in sides:
        peers, length = (lax.axis_size(axis), array.shape[dim])
        up = [(i, (i + 1) % peers) for i in range(peers - 1)]
        down = [(j, i) for i, j in up]
        last = lax.slice_in_dim(array, length - width, length, axis=dim)
        leading = lax.slice_in_dim(array, 0, width, axis=dim)
        before = lax.ppermute(last, axis, up)
        after = lax.ppermute(leading, axis, down)
        array = jnp.concatenate([before, array, after], axis=dim)
    return array


def activate(hidden, gain_vec):
    inverse_rms = lax.rsqrt(jnp.mean(hidden * hidden, axis=-1, keepdims=True) + EPS)
    return jax.nn.silu(hidden * inverse_rms * gain_vec)


def build_table(features, border_list):
    channels = features.shape[1]
    edge_rows = features[border_list]
    neighbour_rows = with_halo(edge_rows, (("gx", 0), ("gy", 1)), 1)
    zero_row = jnp.zeros((1, channels), features.dtype)
    return jnp.concatenate([features, neighbour_rows.reshape(-1, channels), zero_row], axis=0)


def gather_local(rows, kernel_map):
    voxels = rows.shape[0]
    local_rows = jnp.arange(voxels, dtype=jnp.int32)
    selector = (kernel_map[:, :, None] == local_rows[None, None, :]).astype(rows.dtype)
    picked = jnp.einsum("kvu,uc->kvc", selector, rows, preferred_element_type=jnp.float32)
    return picked.astype(rows.dtype)


def halo_layout(kernel_map, border_list):
    voxels = kernel_map.shape[1]
    boundary = border_list.shape[2]
    border_flat = border_list.reshape(-1)
    border_hot = (jnp.arange(voxels, dtype=jnp.int32)[:, None] == border_flat[None, :])
    named = jnp.einsum(
        "kv,vb->kb",
        kernel_map.astype(jnp.float32),
        border_hot.astype(jnp.float32),
        precision=lax.Precision.HIGHEST,
    )
    expected = np.zeros((27, 2, 2, boundary), np.int32)
    for k in range(27):
        step_x, step_y = k // 9 - 1, k // 3 % 3 - 1
        for i in range(2):
            for j in range(2):
                cell = (i + 1 + step_x) * 4 + (j + 1 + step_y)
                expected[k, i, j] = cell * boundary + np.arange(boundary)
    expected = jnp.asarray(expected.reshape(27, -1))
    flag = named == (expected + voxels).astype(jnp.float32)
    target = jnp.where(flag, expected, -1)
    return border_hot, target


def halo_hot(target, halo_count):
    return target[:, :, None] == jnp.arange(halo_count, dtype=jnp.int32)[None, None, :]


def halo_pick(halo, target):
    channels = halo.shape[-1]
    flat = halo.reshape(-1, channels)
    picked = jnp.einsum(
        "kbr,rc->kbc",
        halo_hot(target, flat.shape[0]).astype(flat.dtype),
        flat,
        preferred_element_type=jnp.float32,
    )
    return picked.astype(halo.dtype)


def edge_halo(features, border_hot, border_list):
    channels = features.shape[1]
    edge_rows = jnp.einsum(
        "vb,vc->bc", border_hot.astype(features.dtype), features, preferred_element_type=jnp.float32
    ).astype(features.dtype)
    edge_rows = edge_rows.reshape(border_list.shape + (channels,))
    return with_halo(edge_rows, (("gx", 0), ("gy", 1)), 1)


def conv_forward(features, kernel_map, border_list, border_hot, target, weight):
    gathered = gather_local(features, kernel_map)
    halo_rows = halo_pick(edge_halo(features, border_hot, border_list), target)
    local_out = jnp.einsum("kvc,kcd->vd", gathered, weight, preferred_element_type=jnp.float32)
    border_out = jnp.einsum("kbc,kcd->bd", halo_rows, weight, preferred_element_type=jnp.float32)
    placed = jnp.einsum(
        "vb,bd->vd", border_hot.astype(jnp.float32), border_out, precision=lax.Precision.HIGHEST
    )
    return local_out + placed, gathered, halo_rows


def backward_conv(gathered, halo_rows, kernel_map, weight, grad_rows, border_hot, target, border_list):
    grad_border = jnp.einsum(
        "vb,vd->bd", border_hot.astype(grad_rows.dtype), grad_rows, preferred_element_type=jnp.float32
    ).astype(grad_rows.dtype)
    weight_grad = jnp.einsum(
        "kvc,vd->kcd", gathered, grad_rows, preferred_element_type=jnp.float32
    ) + jnp.einsum("kbc,bd->kcd", halo_rows, grad_border, preferred_element_type=jnp.float32)
    flipped_weight = jnp.swapaxes(weight[::-1], 1, 2)
    grad_gathered = gather_local(grad_rows, kernel_map)
    local_part = jnp.einsum(
        "kvc,kcd->vd", grad_gathered, flipped_weight, preferred_element_type=jnp.float32
    )
    channels = grad_rows.shape[1]
    boundary = border_list.shape[2]
    spread = jnp.einsum(
        "kbr,bd->rkd",
        halo_hot(target, 16 * boundary).astype(grad_border.dtype),
        grad_border,
        preferred_element_type=jnp.float32,
    ).astype(grad_border.dtype)
    halo_grad = jnp.einsum(
        "rkd,kcd->rc", spread, weight, preferred_element_type=jnp.float32
    ).reshape(4, 4, boundary, channels)
    rows_end = jnp.stack([halo_grad[0], halo_grad[3]], axis=0)
    cols_end = jnp.stack([halo_grad[:, 0], halo_grad[:, 3]], axis=1)
    corner_end = jnp.stack([rows_end[:, 0], rows_end[:, 3]], axis=1)
    payload = jnp.stack([rows_end[:, 1:3], cols_end[1:3], corner_end], axis=2)
    received = with_halo(payload.astype(jnp.bfloat16), (("gx", 0), ("gy", 1)), 1).astype(
        payload.dtype
    )
    from_rows = jnp.stack([received[0, 1:3, 0], received[3, 1:3, 0]], axis=0)
    from_cols = jnp.stack([received[1:3, 0, 1], received[1:3, 3, 1]], axis=1)
    corner_low = jnp.stack([received[0, 0, 2], received[0, 3, 2]], axis=0)
    corner_high = jnp.stack([received[3, 0, 2], received[3, 3, 2]], axis=0)
    from_corner = jnp.stack([corner_low, corner_high], axis=0)
    folded = halo_grad[1:3, 1:3] + from_rows + from_cols + from_corner
    result = local_part + jnp.einsum(
        "vb,bd->vd",
        border_hot.astype(jnp.float32),
        folded.reshape(-1, channels),
        precision=lax.Precision.HIGHEST,
    )
    return (result, weight_grad)


HALVING_STEPS = (("gy", 1), ("gy", 2), ("gx", 1), ("gx", 4), ("gy", 4), ("gx", 2), ("gx", 8))


def tree_psum(parts):
    flat = jnp.concatenate([jnp.ravel(p).astype(jnp.float32) for p in parts])
    lanes = 128
    rows = -(-flat.shape[0] // lanes)
    rows = -(-rows // (8 * 2 ** len(HALVING_STEPS))) * (8 * 2 ** len(HALVING_STEPS))
    x = jnp.pad(flat, (0, rows * lanes - flat.shape[0])).reshape(rows, lanes)
    bits = []
    for axis, mask in HALVING_STEPS:
        peers = lax.axis_size(axis)
        bit = (lax.axis_index(axis) // mask) % 2
        bits.append(bit)
        half = x.shape[0] // 2
        low, high = x[:half], x[half:]
        send = jnp.where(bit == 1, low, high)
        keep = jnp.where(bit == 1, high, low)
        x = keep + lax.ppermute(send, axis, [(i, i ^ mask) for i in range(peers)])
    for (axis, mask), bit in reversed(list(zip(HALVING_STEPS, bits))):
        peers = lax.axis_size(axis)
        other = lax.ppermute(x, axis, [(i, i ^ mask) for i in range(peers)])
        x = jnp.where(bit == 1, jnp.concatenate([other, x]), jnp.concatenate([x, other]))
    flat = x.reshape(-1)
    out, start = [], 0
    for p in parts:
        size = math.prod(p.shape)
        out.append(flat[start:start + size].reshape(p.shape))
        start += size
    return tuple(out)


def slot_positions(destination, devices, capacity):
    points = destination.shape[0]
    block = math.gcd(points, 128)
    blocks = points // block
    dest_hot = destination[:, None] == jnp.arange(devices, dtype=jnp.int32)[None, :]
    grouped = dest_hot.astype(jnp.bfloat16).reshape(blocks, block, devices)
    lower = (
        jnp.arange(block, dtype=jnp.int32)[:, None] > jnp.arange(block, dtype=jnp.int32)[None, :]
    ).astype(jnp.bfloat16)
    within = jnp.einsum("ij,bjd->bid", lower, grouped, preferred_element_type=jnp.float32)
    totals = jnp.sum(grouped.astype(jnp.float32), axis=1)
    lower_blocks = (
        jnp.arange(blocks, dtype=jnp.int32)[:, None] > jnp.arange(blocks, dtype=jnp.int32)[None, :]
    ).astype(jnp.float32)
    offsets = jnp.einsum("ab,bd->ad", lower_blocks, totals, precision=lax.Precision.HIGHEST)
    earlier = (within + offsets[:, None, :]).reshape(points, devices)
    rank = jnp.sum(jnp.where(dest_hot, earlier, 0.0), axis=1).astype(jnp.int32)
    return destination * capacity + rank


def send_points(send_rows):
    return lax.all_to_all(send_rows, ("gx", "gy"), split_axis=0, concat_axis=0, tiled=True)


def return_grads(slot_grads):
    returned = lax.all_to_all(slot_grads, ("gx", "gy"), split_axis=0, concat_axis=0, tiled=True)
    return returned


def local(
    point_feats,
    point_dest,
    point_voxel,
    kernel_map,
    border_list,
    conv_one,
    conv_two,
    gain_one,
    gain_two,
    decoder_in,
    decoder_bias,
    decoder_out,
    target,
):
    devices = lax.axis_size("gx") * lax.axis_size("gy")
    voxels = kernel_map.shape[1]
    points, channels = point_feats.shape
    capacity = 2 * points // devices
    destination = point_dest[:, 0]
    position = slot_positions(destination, devices, capacity)
    slot_hot = (
        jnp.arange(devices * capacity, dtype=jnp.int32)[:, None] == position[None, :]
    ).astype(jnp.bfloat16)
    id_high = (point_voxel // 32 + 1).astype(jnp.bfloat16)
    id_low = (point_voxel % 32).astype(jnp.bfloat16)
    payload = jnp.concatenate(
        [
            point_feats,
            jnp.ones((points, 1), jnp.bfloat16),
            id_high[:, None],
            id_low[:, None],
        ],
        axis=1,
    )
    send = jnp.einsum(
        "sp,pc->sc", slot_hot, payload, preferred_element_type=jnp.float32
    ).astype(jnp.bfloat16)
    got = send_points(send.reshape(devices, capacity, channels + 3)).reshape(-1, channels + 3)
    flat_ids = ((got[:, channels + 1].astype(jnp.float32) - 1.0) * 32.0 + got[:, channels + 2].astype(jnp.float32)).astype(jnp.int32)
    voxel_rows = jnp.arange(voxels, dtype=jnp.int32)
    slot_match = (flat_ids[:, None] == voxel_rows[None, :]).astype(jnp.bfloat16)
    pooled = jnp.einsum(
        "sv,sc->vc", slot_match, got[:, : channels + 1], preferred_element_type=jnp.float32
    )
    pooled_sum = pooled[:, :channels]
    counts = pooled[:, channels]
    inverse = 1.0 / jnp.maximum(counts, 1.0)
    x_zero = (pooled_sum * inverse[:, None]).astype(jnp.bfloat16)
    border_hot, halo_target = halo_layout(kernel_map, border_list)
    hidden_one, gathered_one, halo_one = conv_forward(
        x_zero, kernel_map, border_list, border_hot, halo_target, conv_one
    )
    act_one = activate(hidden_one, gain_one).astype(jnp.bfloat16)
    hidden_two, gathered_two, halo_two = conv_forward(
        act_one, kernel_map, border_list, border_hot, halo_target, conv_two
    )
    block_out = (x_zero.astype(jnp.float32) + activate(hidden_two, gain_two)).astype(jnp.bfloat16)
    pre_dec = jnp.dot(block_out, decoder_in, preferred_element_type=jnp.float32) + decoder_bias
    dec_hidden = jax.nn.silu(pre_dec)
    sdf_values = jnp.sum(dec_hidden * decoder_out, axis=-1)
    whole_count = voxels * devices
    error_sdf = sdf_values - target
    loss_part = jnp.sum(error_sdf * error_sdf) / (2.0 * whole_count)
    grad_sdf = error_sdf / whole_count
    grad_out_part = jnp.sum(dec_hidden * grad_sdf[:, None], axis=0)
    _, pull_silu = jax.vjp(jax.nn.silu, pre_dec)
    grad_pre = pull_silu(grad_sdf[:, None] * decoder_out)[0]
    grad_bias_part = jnp.sum(grad_pre, axis=0)
    grad_pre_low = grad_pre.astype(jnp.bfloat16)
    grad_in_part = lax.dot_general(
        block_out, grad_pre_low, (((0,), (0,)), ((), ())), preferred_element_type=jnp.float32
    )
    grad_block = lax.dot_general(
        grad_pre_low, decoder_in, (((1,), (1,)), ((), ())), preferred_element_type=jnp.float32
    )
    _, pull_two = jax.vjp(lambda hidden: activate(hidden, gain_two), hidden_two)
    grad_hidden_two = pull_two(grad_block)[0].astype(jnp.bfloat16)
    grad_act_one, weight_grad_two = backward_conv(
        gathered_two, halo_two, kernel_map, conv_two, grad_hidden_two, border_hot, halo_target, border_list
    )
    _, pull_one = jax.vjp(lambda hidden: activate(hidden, gain_one), hidden_one)
    grad_hidden_one = pull_one(grad_act_one)[0].astype(jnp.bfloat16)
    input_part, weight_grad_one = backward_conv(
        gathered_one, halo_one, kernel_map, conv_one, grad_hidden_one, border_hot, halo_target, border_list
    )
    grad_x_zero = grad_block + input_part
    scaled = (grad_x_zero * inverse[:, None]).astype(jnp.bfloat16)
    slot_values = jnp.einsum(
        "sv,vc->sc", slot_match, scaled, preferred_element_type=jnp.float32
    ).astype(jnp.bfloat16)
    returned = return_grads(slot_values.reshape(devices, capacity, channels)).reshape(-1, channels)
    grad_points = jnp.einsum(
        "sp,sc->pc", slot_hot, returned, preferred_element_type=jnp.float32
    ).astype(jnp.bfloat16)
    parts = (weight_grad_one, weight_grad_two, grad_in_part, grad_bias_part, grad_out_part, loss_part)
    summed = tree_psum(parts)
    (
        grad_conv_one,
        grad_conv_two,
        grad_decoder_in,
        grad_decoder_bias,
        grad_decoder_out,
        loss_value,
    ) = summed
    return (
        sdf_values,
        loss_value,
        grad_conv_one,
        grad_conv_two,
        grad_decoder_in,
        grad_decoder_bias,
        grad_decoder_out,
        grad_points,
    )


def solution(mesh):
    in_specs = (
        P(("gx", "gy"), None),
        P(("gx", "gy"), None),
        P(("gx", "gy")),
        P(None, ("gx", "gy")),
        P("gx", "gy", None),
        P(),
        P(),
        P(),
        P(),
        P(),
        P(),
        P(),
        P(("gx", "gy")),
    )
    out_specs = (P(("gx", "gy")), P(), P(), P(), P(), P(), P(), P(("gx", "gy"), None))
    return jax.shard_map(local, mesh=mesh, in_specs=in_specs, out_specs=out_specs, check_vma=False)
```

```python
import math

import jax
import numpy as np
import jax.numpy as jnp
from jax import lax
from jax.sharding import PartitionSpec as P

EPS = 1e-05


def with_halo(array, sides, width):
    for axis, dim in sides:
        peers, length = (lax.axis_size(axis), array.shape[dim])
        up = [(i, (i + 1) % peers) for i in range(peers - 1)]
        down = [(j, i) for i, j in up]
        last = lax.slice_in_dim(array, length - width, length, axis=dim)
        leading = lax.slice_in_dim(array, 0, width, axis=dim)
        before = lax.ppermute(last, axis, up)
        after = lax.ppermute(leading, axis, down)
        array = jnp.concatenate([before, array, after], axis=dim)
    return array


def activate(hidden, gain_vec):
    inverse_rms = lax.rsqrt(jnp.mean(hidden * hidden, axis=-1, keepdims=True) + EPS)
    return jax.nn.silu(hidden * inverse_rms * gain_vec)


def build_table(features, border_list):
    channels = features.shape[1]
    edge_rows = features[border_list]
    neighbour_rows = with_halo(edge_rows, (("gx", 0), ("gy", 1)), 1)
    zero_row = jnp.zeros((1, channels), features.dtype)
    return jnp.concatenate([features, neighbour_rows.reshape(-1, channels), zero_row], axis=0)


def gather_local(rows, kernel_map):
    voxels = rows.shape[0]
    local_rows = jnp.arange(voxels, dtype=jnp.int32)
    selector = (kernel_map[:, :, None] == local_rows[None, None, :]).astype(rows.dtype)
    picked = jnp.einsum("kvu,uc->kvc", selector, rows, preferred_element_type=jnp.float32)
    return picked.astype(rows.dtype)


def halo_layout(kernel_map, border_list):
    voxels = kernel_map.shape[1]
    boundary = border_list.shape[2]
    border_flat = border_list.reshape(-1)
    border_hot = (jnp.arange(voxels, dtype=jnp.int32)[:, None] == border_flat[None, :])
    named = jnp.einsum(
        "kv,vb->kb",
        kernel_map.astype(jnp.float32),
        border_hot.astype(jnp.float32),
        precision=lax.Precision.HIGHEST,
    )
    expected = np.zeros((27, 2, 2, boundary), np.int32)
    for k in range(27):
        step_x, step_y = k // 9 - 1, k // 3 % 3 - 1
        for i in range(2):
            for j in range(2):
                cell = (i + 1 + step_x) * 4 + (j + 1 + step_y)
                expected[k, i, j] = cell * boundary + np.arange(boundary)
    expected = jnp.asarray(expected.reshape(27, -1))
    flag = named == (expected + voxels).astype(jnp.float32)
    target = jnp.where(flag, expected, -1)
    return border_hot, target


def halo_hot(target, halo_count):
    return target[:, :, None] == jnp.arange(halo_count, dtype=jnp.int32)[None, None, :]


def halo_pick(halo, target):
    channels = halo.shape[-1]
    flat = halo.reshape(-1, channels)
    picked = jnp.einsum(
        "kbr,rc->kbc",
        halo_hot(target, flat.shape[0]).astype(flat.dtype),
        flat,
        preferred_element_type=jnp.float32,
    )
    return picked.astype(halo.dtype)


def edge_halo(features, border_hot, border_list):
    channels = features.shape[1]
    edge_rows = jnp.einsum(
        "vb,vc->bc", border_hot.astype(features.dtype), features, preferred_element_type=jnp.float32
    ).astype(features.dtype)
    edge_rows = edge_rows.reshape(border_list.shape + (channels,))
    return with_halo(edge_rows, (("gx", 0), ("gy", 1)), 1)


def conv_forward(features, kernel_map, border_list, border_hot, target, weight):
    gathered = gather_local(features, kernel_map)
    halo_rows = halo_pick(edge_halo(features, border_hot, border_list), target)
    local_out = jnp.einsum("kvc,kcd->vd", gathered, weight, preferred_element_type=jnp.float32)
    border_out = jnp.einsum("kbc,kcd->bd", halo_rows, weight, preferred_element_type=jnp.float32)
    placed = jnp.einsum(
        "vb,bd->vd", border_hot.astype(jnp.float32), border_out, precision=lax.Precision.HIGHEST
    )
    return local_out + placed, gathered, halo_rows


def backward_conv(gathered, halo_rows, kernel_map, weight, grad_rows, border_hot, target, border_list):
    grad_border = jnp.einsum(
        "vb,vd->bd", border_hot.astype(grad_rows.dtype), grad_rows, preferred_element_type=jnp.float32
    ).astype(grad_rows.dtype)
    weight_grad = jnp.einsum(
        "kvc,vd->kcd", gathered, grad_rows, preferred_element_type=jnp.float32
    ) + jnp.einsum("kbc,bd->kcd", halo_rows, grad_border, preferred_element_type=jnp.float32)
    flipped_weight = jnp.swapaxes(weight[::-1], 1, 2)
    grad_gathered = gather_local(grad_rows, kernel_map)
    local_part = jnp.einsum(
        "kvc,kcd->vd", grad_gathered, flipped_weight, preferred_element_type=jnp.float32
    )
    channels = grad_rows.shape[1]
    boundary = border_list.shape[2]
    spread = jnp.einsum(
        "kbr,bd->rkd",
        halo_hot(target, 16 * boundary).astype(grad_border.dtype),
        grad_border,
        preferred_element_type=jnp.float32,
    ).astype(grad_border.dtype)
    halo_grad = jnp.einsum(
        "rkd,kcd->rc", spread, weight, preferred_element_type=jnp.float32
    ).reshape(4, 4, boundary, channels)
    rows_end = jnp.stack([halo_grad[0], halo_grad[3]], axis=0)
    cols_end = jnp.stack([halo_grad[:, 0], halo_grad[:, 3]], axis=1)
    corner_end = jnp.stack([rows_end[:, 0], rows_end[:, 3]], axis=1)
    payload = jnp.stack([rows_end[:, 1:3], cols_end[1:3], corner_end], axis=2)
    received = with_halo(payload.astype(jnp.bfloat16), (("gx", 0), ("gy", 1)), 1).astype(
        payload.dtype
    )
    from_rows = jnp.stack([received[0, 1:3, 0], received[3, 1:3, 0]], axis=0)
    from_cols = jnp.stack([received[1:3, 0, 1], received[1:3, 3, 1]], axis=1)
    corner_low = jnp.stack([received[0, 0, 2], received[0, 3, 2]], axis=0)
    corner_high = jnp.stack([received[3, 0, 2], received[3, 3, 2]], axis=0)
    from_corner = jnp.stack([corner_low, corner_high], axis=0)
    folded = halo_grad[1:3, 1:3] + from_rows + from_cols + from_corner
    result = local_part + jnp.einsum(
        "vb,bd->vd",
        border_hot.astype(jnp.float32),
        folded.reshape(-1, channels),
        precision=lax.Precision.HIGHEST,
    )
    return (result, weight_grad)


TREE_STEPS = (("gy", 1, 2), ("gy", 2, 4), ("gx", 1, 4), ("gx", 4, 4))


def tree_psum(parts):
    flat = jnp.concatenate([jnp.ravel(p).astype(jnp.float32) for p in parts])
    lanes = 128
    spread = math.prod(radix for _, _, radix in TREE_STEPS)
    rows = -(-flat.shape[0] // lanes)
    rows = -(-rows // (8 * spread)) * (8 * spread)
    x = jnp.pad(flat, (0, rows * lanes - flat.shape[0])).reshape(rows, lanes)
    digits = []
    for axis, stride, radix in TREE_STEPS:
        peers = lax.axis_size(axis)
        digit = (lax.axis_index(axis) // stride) % radix
        digits.append(digit)
        pieces = x.reshape(radix, x.shape[0] // radix, lanes)
        total = lax.dynamic_index_in_dim(pieces, digit, 0, keepdims=False)
        for shift in range(1, radix):
            outgoing = lax.dynamic_index_in_dim(pieces, (digit + shift) % radix, 0, keepdims=False)
            pairs = [
                (i, i + (((i // stride) % radix + shift) % radix - (i // stride) % radix) * stride)
                for i in range(peers)
            ]
            total = total + lax.ppermute(outgoing, axis, pairs)
        x = total
    for (axis, stride, radix), digit in reversed(list(zip(TREE_STEPS, digits))):
        peers = lax.axis_size(axis)
        held = [x]
        for shift in range(1, radix):
            pairs = [
                (i, i + (((i // stride) % radix + shift) % radix - (i // stride) % radix) * stride)
                for i in range(peers)
            ]
            held.append(lax.ppermute(x, axis, pairs))
        backwards = jnp.stack(held[::-1] * 2, axis=0)
        x = lax.dynamic_slice_in_dim(backwards, (radix - 1 - digit) % radix, radix, axis=0)
        x = x.reshape(-1, lanes)
    flat = x.reshape(-1)
    out, start = [], 0
    for p in parts:
        size = math.prod(p.shape)
        out.append(flat[start:start + size].reshape(p.shape))
        start += size
    return tuple(out)


def slot_positions(destination, devices, capacity):
    points = destination.shape[0]
    block = math.gcd(points, 128)
    blocks = points // block
    dest_hot = destination[:, None] == jnp.arange(devices, dtype=jnp.int32)[None, :]
    grouped = dest_hot.astype(jnp.bfloat16).reshape(blocks, block, devices)
    lower = (
        jnp.arange(block, dtype=jnp.int32)[:, None] > jnp.arange(block, dtype=jnp.int32)[None, :]
    ).astype(jnp.bfloat16)
    within = jnp.einsum("ij,bjd->bid", lower, grouped, preferred_element_type=jnp.float32)
    totals = jnp.sum(grouped.astype(jnp.float32), axis=1)
    lower_blocks = (
        jnp.arange(blocks, dtype=jnp.int32)[:, None] > jnp.arange(blocks, dtype=jnp.int32)[None, :]
    ).astype(jnp.float32)
    offsets = jnp.einsum("ab,bd->ad", lower_blocks, totals, precision=lax.Precision.HIGHEST)
    earlier = (within + offsets[:, None, :]).reshape(points, devices)
    rank = jnp.sum(jnp.where(dest_hot, earlier, 0.0), axis=1).astype(jnp.int32)
    return destination * capacity + rank


def send_points(send_rows):
    return lax.all_to_all(send_rows, ("gx", "gy"), split_axis=0, concat_axis=0, tiled=True)


def return_grads(slot_grads):
    returned = lax.all_to_all(slot_grads, ("gx", "gy"), split_axis=0, concat_axis=0, tiled=True)
    return returned


def local(
    point_feats,
    point_dest,
    point_voxel,
    kernel_map,
    border_list,
    conv_one,
    conv_two,
    gain_one,
    gain_two,
    decoder_in,
    decoder_bias,
    decoder_out,
    target,
):
    devices = lax.axis_size("gx") * lax.axis_size("gy")
    voxels = kernel_map.shape[1]
    points, channels = point_feats.shape
    capacity = 2 * points // devices
    destination = point_dest[:, 0]
    position = slot_positions(destination, devices, capacity)
    slot_hot = (
        jnp.arange(devices * capacity, dtype=jnp.int32)[:, None] == position[None, :]
    ).astype(jnp.bfloat16)
    id_high = (point_voxel // 32 + 1).astype(jnp.bfloat16)
    id_low = (point_voxel % 32).astype(jnp.bfloat16)
    payload = jnp.concatenate(
        [
            point_feats,
            jnp.ones((points, 1), jnp.bfloat16),
            id_high[:, None],
            id_low[:, None],
        ],
        axis=1,
    )
    send = jnp.einsum(
        "sp,pc->sc", slot_hot, payload, preferred_element_type=jnp.float32
    ).astype(jnp.bfloat16)
    got = send_points(send.reshape(devices, capacity * (channels + 3))).reshape(-1, channels + 3)
    flat_ids = ((got[:, channels + 1].astype(jnp.float32) - 1.0) * 32.0 + got[:, channels + 2].astype(jnp.float32)).astype(jnp.int32)
    voxel_rows = jnp.arange(voxels, dtype=jnp.int32)
    slot_match = (flat_ids[:, None] == voxel_rows[None, :]).astype(jnp.bfloat16)
    pooled = jnp.einsum(
        "sv,sc->vc", slot_match, got[:, : channels + 1], preferred_element_type=jnp.float32
    )
    pooled_sum = pooled[:, :channels]
    counts = pooled[:, channels]
    inverse = 1.0 / jnp.maximum(counts, 1.0)
    x_zero = (pooled_sum * inverse[:, None]).astype(jnp.bfloat16)
    border_hot, halo_target = halo_layout(kernel_map, border_list)
    hidden_one, gathered_one, halo_one = conv_forward(
        x_zero, kernel_map, border_list, border_hot, halo_target, conv_one
    )
    act_one = activate(hidden_one, gain_one).astype(jnp.bfloat16)
    hidden_two, gathered_two, halo_two = conv_forward(
        act_one, kernel_map, border_list, border_hot, halo_target, conv_two
    )
    block_out = (x_zero.astype(jnp.float32) + activate(hidden_two, gain_two)).astype(jnp.bfloat16)
    pre_dec = jnp.dot(block_out, decoder_in, preferred_element_type=jnp.float32) + decoder_bias
    dec_hidden = jax.nn.silu(pre_dec)
    sdf_values = jnp.sum(dec_hidden * decoder_out, axis=-1)
    whole_count = voxels * devices
    error_sdf = sdf_values - target
    loss_part = jnp.sum(error_sdf * error_sdf) / (2.0 * whole_count)
    grad_sdf = error_sdf / whole_count
    grad_out_part = jnp.sum(dec_hidden * grad_sdf[:, None], axis=0)
    _, pull_silu = jax.vjp(jax.nn.silu, pre_dec)
    grad_pre = pull_silu(grad_sdf[:, None] * decoder_out)[0]
    grad_bias_part = jnp.sum(grad_pre, axis=0)
    grad_pre_low = grad_pre.astype(jnp.bfloat16)
    grad_in_part = lax.dot_general(
        block_out, grad_pre_low, (((0,), (0,)), ((), ())), preferred_element_type=jnp.float32
    )
    grad_block = lax.dot_general(
        grad_pre_low, decoder_in, (((1,), (1,)), ((), ())), preferred_element_type=jnp.float32
    )
    _, pull_two = jax.vjp(lambda hidden: activate(hidden, gain_two), hidden_two)
    grad_hidden_two = pull_two(grad_block)[0].astype(jnp.bfloat16)
    grad_act_one, weight_grad_two = backward_conv(
        gathered_two, halo_two, kernel_map, conv_two, grad_hidden_two, border_hot, halo_target, border_list
    )
    _, pull_one = jax.vjp(lambda hidden: activate(hidden, gain_one), hidden_one)
    grad_hidden_one = pull_one(grad_act_one)[0].astype(jnp.bfloat16)
    input_part, weight_grad_one = backward_conv(
        gathered_one, halo_one, kernel_map, conv_one, grad_hidden_one, border_hot, halo_target, border_list
    )
    grad_x_zero = grad_block + input_part
    scaled = (grad_x_zero * inverse[:, None]).astype(jnp.bfloat16)
    slot_values = jnp.einsum(
        "sv,vc->sc", slot_match, scaled, preferred_element_type=jnp.float32
    ).astype(jnp.bfloat16)
    returned = return_grads(slot_values.reshape(devices, capacity, channels)).reshape(-1, channels)
    grad_points = jnp.einsum(
        "sp,sc->pc", slot_hot, returned, preferred_element_type=jnp.float32
    ).astype(jnp.bfloat16)
    parts = (weight_grad_one, weight_grad_two, grad_in_part, grad_bias_part, grad_out_part, loss_part)
    summed = tree_psum(parts)
    (
        grad_conv_one,
        grad_conv_two,
        grad_decoder_in,
        grad_decoder_bias,
        grad_decoder_out,
        loss_value,
    ) = summed
    return (
        sdf_values,
        loss_value,
        grad_conv_one,
        grad_conv_two,
        grad_decoder_in,
        grad_decoder_bias,
        grad_decoder_out,
        grad_points,
    )


def solution(mesh):
    in_specs = (
        P(("gx", "gy"), None),
        P(("gx", "gy"), None),
        P(("gx", "gy")),
        P(None, ("gx", "gy")),
        P("gx", "gy", None),
        P(),
        P(),
        P(),
        P(),
        P(),
        P(),
        P(),
        P(("gx", "gy")),
    )
    out_specs = (P(("gx", "gy")), P(), P(), P(), P(), P(), P(), P(("gx", "gy"), None))
    return jax.shard_map(local, mesh=mesh, in_specs=in_specs, out_specs=out_specs, check_vma=False)
```

```python
import math

import jax
import numpy as np
import jax.numpy as jnp
from jax import lax
from jax.sharding import PartitionSpec as P

EPS = 1e-05


def with_halo(array, sides, width):
    for axis, dim in sides:
        peers, length = (lax.axis_size(axis), array.shape[dim])
        up = [(i, (i + 1) % peers) for i in range(peers - 1)]
        down = [(j, i) for i, j in up]
        last = lax.slice_in_dim(array, length - width, length, axis=dim)
        leading = lax.slice_in_dim(array, 0, width, axis=dim)
        before = lax.ppermute(last, axis, up)
        after = lax.ppermute(leading, axis, down)
        array = jnp.concatenate([before, array, after], axis=dim)
    return array


def activate(hidden, gain_vec):
    inverse_rms = lax.rsqrt(jnp.mean(hidden * hidden, axis=-1, keepdims=True) + EPS)
    return jax.nn.silu(hidden * inverse_rms * gain_vec)


def build_table(features, border_list):
    channels = features.shape[1]
    edge_rows = features[border_list]
    neighbour_rows = with_halo(edge_rows, (("gx", 0), ("gy", 1)), 1)
    zero_row = jnp.zeros((1, channels), features.dtype)
    return jnp.concatenate([features, neighbour_rows.reshape(-1, channels), zero_row], axis=0)


def gather_local(rows, kernel_map):
    voxels = rows.shape[0]
    local_rows = jnp.arange(voxels, dtype=jnp.int32)
    selector = (kernel_map[:, :, None] == local_rows[None, None, :]).astype(rows.dtype)
    picked = jnp.einsum("kvu,uc->kvc", selector, rows, preferred_element_type=jnp.float32)
    return picked.astype(rows.dtype)


def halo_layout(kernel_map, border_list):
    voxels = kernel_map.shape[1]
    boundary = border_list.shape[2]
    border_flat = border_list.reshape(-1)
    border_hot = (jnp.arange(voxels, dtype=jnp.int32)[:, None] == border_flat[None, :])
    named = jnp.einsum(
        "kv,vb->kb",
        kernel_map.astype(jnp.float32),
        border_hot.astype(jnp.float32),
        precision=lax.Precision.HIGHEST,
    )
    expected = np.zeros((27, 2, 2, boundary), np.int32)
    for k in range(27):
        step_x, step_y = k // 9 - 1, k // 3 % 3 - 1
        for i in range(2):
            for j in range(2):
                cell = (i + 1 + step_x) * 4 + (j + 1 + step_y)
                expected[k, i, j] = cell * boundary + np.arange(boundary)
    expected = jnp.asarray(expected.reshape(27, -1))
    flag = named == (expected + voxels).astype(jnp.float32)
    target = jnp.where(flag, expected, -1)
    return border_hot, target


def halo_hot(target, halo_count):
    return target[:, :, None] == jnp.arange(halo_count, dtype=jnp.int32)[None, None, :]


def halo_pick(halo, target):
    channels = halo.shape[-1]
    flat = halo.reshape(-1, channels)
    picked = jnp.einsum(
        "kbr,rc->kbc",
        halo_hot(target, flat.shape[0]).astype(flat.dtype),
        flat,
        preferred_element_type=jnp.float32,
    )
    return picked.astype(halo.dtype)


def edge_halo(features, border_hot, border_list):
    channels = features.shape[1]
    edge_rows = jnp.einsum(
        "vb,vc->bc", border_hot.astype(features.dtype), features, preferred_element_type=jnp.float32
    ).astype(features.dtype)
    edge_rows = edge_rows.reshape(border_list.shape + (channels,))
    return with_halo(edge_rows, (("gx", 0), ("gy", 1)), 1)


def conv_forward(features, kernel_map, border_list, border_hot, target, weight):
    gathered = gather_local(features, kernel_map)
    halo_rows = halo_pick(edge_halo(features, border_hot, border_list), target)
    local_out = jnp.einsum("kvc,kcd->vd", gathered, weight, preferred_element_type=jnp.float32)
    border_out = jnp.einsum("kbc,kcd->bd", halo_rows, weight, preferred_element_type=jnp.float32)
    placed = jnp.einsum(
        "vb,bd->vd", border_hot.astype(jnp.float32), border_out, precision=lax.Precision.HIGHEST
    )
    return local_out + placed, gathered, halo_rows


def backward_conv(gathered, halo_rows, kernel_map, weight, grad_rows, border_hot, target, border_list):
    grad_border = jnp.einsum(
        "vb,vd->bd", border_hot.astype(grad_rows.dtype), grad_rows, preferred_element_type=jnp.float32
    ).astype(grad_rows.dtype)
    weight_grad = jnp.einsum(
        "kvc,vd->kcd", gathered, grad_rows, preferred_element_type=jnp.float32
    ) + jnp.einsum("kbc,bd->kcd", halo_rows, grad_border, preferred_element_type=jnp.float32)
    flipped_weight = jnp.swapaxes(weight[::-1], 1, 2)
    grad_gathered = gather_local(grad_rows, kernel_map)
    local_part = jnp.einsum(
        "kvc,kcd->vd", grad_gathered, flipped_weight, preferred_element_type=jnp.float32
    )
    channels = grad_rows.shape[1]
    boundary = border_list.shape[2]
    spread = jnp.einsum(
        "kbr,bd->rkd",
        halo_hot(target, 16 * boundary).astype(grad_border.dtype),
        grad_border,
        preferred_element_type=jnp.float32,
    ).astype(grad_border.dtype)
    halo_grad = jnp.einsum(
        "rkd,kcd->rc", spread, weight, preferred_element_type=jnp.float32
    ).reshape(4, 4, boundary, channels)
    rows_end = jnp.stack([halo_grad[0], halo_grad[3]], axis=0)
    cols_end = jnp.stack([halo_grad[:, 0], halo_grad[:, 3]], axis=1)
    corner_end = jnp.stack([rows_end[:, 0], rows_end[:, 3]], axis=1)
    payload = jnp.stack([rows_end[:, 1:3], cols_end[1:3], corner_end], axis=2)
    received = with_halo(payload.astype(jnp.bfloat16), (("gx", 0), ("gy", 1)), 1).astype(
        payload.dtype
    )
    from_rows = jnp.stack([received[0, 1:3, 0], received[3, 1:3, 0]], axis=0)
    from_cols = jnp.stack([received[1:3, 0, 1], received[1:3, 3, 1]], axis=1)
    corner_low = jnp.stack([received[0, 0, 2], received[0, 3, 2]], axis=0)
    corner_high = jnp.stack([received[3, 0, 2], received[3, 3, 2]], axis=0)
    from_corner = jnp.stack([corner_low, corner_high], axis=0)
    folded = halo_grad[1:3, 1:3] + from_rows + from_cols + from_corner
    result = local_part + jnp.einsum(
        "vb,bd->vd",
        border_hot.astype(jnp.float32),
        folded.reshape(-1, channels),
        precision=lax.Precision.HIGHEST,
    )
    return (result, weight_grad)


HALVING_STEPS = (("gy", 1), ("gy", 2), ("gx", 1))
DOUBLING_STEPS = (("gx", 4), ("gy", 4), ("gx", 2), ("gx", 8))


def tree_psum(parts):
    flat = jnp.concatenate([jnp.ravel(p).astype(jnp.float32) for p in parts])
    lanes = 128
    rows = -(-flat.shape[0] // lanes)
    rows = -(-rows // (8 * 2 ** len(HALVING_STEPS))) * (8 * 2 ** len(HALVING_STEPS))
    x = jnp.pad(flat, (0, rows * lanes - flat.shape[0])).reshape(rows, lanes)
    bits = []
    for axis, mask in HALVING_STEPS:
        peers = lax.axis_size(axis)
        bit = (lax.axis_index(axis) // mask) % 2
        bits.append(bit)
        half = x.shape[0] // 2
        low, high = x[:half], x[half:]
        send = jnp.where(bit == 1, low, high)
        keep = jnp.where(bit == 1, high, low)
        x = keep + lax.ppermute(send, axis, [(i, i ^ mask) for i in range(peers)])
    for axis, mask in DOUBLING_STEPS:
        peers = lax.axis_size(axis)
        bit = (lax.axis_index(axis) // mask) % 2
        other = lax.ppermute(x, axis, [(i, i ^ mask) for i in range(peers)])
        x = jnp.where(bit == 1, other + x, x + other)
    for (axis, mask), bit in reversed(list(zip(HALVING_STEPS, bits))):
        peers = lax.axis_size(axis)
        other = lax.ppermute(x, axis, [(i, i ^ mask) for i in range(peers)])
        x = jnp.where(bit == 1, jnp.concatenate([other, x]), jnp.concatenate([x, other]))
    flat = x.reshape(-1)
    out, start = [], 0
    for p in parts:
        size = math.prod(p.shape)
        out.append(flat[start:start + size].reshape(p.shape))
        start += size
    return tuple(out)


def slot_positions(destination, devices, capacity):
    points = destination.shape[0]
    block = math.gcd(points, 128)
    blocks = points // block
    dest_hot = destination[:, None] == jnp.arange(devices, dtype=jnp.int32)[None, :]
    grouped = dest_hot.astype(jnp.bfloat16).reshape(blocks, block, devices)
    lower = (
        jnp.arange(block, dtype=jnp.int32)[:, None] > jnp.arange(block, dtype=jnp.int32)[None, :]
    ).astype(jnp.bfloat16)
    within = jnp.einsum("ij,bjd->bid", lower, grouped, preferred_element_type=jnp.float32)
    totals = jnp.sum(grouped.astype(jnp.float32), axis=1)
    lower_blocks = (
        jnp.arange(blocks, dtype=jnp.int32)[:, None] > jnp.arange(blocks, dtype=jnp.int32)[None, :]
    ).astype(jnp.float32)
    offsets = jnp.einsum("ab,bd->ad", lower_blocks, totals, precision=lax.Precision.HIGHEST)
    earlier = (within + offsets[:, None, :]).reshape(points, devices)
    rank = jnp.sum(jnp.where(dest_hot, earlier, 0.0), axis=1).astype(jnp.int32)
    return destination * capacity + rank


def send_points(send_rows):
    return lax.all_to_all(send_rows, ("gx", "gy"), split_axis=0, concat_axis=0, tiled=True)


def return_grads(slot_grads):
    returned = lax.all_to_all(slot_grads, ("gx", "gy"), split_axis=0, concat_axis=0, tiled=True)
    return returned


def local(
    point_feats,
    point_dest,
    point_voxel,
    kernel_map,
    border_list,
    conv_one,
    conv_two,
    gain_one,
    gain_two,
    decoder_in,
    decoder_bias,
    decoder_out,
    target,
):
    devices = lax.axis_size("gx") * lax.axis_size("gy")
    voxels = kernel_map.shape[1]
    points, channels = point_feats.shape
    capacity = 2 * points // devices
    destination = point_dest[:, 0]
    position = slot_positions(destination, devices, capacity)
    slot_hot = (
        jnp.arange(devices * capacity, dtype=jnp.int32)[:, None] == position[None, :]
    ).astype(jnp.bfloat16)
    id_high = (point_voxel // 32 + 1).astype(jnp.bfloat16)
    id_low = (point_voxel % 32).astype(jnp.bfloat16)
    payload = jnp.concatenate(
        [
            point_feats,
            jnp.ones((points, 1), jnp.bfloat16),
            id_high[:, None],
            id_low[:, None],
        ],
        axis=1,
    )
    send = jnp.einsum(
        "sp,pc->sc", slot_hot, payload, preferred_element_type=jnp.float32
    ).astype(jnp.bfloat16)
    got = send_points(send.reshape(devices, capacity, channels + 3)).reshape(-1, channels + 3)
    flat_ids = ((got[:, channels + 1].astype(jnp.float32) - 1.0) * 32.0 + got[:, channels + 2].astype(jnp.float32)).astype(jnp.int32)
    voxel_rows = jnp.arange(voxels, dtype=jnp.int32)
    slot_match = (flat_ids[:, None] == voxel_rows[None, :]).astype(jnp.bfloat16)
    pooled = jnp.einsum(
        "sv,sc->vc", slot_match, got[:, : channels + 1], preferred_element_type=jnp.float32
    )
    pooled_sum = pooled[:, :channels]
    counts = pooled[:, channels]
    inverse = 1.0 / jnp.maximum(counts, 1.0)
    x_zero = (pooled_sum * inverse[:, None]).astype(jnp.bfloat16)
    border_hot, halo_target = halo_layout(kernel_map, border_list)
    hidden_one, gathered_one, halo_one = conv_forward(
        x_zero, kernel_map, border_list, border_hot, halo_target, conv_one
    )
    act_one = activate(hidden_one, gain_one).astype(jnp.bfloat16)
    hidden_two, gathered_two, halo_two = conv_forward(
        act_one, kernel_map, border_list, border_hot, halo_target, conv_two
    )
    block_out = (x_zero.astype(jnp.float32) + activate(hidden_two, gain_two)).astype(jnp.bfloat16)
    pre_dec = jnp.dot(block_out, decoder_in, preferred_element_type=jnp.float32) + decoder_bias
    dec_hidden = jax.nn.silu(pre_dec)
    sdf_values = jnp.sum(dec_hidden * decoder_out, axis=-1)
    whole_count = voxels * devices
    error_sdf = sdf_values - target
    loss_part = jnp.sum(error_sdf * error_sdf) / (2.0 * whole_count)
    grad_sdf = error_sdf / whole_count
    grad_out_part = jnp.sum(dec_hidden * grad_sdf[:, None], axis=0)
    _, pull_silu = jax.vjp(jax.nn.silu, pre_dec)
    grad_pre = pull_silu(grad_sdf[:, None] * decoder_out)[0]
    grad_bias_part = jnp.sum(grad_pre, axis=0)
    grad_pre_low = grad_pre.astype(jnp.bfloat16)
    grad_in_part = lax.dot_general(
        block_out, grad_pre_low, (((0,), (0,)), ((), ())), preferred_element_type=jnp.float32
    )
    grad_block = lax.dot_general(
        grad_pre_low, decoder_in, (((1,), (1,)), ((), ())), preferred_element_type=jnp.float32
    )
    _, pull_two = jax.vjp(lambda hidden: activate(hidden, gain_two), hidden_two)
    grad_hidden_two = pull_two(grad_block)[0].astype(jnp.bfloat16)
    grad_act_one, weight_grad_two = backward_conv(
        gathered_two, halo_two, kernel_map, conv_two, grad_hidden_two, border_hot, halo_target, border_list
    )
    _, pull_one = jax.vjp(lambda hidden: activate(hidden, gain_one), hidden_one)
    grad_hidden_one = pull_one(grad_act_one)[0].astype(jnp.bfloat16)
    input_part, weight_grad_one = backward_conv(
        gathered_one, halo_one, kernel_map, conv_one, grad_hidden_one, border_hot, halo_target, border_list
    )
    grad_x_zero = grad_block + input_part
    scaled = (grad_x_zero * inverse[:, None]).astype(jnp.bfloat16)
    slot_values = jnp.einsum(
        "sv,vc->sc", slot_match, scaled, preferred_element_type=jnp.float32
    ).astype(jnp.bfloat16)
    returned = return_grads(slot_values.reshape(devices, capacity, channels)).reshape(-1, channels)
    grad_points = jnp.einsum(
        "sp,sc->pc", slot_hot, returned, preferred_element_type=jnp.float32
    ).astype(jnp.bfloat16)
    parts = (weight_grad_one, weight_grad_two, grad_in_part, grad_bias_part, grad_out_part, loss_part)
    summed = tree_psum(parts)
    (
        grad_conv_one,
        grad_conv_two,
        grad_decoder_in,
        grad_decoder_bias,
        grad_decoder_out,
        loss_value,
    ) = summed
    return (
        sdf_values,
        loss_value,
        grad_conv_one,
        grad_conv_two,
        grad_decoder_in,
        grad_decoder_bias,
        grad_decoder_out,
        grad_points,
    )


def solution(mesh):
    in_specs = (
        P(("gx", "gy"), None),
        P(("gx", "gy"), None),
        P(("gx", "gy")),
        P(None, ("gx", "gy")),
        P("gx", "gy", None),
        P(),
        P(),
        P(),
        P(),
        P(),
        P(),
        P(),
        P(("gx", "gy")),
    )
    out_specs = (P(("gx", "gy")), P(), P(), P(), P(), P(), P(), P(("gx", "gy"), None))
    return jax.shard_map(local, mesh=mesh, in_specs=in_specs, out_specs=out_specs, check_vma=False)
```

```python
import math

import jax
import numpy as np
import jax.numpy as jnp
from jax import lax
from jax.sharding import PartitionSpec as P

EPS = 1e-05


def with_halo(array, sides, width):
    for axis, dim in sides:
        peers, length = (lax.axis_size(axis), array.shape[dim])
        up = [(i, (i + 1) % peers) for i in range(peers - 1)]
        down = [(j, i) for i, j in up]
        last = lax.slice_in_dim(array, length - width, length, axis=dim)
        leading = lax.slice_in_dim(array, 0, width, axis=dim)
        before = lax.ppermute(last, axis, up)
        after = lax.ppermute(leading, axis, down)
        array = jnp.concatenate([before, array, after], axis=dim)
    return array


def activate(hidden, gain_vec):
    inverse_rms = lax.rsqrt(jnp.mean(hidden * hidden, axis=-1, keepdims=True) + EPS)
    return jax.nn.silu(hidden * inverse_rms * gain_vec)


def build_table(features, border_list):
    channels = features.shape[1]
    edge_rows = features[border_list]
    neighbour_rows = with_halo(edge_rows, (("gx", 0), ("gy", 1)), 1)
    zero_row = jnp.zeros((1, channels), features.dtype)
    return jnp.concatenate([features, neighbour_rows.reshape(-1, channels), zero_row], axis=0)


def gather_local(rows, kernel_map):
    voxels, channels = rows.shape
    chunk = 256 if voxels % 256 == 0 else voxels
    chunks = voxels // chunk
    starts = chunk * jnp.arange(chunks, dtype=jnp.int32)
    shifted = (kernel_map[:, :, None] - starts[None, None, :]).astype(jnp.bfloat16)
    within = jnp.arange(chunk, dtype=jnp.int32).astype(jnp.bfloat16)
    selector = (shifted[:, :, :, None] == within[None, None, None, :]).astype(rows.dtype)
    picked = jnp.einsum(
        "kvcu,cud->kvd",
        selector,
        rows.reshape(chunks, chunk, channels),
        preferred_element_type=jnp.float32,
    )
    return picked.astype(rows.dtype)


def halo_layout(kernel_map, border_list):
    voxels = kernel_map.shape[1]
    boundary = border_list.shape[2]
    border_flat = border_list.reshape(-1)
    border_hot = (jnp.arange(voxels, dtype=jnp.int32)[:, None] == border_flat[None, :])
    named = jnp.einsum(
        "kv,vb->kb",
        kernel_map.astype(jnp.float32),
        border_hot.astype(jnp.float32),
        precision=lax.Precision.HIGHEST,
    )
    expected = np.zeros((27, 2, 2, boundary), np.int32)
    for k in range(27):
        step_x, step_y = k // 9 - 1, k // 3 % 3 - 1
        for i in range(2):
            for j in range(2):
                cell = (i + 1 + step_x) * 4 + (j + 1 + step_y)
                expected[k, i, j] = cell * boundary + np.arange(boundary)
    expected = jnp.asarray(expected.reshape(27, -1))
    flag = named == (expected + voxels).astype(jnp.float32)
    target = jnp.where(flag, expected, -1)
    return border_hot, target


def halo_hot(target, halo_count):
    return target[:, :, None] == jnp.arange(halo_count, dtype=jnp.int32)[None, None, :]


def halo_pick(halo, target):
    channels = halo.shape[-1]
    flat = halo.reshape(-1, channels)
    picked = jnp.einsum(
        "kbr,rc->kbc",
        halo_hot(target, flat.shape[0]).astype(flat.dtype),
        flat,
        preferred_element_type=jnp.float32,
    )
    return picked.astype(halo.dtype)


def edge_halo(features, border_hot, border_list):
    channels = features.shape[1]
    edge_rows = jnp.einsum(
        "vb,vc->bc", border_hot.astype(features.dtype), features, preferred_element_type=jnp.float32
    ).astype(features.dtype)
    edge_rows = edge_rows.reshape(border_list.shape + (channels,))
    return with_halo(edge_rows, (("gx", 0), ("gy", 1)), 1)


def conv_forward(features, kernel_map, border_list, border_hot, target, weight):
    gathered = gather_local(features, kernel_map)
    halo_rows = halo_pick(edge_halo(features, border_hot, border_list), target)
    local_out = jnp.einsum("kvc,kcd->vd", gathered, weight, preferred_element_type=jnp.float32)
    border_out = jnp.einsum("kbc,kcd->bd", halo_rows, weight, preferred_element_type=jnp.float32)
    placed = jnp.einsum(
        "vb,bd->vd", border_hot.astype(jnp.float32), border_out, precision=lax.Precision.HIGHEST
    )
    return local_out + placed, gathered, halo_rows


def backward_conv(gathered, halo_rows, kernel_map, weight, grad_rows, border_hot, target, border_list):
    grad_border = jnp.einsum(
        "vb,vd->bd", border_hot.astype(grad_rows.dtype), grad_rows, preferred_element_type=jnp.float32
    ).astype(grad_rows.dtype)
    weight_grad = jnp.einsum(
        "kvc,vd->kcd", gathered, grad_rows, preferred_element_type=jnp.float32
    ) + jnp.einsum("kbc,bd->kcd", halo_rows, grad_border, preferred_element_type=jnp.float32)
    flipped_weight = jnp.swapaxes(weight[::-1], 1, 2)
    grad_gathered = gather_local(grad_rows, kernel_map)
    local_part = jnp.einsum(
        "kvc,kcd->vd", grad_gathered, flipped_weight, preferred_element_type=jnp.float32
    )
    channels = grad_rows.shape[1]
    boundary = border_list.shape[2]
    spread = jnp.einsum(
        "kbr,bd->rkd",
        halo_hot(target, 16 * boundary).astype(grad_border.dtype),
        grad_border,
        preferred_element_type=jnp.float32,
    ).astype(grad_border.dtype)
    halo_grad = jnp.einsum(
        "rkd,kcd->rc", spread, weight, preferred_element_type=jnp.float32
    ).reshape(4, 4, boundary, channels)
    rows_end = jnp.stack([halo_grad[0], halo_grad[3]], axis=0)
    cols_end = jnp.stack([halo_grad[:, 0], halo_grad[:, 3]], axis=1)
    corner_end = jnp.stack([rows_end[:, 0], rows_end[:, 3]], axis=1)
    payload = jnp.stack([rows_end[:, 1:3], cols_end[1:3], corner_end], axis=2)
    received = with_halo(payload.astype(jnp.bfloat16), (("gx", 0), ("gy", 1)), 1).astype(
        payload.dtype
    )
    from_rows = jnp.stack([received[0, 1:3, 0], received[3, 1:3, 0]], axis=0)
    from_cols = jnp.stack([received[1:3, 0, 1], received[1:3, 3, 1]], axis=1)
    corner_low = jnp.stack([received[0, 0, 2], received[0, 3, 2]], axis=0)
    corner_high = jnp.stack([received[3, 0, 2], received[3, 3, 2]], axis=0)
    from_corner = jnp.stack([corner_low, corner_high], axis=0)
    folded = halo_grad[1:3, 1:3] + from_rows + from_cols + from_corner
    result = local_part + jnp.einsum(
        "vb,bd->vd",
        border_hot.astype(jnp.float32),
        folded.reshape(-1, channels),
        precision=lax.Precision.HIGHEST,
    )
    return (result, weight_grad)


HALVING_STEPS = (("gy", 1), ("gy", 2), ("gx", 1))
DOUBLING_STEPS = (("gx", 4), ("gy", 4), ("gx", 2), ("gx", 8))


def tree_psum(parts):
    flat = jnp.concatenate([jnp.ravel(p).astype(jnp.float32) for p in parts])
    lanes = 128
    rows = -(-flat.shape[0] // lanes)
    rows = -(-rows // (8 * 2 ** len(HALVING_STEPS))) * (8 * 2 ** len(HALVING_STEPS))
    x = jnp.pad(flat, (0, rows * lanes - flat.shape[0])).reshape(rows, lanes)
    bits = []
    for axis, mask in HALVING_STEPS:
        peers = lax.axis_size(axis)
        bit = (lax.axis_index(axis) // mask) % 2
        bits.append(bit)
        half = x.shape[0] // 2
        low, high = x[:half], x[half:]
        send = jnp.where(bit == 1, low, high)
        keep = jnp.where(bit == 1, high, low)
        x = keep + lax.ppermute(send, axis, [(i, i ^ mask) for i in range(peers)])
    for axis, mask in DOUBLING_STEPS:
        peers = lax.axis_size(axis)
        bit = (lax.axis_index(axis) // mask) % 2
        other = lax.ppermute(x, axis, [(i, i ^ mask) for i in range(peers)])
        x = jnp.where(bit == 1, other + x, x + other)
    for (axis, mask), bit in reversed(list(zip(HALVING_STEPS, bits))):
        peers = lax.axis_size(axis)
        other = lax.ppermute(x, axis, [(i, i ^ mask) for i in range(peers)])
        x = jnp.where(bit == 1, jnp.concatenate([other, x]), jnp.concatenate([x, other]))
    flat = x.reshape(-1)
    out, start = [], 0
    for p in parts:
        size = math.prod(p.shape)
        out.append(flat[start:start + size].reshape(p.shape))
        start += size
    return tuple(out)


def slot_positions(destination, devices, capacity):
    points = destination.shape[0]
    block = math.gcd(points, 128)
    blocks = points // block
    dest_hot = destination[:, None] == jnp.arange(devices, dtype=jnp.int32)[None, :]
    grouped = dest_hot.astype(jnp.bfloat16).reshape(blocks, block, devices)
    lower = (
        jnp.arange(block, dtype=jnp.int32)[:, None] > jnp.arange(block, dtype=jnp.int32)[None, :]
    ).astype(jnp.bfloat16)
    within = jnp.einsum("ij,bjd->bid", lower, grouped, preferred_element_type=jnp.float32)
    totals = jnp.sum(grouped.astype(jnp.float32), axis=1)
    lower_blocks = (
        jnp.arange(blocks, dtype=jnp.int32)[:, None] > jnp.arange(blocks, dtype=jnp.int32)[None, :]
    ).astype(jnp.float32)
    offsets = jnp.einsum("ab,bd->ad", lower_blocks, totals, precision=lax.Precision.HIGHEST)
    earlier = (within + offsets[:, None, :]).reshape(points, devices)
    rank = jnp.sum(jnp.where(dest_hot, earlier, 0.0), axis=1).astype(jnp.int32)
    return destination * capacity + rank


def send_points(send_rows):
    return lax.all_to_all(send_rows, ("gx", "gy"), split_axis=0, concat_axis=0, tiled=True)


def return_grads(slot_grads):
    returned = lax.all_to_all(slot_grads, ("gx", "gy"), split_axis=0, concat_axis=0, tiled=True)
    return returned


def local(
    point_feats,
    point_dest,
    point_voxel,
    kernel_map,
    border_list,
    conv_one,
    conv_two,
    gain_one,
    gain_two,
    decoder_in,
    decoder_bias,
    decoder_out,
    target,
):
    devices = lax.axis_size("gx") * lax.axis_size("gy")
    voxels = kernel_map.shape[1]
    points, channels = point_feats.shape
    capacity = 2 * points // devices
    destination = point_dest[:, 0]
    position = slot_positions(destination, devices, capacity)
    slot_hot = (
        jnp.arange(devices * capacity, dtype=jnp.int32)[:, None] == position[None, :]
    ).astype(jnp.bfloat16)
    id_high = (point_voxel // 32 + 1).astype(jnp.bfloat16)
    id_low = (point_voxel % 32).astype(jnp.bfloat16)
    payload = jnp.concatenate(
        [
            point_feats,
            jnp.ones((points, 1), jnp.bfloat16),
            id_high[:, None],
            id_low[:, None],
        ],
        axis=1,
    )
    send = jnp.einsum(
        "sp,pc->sc", slot_hot, payload, preferred_element_type=jnp.float32
    ).astype(jnp.bfloat16)
    got = send_points(send.reshape(devices, capacity, channels + 3)).reshape(-1, channels + 3)
    flat_ids = ((got[:, channels + 1].astype(jnp.float32) - 1.0) * 32.0 + got[:, channels + 2].astype(jnp.float32)).astype(jnp.int32)
    voxel_rows = jnp.arange(voxels, dtype=jnp.int32)
    slot_match = (flat_ids[:, None] == voxel_rows[None, :]).astype(jnp.bfloat16)
    pooled = jnp.einsum(
        "sv,sc->vc", slot_match, got[:, : channels + 1], preferred_element_type=jnp.float32
    )
    pooled_sum = pooled[:, :channels]
    counts = pooled[:, channels]
    inverse = 1.0 / jnp.maximum(counts, 1.0)
    x_zero = (pooled_sum * inverse[:, None]).astype(jnp.bfloat16)
    border_hot, halo_target = halo_layout(kernel_map, border_list)
    hidden_one, gathered_one, halo_one = conv_forward(
        x_zero, kernel_map, border_list, border_hot, halo_target, conv_one
    )
    act_one = activate(hidden_one, gain_one).astype(jnp.bfloat16)
    hidden_two, gathered_two, halo_two = conv_forward(
        act_one, kernel_map, border_list, border_hot, halo_target, conv_two
    )
    block_out = (x_zero.astype(jnp.float32) + activate(hidden_two, gain_two)).astype(jnp.bfloat16)
    pre_dec = jnp.dot(block_out, decoder_in, preferred_element_type=jnp.float32) + decoder_bias
    dec_hidden = jax.nn.silu(pre_dec)
    sdf_values = jnp.sum(dec_hidden * decoder_out, axis=-1)
    whole_count = voxels * devices
    error_sdf = sdf_values - target
    loss_part = jnp.sum(error_sdf * error_sdf) / (2.0 * whole_count)
    grad_sdf = error_sdf / whole_count
    grad_out_part = jnp.sum(dec_hidden * grad_sdf[:, None], axis=0)
    _, pull_silu = jax.vjp(jax.nn.silu, pre_dec)
    grad_pre = pull_silu(grad_sdf[:, None] * decoder_out)[0]
    grad_bias_part = jnp.sum(grad_pre, axis=0)
    grad_pre_low = grad_pre.astype(jnp.bfloat16)
    grad_in_part = lax.dot_general(
        block_out, grad_pre_low, (((0,), (0,)), ((), ())), preferred_element_type=jnp.float32
    )
    grad_block = lax.dot_general(
        grad_pre_low, decoder_in, (((1,), (1,)), ((), ())), preferred_element_type=jnp.float32
    )
    _, pull_two = jax.vjp(lambda hidden: activate(hidden, gain_two), hidden_two)
    grad_hidden_two = pull_two(grad_block)[0].astype(jnp.bfloat16)
    grad_act_one, weight_grad_two = backward_conv(
        gathered_two, halo_two, kernel_map, conv_two, grad_hidden_two, border_hot, halo_target, border_list
    )
    _, pull_one = jax.vjp(lambda hidden: activate(hidden, gain_one), hidden_one)
    grad_hidden_one = pull_one(grad_act_one)[0].astype(jnp.bfloat16)
    input_part, weight_grad_one = backward_conv(
        gathered_one, halo_one, kernel_map, conv_one, grad_hidden_one, border_hot, halo_target, border_list
    )
    grad_x_zero = grad_block + input_part
    scaled = (grad_x_zero * inverse[:, None]).astype(jnp.bfloat16)
    slot_values = jnp.einsum(
        "sv,vc->sc", slot_match, scaled, preferred_element_type=jnp.float32
    ).astype(jnp.bfloat16)
    returned = return_grads(slot_values.reshape(devices, capacity, channels)).reshape(-1, channels)
    grad_points = jnp.einsum(
        "sp,sc->pc", slot_hot, returned, preferred_element_type=jnp.float32
    ).astype(jnp.bfloat16)
    parts = (weight_grad_one, weight_grad_two, grad_in_part, grad_bias_part, grad_out_part, loss_part)
    summed = tree_psum(parts)
    (
        grad_conv_one,
        grad_conv_two,
        grad_decoder_in,
        grad_decoder_bias,
        grad_decoder_out,
        loss_value,
    ) = summed
    return (
        sdf_values,
        loss_value,
        grad_conv_one,
        grad_conv_two,
        grad_decoder_in,
        grad_decoder_bias,
        grad_decoder_out,
        grad_points,
    )


def solution(mesh):
    in_specs = (
        P(("gx", "gy"), None),
        P(("gx", "gy"), None),
        P(("gx", "gy")),
        P(None, ("gx", "gy")),
        P("gx", "gy", None),
        P(),
        P(),
        P(),
        P(),
        P(),
        P(),
        P(),
        P(("gx", "gy")),
    )
    out_specs = (P(("gx", "gy")), P(), P(), P(), P(), P(), P(), P(("gx", "gy"), None))
    return jax.shard_map(local, mesh=mesh, in_specs=in_specs, out_specs=out_specs, check_vma=False)
```

```python
import math

import jax
import numpy as np
import jax.numpy as jnp
from jax import lax
from jax.experimental import pallas as pl
from jax.experimental.pallas import tpu as pltpu
from jax.sharding import PartitionSpec as P

EPS = 1e-05


def with_halo(array, sides, width):
    for axis, dim in sides:
        peers, length = (lax.axis_size(axis), array.shape[dim])
        up = [(i, (i + 1) % peers) for i in range(peers - 1)]
        down = [(j, i) for i, j in up]
        last = lax.slice_in_dim(array, length - width, length, axis=dim)
        leading = lax.slice_in_dim(array, 0, width, axis=dim)
        before = lax.ppermute(last, axis, up)
        after = lax.ppermute(leading, axis, down)
        array = jnp.concatenate([before, array, after], axis=dim)
    return array


def activate(hidden, gain_vec):
    inverse_rms = lax.rsqrt(jnp.mean(hidden * hidden, axis=-1, keepdims=True) + EPS)
    return jax.nn.silu(hidden * inverse_rms * gain_vec)


def build_table(features, border_list):
    channels = features.shape[1]
    edge_rows = features[border_list]
    neighbour_rows = with_halo(edge_rows, (("gx", 0), ("gy", 1)), 1)
    zero_row = jnp.zeros((1, channels), features.dtype)
    return jnp.concatenate([features, neighbour_rows.reshape(-1, channels), zero_row], axis=0)


def gather_local(rows, kernel_map):
    voxels = rows.shape[0]
    local_rows = jnp.arange(voxels, dtype=jnp.int32)
    selector = (kernel_map[:, :, None] == local_rows[None, None, :]).astype(rows.dtype)
    picked = jnp.einsum("kvu,uc->kvc", selector, rows, preferred_element_type=jnp.float32)
    return picked.astype(rows.dtype)


def pair_gather_kernel(map_ref, rows_ref, rows_t_ref, low_ref, high_ref):
    voxels = rows_ref.shape[0]
    pairs = low_ref.shape[0]
    rows = rows_ref[...]
    rows_t = rows_t_ref[...]
    local_rows = lax.broadcasted_iota(jnp.int32, (voxels, voxels), 1)
    for k in range(pairs):
        selector = (map_ref[:, k:k + 1] == local_rows).astype(rows.dtype)
        low_ref[k] = jnp.dot(selector, rows, preferred_element_type=jnp.float32).astype(low_ref.dtype)
        high_ref[k] = jnp.dot(rows_t, selector, preferred_element_type=jnp.float32).astype(high_ref.dtype)


def gather_pairs(rows, kernel_map):
    voxels, channels = rows.shape
    pairs = kernel_map.shape[0] // 2
    return pl.pallas_call(
        pair_gather_kernel,
        out_shape=(
            jax.ShapeDtypeStruct((pairs, voxels, channels), rows.dtype),
            jax.ShapeDtypeStruct((pairs, channels, voxels), rows.dtype),
        ),
        in_specs=[pl.BlockSpec(memory_space=pltpu.VMEM)] * 3,
        out_specs=(pl.BlockSpec(memory_space=pltpu.VMEM), pl.BlockSpec(memory_space=pltpu.VMEM)),
        compiler_params=pltpu.CompilerParams(vmem_limit_bytes=48 * 1024 * 1024),
        cost_estimate=pl.CostEstimate(
            flops=4 * pairs * voxels * voxels * channels,
            bytes_accessed=2 * (2 * pairs + 2) * voxels * channels + 4 * pairs * voxels,
            transcendentals=0,
        ),
    )(jnp.transpose(kernel_map[:pairs]), rows, jnp.transpose(rows))


def pair_conv(low, rows, high, weight):
    pairs = low.shape[0]
    return (
        jnp.einsum("kvc,kcd->vd", low, weight[:pairs], preferred_element_type=jnp.float32)
        + jnp.dot(rows, weight[pairs], preferred_element_type=jnp.float32)
        + jnp.einsum("kcv,kcd->vd", high, weight[pairs + 1:][::-1], preferred_element_type=jnp.float32)
    )


def halo_layout(kernel_map, border_list):
    voxels = kernel_map.shape[1]
    boundary = border_list.shape[2]
    border_flat = border_list.reshape(-1)
    border_hot = (jnp.arange(voxels, dtype=jnp.int32)[:, None] == border_flat[None, :])
    named = jnp.einsum(
        "kv,vb->kb",
        kernel_map.astype(jnp.float32),
        border_hot.astype(jnp.float32),
        precision=lax.Precision.HIGHEST,
    )
    expected = np.zeros((27, 2, 2, boundary), np.int32)
    for k in range(27):
        step_x, step_y = k // 9 - 1, k // 3 % 3 - 1
        for i in range(2):
            for j in range(2):
                cell = (i + 1 + step_x) * 4 + (j + 1 + step_y)
                expected[k, i, j] = cell * boundary + np.arange(boundary)
    expected = jnp.asarray(expected.reshape(27, -1))
    flag = named == (expected + voxels).astype(jnp.float32)
    target = jnp.where(flag, expected, -1)
    return border_hot, target


def halo_hot(target, halo_count):
    return target[:, :, None] == jnp.arange(halo_count, dtype=jnp.int32)[None, None, :]


def halo_pick(halo, target):
    channels = halo.shape[-1]
    flat = halo.reshape(-1, channels)
    picked = jnp.einsum(
        "kbr,rc->kbc",
        halo_hot(target, flat.shape[0]).astype(flat.dtype),
        flat,
        preferred_element_type=jnp.float32,
    )
    return picked.astype(halo.dtype)


def edge_halo(features, border_hot, border_list):
    channels = features.shape[1]
    edge_rows = jnp.einsum(
        "vb,vc->bc", border_hot.astype(features.dtype), features, preferred_element_type=jnp.float32
    ).astype(features.dtype)
    edge_rows = edge_rows.reshape(border_list.shape + (channels,))
    return with_halo(edge_rows, (("gx", 0), ("gy", 1)), 1)


def conv_forward(features, kernel_map, border_list, border_hot, target, weight):
    low, high = gather_pairs(features, kernel_map)
    halo_rows = halo_pick(edge_halo(features, border_hot, border_list), target)
    local_out = pair_conv(low, features, high, weight)
    border_out = jnp.einsum("kbc,kcd->bd", halo_rows, weight, preferred_element_type=jnp.float32)
    placed = jnp.einsum(
        "vb,bd->vd", border_hot.astype(jnp.float32), border_out, precision=lax.Precision.HIGHEST
    )
    return local_out + placed, (low, features, high), halo_rows


def backward_conv(gathered, halo_rows, kernel_map, weight, grad_rows, border_hot, target, border_list):
    grad_border = jnp.einsum(
        "vb,vd->bd", border_hot.astype(grad_rows.dtype), grad_rows, preferred_element_type=jnp.float32
    ).astype(grad_rows.dtype)
    low, centre, high = gathered
    pairs = low.shape[0]
    weight_grad = jnp.concatenate(
        [
            jnp.einsum("kvc,vd->kcd", low, grad_rows, preferred_element_type=jnp.float32),
            jnp.einsum("vc,vd->cd", centre, grad_rows, preferred_element_type=jnp.float32)[None],
            jnp.einsum("kcv,vd->kcd", high, grad_rows, preferred_element_type=jnp.float32)[::-1],
        ],
        axis=0,
    ) + jnp.einsum("kbc,bd->kcd", halo_rows, grad_border, preferred_element_type=jnp.float32)
    flipped_weight = jnp.swapaxes(weight[::-1], 1, 2)
    grad_low, grad_high = gather_pairs(grad_rows, kernel_map)
    local_part = pair_conv(grad_low, grad_rows, grad_high, flipped_weight)
    channels = grad_rows.shape[1]
    boundary = border_list.shape[2]
    spread = jnp.einsum(
        "kbr,bd->rkd",
        halo_hot(target, 16 * boundary).astype(grad_border.dtype),
        grad_border,
        preferred_element_type=jnp.float32,
    ).astype(grad_border.dtype)
    halo_grad = jnp.einsum(
        "rkd,kcd->rc", spread, weight, preferred_element_type=jnp.float32
    ).reshape(4, 4, boundary, channels)
    rows_end = jnp.stack([halo_grad[0], halo_grad[3]], axis=0)
    cols_end = jnp.stack([halo_grad[:, 0], halo_grad[:, 3]], axis=1)
    corner_end = jnp.stack([rows_end[:, 0], rows_end[:, 3]], axis=1)
    payload = jnp.stack([rows_end[:, 1:3], cols_end[1:3], corner_end], axis=2)
    received = with_halo(payload.astype(jnp.bfloat16), (("gx", 0), ("gy", 1)), 1).astype(
        payload.dtype
    )
    from_rows = jnp.stack([received[0, 1:3, 0], received[3, 1:3, 0]], axis=0)
    from_cols = jnp.stack([received[1:3, 0, 1], received[1:3, 3, 1]], axis=1)
    corner_low = jnp.stack([received[0, 0, 2], received[0, 3, 2]], axis=0)
    corner_high = jnp.stack([received[3, 0, 2], received[3, 3, 2]], axis=0)
    from_corner = jnp.stack([corner_low, corner_high], axis=0)
    folded = halo_grad[1:3, 1:3] + from_rows + from_cols + from_corner
    result = local_part + jnp.einsum(
        "vb,bd->vd",
        border_hot.astype(jnp.float32),
        folded.reshape(-1, channels),
        precision=lax.Precision.HIGHEST,
    )
    return (result, weight_grad)


HALVING_STEPS = (("gy", 1), ("gy", 2), ("gx", 1))
DOUBLING_STEPS = (("gx", 4), ("gy", 4), ("gx", 2), ("gx", 8))


def tree_psum(parts):
    flat = jnp.concatenate([jnp.ravel(p).astype(jnp.float32) for p in parts])
    lanes = 128
    rows = -(-flat.shape[0] // lanes)
    rows = -(-rows // (8 * 2 ** len(HALVING_STEPS))) * (8 * 2 ** len(HALVING_STEPS))
    x = jnp.pad(flat, (0, rows * lanes - flat.shape[0])).reshape(rows, lanes)
    bits = []
    for axis, mask in HALVING_STEPS:
        peers = lax.axis_size(axis)
        bit = (lax.axis_index(axis) // mask) % 2
        bits.append(bit)
        half = x.shape[0] // 2
        low, high = x[:half], x[half:]
        send = jnp.where(bit == 1, low, high)
        keep = jnp.where(bit == 1, high, low)
        x = keep + lax.ppermute(send, axis, [(i, i ^ mask) for i in range(peers)])
    for axis, mask in DOUBLING_STEPS:
        peers = lax.axis_size(axis)
        bit = (lax.axis_index(axis) // mask) % 2
        other = lax.ppermute(x, axis, [(i, i ^ mask) for i in range(peers)])
        x = jnp.where(bit == 1, other + x, x + other)
    for (axis, mask), bit in reversed(list(zip(HALVING_STEPS, bits))):
        peers = lax.axis_size(axis)
        other = lax.ppermute(x, axis, [(i, i ^ mask) for i in range(peers)])
        x = jnp.where(bit == 1, jnp.concatenate([other, x]), jnp.concatenate([x, other]))
    flat = x.reshape(-1)
    out, start = [], 0
    for p in parts:
        size = math.prod(p.shape)
        out.append(flat[start:start + size].reshape(p.shape))
        start += size
    return tuple(out)


def slot_positions(destination, devices, capacity):
    points = destination.shape[0]
    block = math.gcd(points, 128)
    blocks = points // block
    dest_hot = destination[:, None] == jnp.arange(devices, dtype=jnp.int32)[None, :]
    grouped = dest_hot.astype(jnp.bfloat16).reshape(blocks, block, devices)
    lower = (
        jnp.arange(block, dtype=jnp.int32)[:, None] > jnp.arange(block, dtype=jnp.int32)[None, :]
    ).astype(jnp.bfloat16)
    within = jnp.einsum("ij,bjd->bid", lower, grouped, preferred_element_type=jnp.float32)
    totals = jnp.sum(grouped.astype(jnp.float32), axis=1)
    lower_blocks = (
        jnp.arange(blocks, dtype=jnp.int32)[:, None] > jnp.arange(blocks, dtype=jnp.int32)[None, :]
    ).astype(jnp.float32)
    offsets = jnp.einsum("ab,bd->ad", lower_blocks, totals, precision=lax.Precision.HIGHEST)
    earlier = (within + offsets[:, None, :]).reshape(points, devices)
    rank = jnp.sum(jnp.where(dest_hot, earlier, 0.0), axis=1).astype(jnp.int32)
    return destination * capacity + rank


def send_points(send_rows):
    return lax.all_to_all(send_rows, ("gx", "gy"), split_axis=0, concat_axis=0, tiled=True)


def return_grads(slot_grads):
    returned = lax.all_to_all(slot_grads, ("gx", "gy"), split_axis=0, concat_axis=0, tiled=True)
    return returned


def local(
    point_feats,
    point_dest,
    point_voxel,
    kernel_map,
    border_list,
    conv_one,
    conv_two,
    gain_one,
    gain_two,
    decoder_in,
    decoder_bias,
    decoder_out,
    target,
):
    devices = lax.axis_size("gx") * lax.axis_size("gy")
    voxels = kernel_map.shape[1]
    points, channels = point_feats.shape
    capacity = 2 * points // devices
    destination = point_dest[:, 0]
    position = slot_positions(destination, devices, capacity)
    slot_hot = (
        jnp.arange(devices * capacity, dtype=jnp.int32)[:, None] == position[None, :]
    ).astype(jnp.bfloat16)
    id_high = (point_voxel // 32 + 1).astype(jnp.bfloat16)
    id_low = (point_voxel % 32).astype(jnp.bfloat16)
    payload = jnp.concatenate(
        [
            point_feats,
            jnp.ones((points, 1), jnp.bfloat16),
            id_high[:, None],
            id_low[:, None],
        ],
        axis=1,
    )
    send = jnp.einsum(
        "sp,pc->sc", slot_hot, payload, preferred_element_type=jnp.float32
    ).astype(jnp.bfloat16)
    got = send_points(send.reshape(devices, capacity, channels + 3)).reshape(-1, channels + 3)
    flat_ids = ((got[:, channels + 1].astype(jnp.float32) - 1.0) * 32.0 + got[:, channels + 2].astype(jnp.float32)).astype(jnp.int32)
    voxel_rows = jnp.arange(voxels, dtype=jnp.int32)
    slot_match = (flat_ids[:, None] == voxel_rows[None, :]).astype(jnp.bfloat16)
    pooled = jnp.einsum(
        "sv,sc->vc", slot_match, got[:, : channels + 1], preferred_element_type=jnp.float32
    )
    pooled_sum = pooled[:, :channels]
    counts = pooled[:, channels]
    inverse = 1.0 / jnp.maximum(counts, 1.0)
    x_zero = (pooled_sum * inverse[:, None]).astype(jnp.bfloat16)
    border_hot, halo_target = halo_layout(kernel_map, border_list)
    hidden_one, gathered_one, halo_one = conv_forward(
        x_zero, kernel_map, border_list, border_hot, halo_target, conv_one
    )
    act_one = activate(hidden_one, gain_one).astype(jnp.bfloat16)
    hidden_two, gathered_two, halo_two = conv_forward(
        act_one, kernel_map, border_list, border_hot, halo_target, conv_two
    )
    block_out = (x_zero.astype(jnp.float32) + activate(hidden_two, gain_two)).astype(jnp.bfloat16)
    pre_dec = jnp.dot(block_out, decoder_in, preferred_element_type=jnp.float32) + decoder_bias
    dec_hidden = jax.nn.silu(pre_dec)
    sdf_values = jnp.sum(dec_hidden * decoder_out, axis=-1)
    whole_count = voxels * devices
    error_sdf = sdf_values - target
    loss_part = jnp.sum(error_sdf * error_sdf) / (2.0 * whole_count)
    grad_sdf = error_sdf / whole_count
    grad_out_part = jnp.sum(dec_hidden * grad_sdf[:, None], axis=0)
    _, pull_silu = jax.vjp(jax.nn.silu, pre_dec)
    grad_pre = pull_silu(grad_sdf[:, None] * decoder_out)[0]
    grad_bias_part = jnp.sum(grad_pre, axis=0)
    grad_pre_low = grad_pre.astype(jnp.bfloat16)
    grad_in_part = lax.dot_general(
        block_out, grad_pre_low, (((0,), (0,)), ((), ())), preferred_element_type=jnp.float32
    )
    grad_block = lax.dot_general(
        grad_pre_low, decoder_in, (((1,), (1,)), ((), ())), preferred_element_type=jnp.float32
    )
    _, pull_two = jax.vjp(lambda hidden: activate(hidden, gain_two), hidden_two)
    grad_hidden_two = pull_two(grad_block)[0].astype(jnp.bfloat16)
    grad_act_one, weight_grad_two = backward_conv(
        gathered_two, halo_two, kernel_map, conv_two, grad_hidden_two, border_hot, halo_target, border_list
    )
    _, pull_one = jax.vjp(lambda hidden: activate(hidden, gain_one), hidden_one)
    grad_hidden_one = pull_one(grad_act_one)[0].astype(jnp.bfloat16)
    input_part, weight_grad_one = backward_conv(
        gathered_one, halo_one, kernel_map, conv_one, grad_hidden_one, border_hot, halo_target, border_list
    )
    grad_x_zero = grad_block + input_part
    scaled = (grad_x_zero * inverse[:, None]).astype(jnp.bfloat16)
    slot_values = jnp.einsum(
        "sv,vc->sc", slot_match, scaled, preferred_element_type=jnp.float32
    ).astype(jnp.bfloat16)
    returned = return_grads(slot_values.reshape(devices, capacity, channels)).reshape(-1, channels)
    grad_points = jnp.einsum(
        "sp,sc->pc", slot_hot, returned, preferred_element_type=jnp.float32
    ).astype(jnp.bfloat16)
    parts = (weight_grad_one, weight_grad_two, grad_in_part, grad_bias_part, grad_out_part, loss_part)
    summed = tree_psum(parts)
    (
        grad_conv_one,
        grad_conv_two,
        grad_decoder_in,
        grad_decoder_bias,
        grad_decoder_out,
        loss_value,
    ) = summed
    return (
        sdf_values,
        loss_value,
        grad_conv_one,
        grad_conv_two,
        grad_decoder_in,
        grad_decoder_bias,
        grad_decoder_out,
        grad_points,
    )


def solution(mesh):
    in_specs = (
        P(("gx", "gy"), None),
        P(("gx", "gy"), None),
        P(("gx", "gy")),
        P(None, ("gx", "gy")),
        P("gx", "gy", None),
        P(),
        P(),
        P(),
        P(),
        P(),
        P(),
        P(),
        P(("gx", "gy")),
    )
    out_specs = (P(("gx", "gy")), P(), P(), P(), P(), P(), P(), P(("gx", "gy"), None))
    return jax.shard_map(local, mesh=mesh, in_specs=in_specs, out_specs=out_specs, check_vma=False)
```

```python
import math

import jax
import numpy as np
import jax.numpy as jnp
from jax import lax
from jax.experimental import pallas as pl
from jax.experimental.pallas import tpu as pltpu
from jax.sharding import PartitionSpec as P

EPS = 1e-05


def with_halo(array, sides, width):
    for axis, dim in sides:
        peers, length = (lax.axis_size(axis), array.shape[dim])
        up = [(i, (i + 1) % peers) for i in range(peers - 1)]
        down = [(j, i) for i, j in up]
        last = lax.slice_in_dim(array, length - width, length, axis=dim)
        leading = lax.slice_in_dim(array, 0, width, axis=dim)
        before = lax.ppermute(last, axis, up)
        after = lax.ppermute(leading, axis, down)
        array = jnp.concatenate([before, array, after], axis=dim)
    return array


def activate(hidden, gain_vec):
    inverse_rms = lax.rsqrt(jnp.mean(hidden * hidden, axis=-1, keepdims=True) + EPS)
    return jax.nn.silu(hidden * inverse_rms * gain_vec)


def build_table(features, border_list):
    channels = features.shape[1]
    edge_rows = features[border_list]
    neighbour_rows = with_halo(edge_rows, (("gx", 0), ("gy", 1)), 1)
    zero_row = jnp.zeros((1, channels), features.dtype)
    return jnp.concatenate([features, neighbour_rows.reshape(-1, channels), zero_row], axis=0)


def gather_local(rows, kernel_map):
    voxels = rows.shape[0]
    local_rows = jnp.arange(voxels, dtype=jnp.int32)
    selector = (kernel_map[:, :, None] == local_rows[None, None, :]).astype(rows.dtype)
    picked = jnp.einsum("kvu,uc->kvc", selector, rows, preferred_element_type=jnp.float32)
    return picked.astype(rows.dtype)


def pair_gather_kernel(map_ref, rows_ref, rows_t_ref, low_ref, high_ref):
    voxels = rows_ref.shape[0]
    pairs = low_ref.shape[0]
    rows = rows_ref[...]
    rows_t = rows_t_ref[...]
    local_rows = lax.broadcasted_iota(jnp.int32, (voxels, voxels), 1)
    for k in range(pairs):
        selector = (map_ref[:, k:k + 1] == local_rows).astype(rows.dtype)
        low_ref[k] = jnp.dot(selector, rows, preferred_element_type=jnp.float32).astype(low_ref.dtype)
        high_ref[pairs - 1 - k] = jnp.dot(rows_t, selector, preferred_element_type=jnp.float32).astype(high_ref.dtype)


def gather_pairs(rows, map_t):
    voxels, channels = rows.shape
    pairs = map_t.shape[1]
    return pl.pallas_call(
        pair_gather_kernel,
        out_shape=(
            jax.ShapeDtypeStruct((pairs, voxels, channels), rows.dtype),
            jax.ShapeDtypeStruct((pairs, channels, voxels), rows.dtype),
        ),
        in_specs=[pl.BlockSpec(memory_space=pltpu.VMEM)] * 3,
        out_specs=(pl.BlockSpec(memory_space=pltpu.VMEM), pl.BlockSpec(memory_space=pltpu.VMEM)),
        compiler_params=pltpu.CompilerParams(vmem_limit_bytes=48 * 1024 * 1024),
        cost_estimate=pl.CostEstimate(
            flops=4 * pairs * voxels * voxels * channels,
            bytes_accessed=2 * (2 * pairs + 2) * voxels * channels + 4 * pairs * voxels,
            transcendentals=0,
        ),
    )(map_t, rows, jnp.transpose(rows))


def pair_conv(low, rows, high, weight):
    pairs = low.shape[0]
    return (
        jnp.einsum("kvc,kcd->vd", low, weight[:pairs], preferred_element_type=jnp.float32)
        + jnp.dot(rows, weight[pairs], preferred_element_type=jnp.float32)
        + jnp.einsum("kcv,kcd->vd", high, weight[pairs + 1:], preferred_element_type=jnp.float32)
    )


def halo_layout(kernel_map, border_list):
    voxels = kernel_map.shape[1]
    boundary = border_list.shape[2]
    border_flat = border_list.reshape(-1)
    border_hot = (jnp.arange(voxels, dtype=jnp.int32)[:, None] == border_flat[None, :])
    named = jnp.einsum(
        "kv,vb->kb",
        kernel_map.astype(jnp.float32),
        border_hot.astype(jnp.float32),
        precision=lax.Precision.HIGHEST,
    )
    expected = np.zeros((27, 2, 2, boundary), np.int32)
    for k in range(27):
        step_x, step_y = k // 9 - 1, k // 3 % 3 - 1
        for i in range(2):
            for j in range(2):
                cell = (i + 1 + step_x) * 4 + (j + 1 + step_y)
                expected[k, i, j] = cell * boundary + np.arange(boundary)
    expected = jnp.asarray(expected.reshape(27, -1))
    flag = named == (expected + voxels).astype(jnp.float32)
    target = jnp.where(flag, expected, -1)
    return border_hot, target


def halo_hot(target, halo_count):
    return target[:, :, None] == jnp.arange(halo_count, dtype=jnp.int32)[None, None, :]


def halo_pick(halo, target):
    channels = halo.shape[-1]
    flat = halo.reshape(-1, channels)
    picked = jnp.einsum(
        "kbr,rc->kbc",
        halo_hot(target, flat.shape[0]).astype(flat.dtype),
        flat,
        preferred_element_type=jnp.float32,
    )
    return picked.astype(halo.dtype)


def edge_halo(features, border_hot, border_list):
    channels = features.shape[1]
    edge_rows = jnp.einsum(
        "vb,vc->bc", border_hot.astype(features.dtype), features, preferred_element_type=jnp.float32
    ).astype(features.dtype)
    edge_rows = edge_rows.reshape(border_list.shape + (channels,))
    return with_halo(edge_rows, (("gx", 0), ("gy", 1)), 1)


def conv_forward(features, kernel_map, border_list, border_hot, target, weight):
    low, high = gather_pairs(features, jnp.transpose(kernel_map[: kernel_map.shape[0] // 2]))
    halo_rows = halo_pick(edge_halo(features, border_hot, border_list), target)
    local_out = pair_conv(low, features, high, weight)
    border_out = jnp.einsum("kbc,kcd->bd", halo_rows, weight, preferred_element_type=jnp.float32)
    placed = jnp.einsum(
        "vb,bd->vd", border_hot.astype(jnp.float32), border_out, precision=lax.Precision.HIGHEST
    )
    return local_out + placed, (low, features, high), halo_rows


def backward_conv(gathered, halo_rows, kernel_map, weight, grad_rows, border_hot, target, border_list):
    grad_border = jnp.einsum(
        "vb,vd->bd", border_hot.astype(grad_rows.dtype), grad_rows, preferred_element_type=jnp.float32
    ).astype(grad_rows.dtype)
    low, centre, high = gathered
    pairs = low.shape[0]
    weight_grad = jnp.concatenate(
        [
            jnp.einsum("kvc,vd->kcd", low, grad_rows, preferred_element_type=jnp.float32),
            jnp.einsum("vc,vd->cd", centre, grad_rows, preferred_element_type=jnp.float32)[None],
            jnp.einsum("kcv,vd->kcd", high, grad_rows, preferred_element_type=jnp.float32),
        ],
        axis=0,
    ) + jnp.einsum("kbc,bd->kcd", halo_rows, grad_border, preferred_element_type=jnp.float32)
    flipped_weight = jnp.swapaxes(weight[::-1], 1, 2)
    grad_low, grad_high = gather_pairs(grad_rows, jnp.transpose(kernel_map[: kernel_map.shape[0] // 2]))
    local_part = pair_conv(grad_low, grad_rows, grad_high, flipped_weight)
    channels = grad_rows.shape[1]
    boundary = border_list.shape[2]
    spread = jnp.einsum(
        "kbr,bd->rkd",
        halo_hot(target, 16 * boundary).astype(grad_border.dtype),
        grad_border,
        preferred_element_type=jnp.float32,
    ).astype(grad_border.dtype)
    halo_grad = jnp.einsum(
        "rkd,kcd->rc", spread, weight, preferred_element_type=jnp.float32
    ).reshape(4, 4, boundary, channels)
    rows_end = jnp.stack([halo_grad[0], halo_grad[3]], axis=0)
    cols_end = jnp.stack([halo_grad[:, 0], halo_grad[:, 3]], axis=1)
    corner_end = jnp.stack([rows_end[:, 0], rows_end[:, 3]], axis=1)
    payload = jnp.stack([rows_end[:, 1:3], cols_end[1:3], corner_end], axis=2)
    received = with_halo(payload.astype(jnp.bfloat16), (("gx", 0), ("gy", 1)), 1).astype(
        payload.dtype
    )
    from_rows = jnp.stack([received[0, 1:3, 0], received[3, 1:3, 0]], axis=0)
    from_cols = jnp.stack([received[1:3, 0, 1], received[1:3, 3, 1]], axis=1)
    corner_low = jnp.stack([received[0, 0, 2], received[0, 3, 2]], axis=0)
    corner_high = jnp.stack([received[3, 0, 2], received[3, 3, 2]], axis=0)
    from_corner = jnp.stack([corner_low, corner_high], axis=0)
    folded = halo_grad[1:3, 1:3] + from_rows + from_cols + from_corner
    result = local_part + jnp.einsum(
        "vb,bd->vd",
        border_hot.astype(jnp.float32),
        folded.reshape(-1, channels),
        precision=lax.Precision.HIGHEST,
    )
    return (result, weight_grad)


HALVING_STEPS = (("gy", 1), ("gy", 2), ("gx", 1))
DOUBLING_STEPS = (("gx", 4), ("gy", 4), ("gx", 2), ("gx", 8))


def tree_psum(parts):
    flat = jnp.concatenate([jnp.ravel(p).astype(jnp.float32) for p in parts])
    lanes = 128
    rows = -(-flat.shape[0] // lanes)
    rows = -(-rows // (8 * 2 ** len(HALVING_STEPS))) * (8 * 2 ** len(HALVING_STEPS))
    x = jnp.pad(flat, (0, rows * lanes - flat.shape[0])).reshape(rows, lanes)
    bits = []
    for axis, mask in HALVING_STEPS:
        peers = lax.axis_size(axis)
        bit = (lax.axis_index(axis) // mask) % 2
        bits.append(bit)
        half = x.shape[0] // 2
        low, high = x[:half], x[half:]
        send = jnp.where(bit == 1, low, high)
        keep = jnp.where(bit == 1, high, low)
        x = keep + lax.ppermute(send, axis, [(i, i ^ mask) for i in range(peers)])
    for axis, mask in DOUBLING_STEPS:
        peers = lax.axis_size(axis)
        bit = (lax.axis_index(axis) // mask) % 2
        other = lax.ppermute(x, axis, [(i, i ^ mask) for i in range(peers)])
        x = jnp.where(bit == 1, other + x, x + other)
    for (axis, mask), bit in reversed(list(zip(HALVING_STEPS, bits))):
        peers = lax.axis_size(axis)
        other = lax.ppermute(x, axis, [(i, i ^ mask) for i in range(peers)])
        x = jnp.where(bit == 1, jnp.concatenate([other, x]), jnp.concatenate([x, other]))
    flat = x.reshape(-1)
    out, start = [], 0
    for p in parts:
        size = math.prod(p.shape)
        out.append(flat[start:start + size].reshape(p.shape))
        start += size
    return tuple(out)


def slot_positions(destination, devices, capacity):
    points = destination.shape[0]
    block = math.gcd(points, 128)
    blocks = points // block
    dest_hot = destination[:, None] == jnp.arange(devices, dtype=jnp.int32)[None, :]
    grouped = dest_hot.astype(jnp.bfloat16).reshape(blocks, block, devices)
    lower = (
        jnp.arange(block, dtype=jnp.int32)[:, None] > jnp.arange(block, dtype=jnp.int32)[None, :]
    ).astype(jnp.bfloat16)
    within = jnp.einsum("ij,bjd->bid", lower, grouped, preferred_element_type=jnp.float32)
    totals = jnp.sum(grouped.astype(jnp.float32), axis=1)
    lower_blocks = (
        jnp.arange(blocks, dtype=jnp.int32)[:, None] > jnp.arange(blocks, dtype=jnp.int32)[None, :]
    ).astype(jnp.float32)
    offsets = jnp.einsum("ab,bd->ad", lower_blocks, totals, precision=lax.Precision.HIGHEST)
    earlier = (within + offsets[:, None, :]).reshape(points, devices)
    rank = jnp.sum(jnp.where(dest_hot, earlier, 0.0), axis=1).astype(jnp.int32)
    return destination * capacity + rank


def send_points(send_rows):
    return lax.all_to_all(send_rows, ("gx", "gy"), split_axis=0, concat_axis=0, tiled=True)


def return_grads(slot_grads):
    returned = lax.all_to_all(slot_grads, ("gx", "gy"), split_axis=0, concat_axis=0, tiled=True)
    return returned


def local(
    point_feats,
    point_dest,
    point_voxel,
    kernel_map,
    border_list,
    conv_one,
    conv_two,
    gain_one,
    gain_two,
    decoder_in,
    decoder_bias,
    decoder_out,
    target,
):
    devices = lax.axis_size("gx") * lax.axis_size("gy")
    voxels = kernel_map.shape[1]
    points, channels = point_feats.shape
    capacity = 2 * points // devices
    destination = point_dest[:, 0]
    position = slot_positions(destination, devices, capacity)
    slot_hot = (
        jnp.arange(devices * capacity, dtype=jnp.int32)[:, None] == position[None, :]
    ).astype(jnp.bfloat16)
    id_high = (point_voxel // 32 + 1).astype(jnp.bfloat16)
    id_low = (point_voxel % 32).astype(jnp.bfloat16)
    payload = jnp.concatenate(
        [
            point_feats,
            jnp.ones((points, 1), jnp.bfloat16),
            id_high[:, None],
            id_low[:, None],
        ],
        axis=1,
    )
    send = jnp.einsum(
        "sp,pc->sc", slot_hot, payload, preferred_element_type=jnp.float32
    ).astype(jnp.bfloat16)
    got = send_points(send.reshape(devices, capacity, channels + 3)).reshape(-1, channels + 3)
    flat_ids = ((got[:, channels + 1].astype(jnp.float32) - 1.0) * 32.0 + got[:, channels + 2].astype(jnp.float32)).astype(jnp.int32)
    voxel_rows = jnp.arange(voxels, dtype=jnp.int32)
    slot_match = (flat_ids[:, None] == voxel_rows[None, :]).astype(jnp.bfloat16)
    pooled = jnp.einsum(
        "sv,sc->vc", slot_match, got[:, : channels + 1], preferred_element_type=jnp.float32
    )
    pooled_sum = pooled[:, :channels]
    counts = pooled[:, channels]
    inverse = 1.0 / jnp.maximum(counts, 1.0)
    x_zero = (pooled_sum * inverse[:, None]).astype(jnp.bfloat16)
    border_hot, halo_target = halo_layout(kernel_map, border_list)
    hidden_one, gathered_one, halo_one = conv_forward(
        x_zero, kernel_map, border_list, border_hot, halo_target, conv_one
    )
    act_one = activate(hidden_one, gain_one).astype(jnp.bfloat16)
    hidden_two, gathered_two, halo_two = conv_forward(
        act_one, kernel_map, border_list, border_hot, halo_target, conv_two
    )
    block_out = (x_zero.astype(jnp.float32) + activate(hidden_two, gain_two)).astype(jnp.bfloat16)
    pre_dec = jnp.dot(block_out, decoder_in, preferred_element_type=jnp.float32) + decoder_bias
    dec_hidden = jax.nn.silu(pre_dec)
    sdf_values = jnp.sum(dec_hidden * decoder_out, axis=-1)
    whole_count = voxels * devices
    error_sdf = sdf_values - target
    loss_part = jnp.sum(error_sdf * error_sdf) / (2.0 * whole_count)
    grad_sdf = error_sdf / whole_count
    grad_out_part = jnp.sum(dec_hidden * grad_sdf[:, None], axis=0)
    _, pull_silu = jax.vjp(jax.nn.silu, pre_dec)
    grad_pre = pull_silu(grad_sdf[:, None] * decoder_out)[0]
    grad_bias_part = jnp.sum(grad_pre, axis=0)
    grad_pre_low = grad_pre.astype(jnp.bfloat16)
    grad_in_part = lax.dot_general(
        block_out, grad_pre_low, (((0,), (0,)), ((), ())), preferred_element_type=jnp.float32
    )
    grad_block = lax.dot_general(
        grad_pre_low, decoder_in, (((1,), (1,)), ((), ())), preferred_element_type=jnp.float32
    )
    _, pull_two = jax.vjp(lambda hidden: activate(hidden, gain_two), hidden_two)
    grad_hidden_two = pull_two(grad_block)[0].astype(jnp.bfloat16)
    grad_act_one, weight_grad_two = backward_conv(
        gathered_two, halo_two, kernel_map, conv_two, grad_hidden_two, border_hot, halo_target, border_list
    )
    _, pull_one = jax.vjp(lambda hidden: activate(hidden, gain_one), hidden_one)
    grad_hidden_one = pull_one(grad_act_one)[0].astype(jnp.bfloat16)
    input_part, weight_grad_one = backward_conv(
        gathered_one, halo_one, kernel_map, conv_one, grad_hidden_one, border_hot, halo_target, border_list
    )
    grad_x_zero = grad_block + input_part
    scaled = (grad_x_zero * inverse[:, None]).astype(jnp.bfloat16)
    slot_values = jnp.einsum(
        "sv,vc->sc", slot_match, scaled, preferred_element_type=jnp.float32
    ).astype(jnp.bfloat16)
    returned = return_grads(slot_values.reshape(devices, capacity, channels)).reshape(-1, channels)
    grad_points = jnp.einsum(
        "sp,sc->pc", slot_hot, returned, preferred_element_type=jnp.float32
    ).astype(jnp.bfloat16)
    parts = (weight_grad_one, weight_grad_two, grad_in_part, grad_bias_part, grad_out_part, loss_part)
    summed = tree_psum(parts)
    (
        grad_conv_one,
        grad_conv_two,
        grad_decoder_in,
        grad_decoder_bias,
        grad_decoder_out,
        loss_value,
    ) = summed
    return (
        sdf_values,
        loss_value,
        grad_conv_one,
        grad_conv_two,
        grad_decoder_in,
        grad_decoder_bias,
        grad_decoder_out,
        grad_points,
    )


def solution(mesh):
    in_specs = (
        P(("gx", "gy"), None),
        P(("gx", "gy"), None),
        P(("gx", "gy")),
        P(None, ("gx", "gy")),
        P("gx", "gy", None),
        P(),
        P(),
        P(),
        P(),
        P(),
        P(),
        P(),
        P(("gx", "gy")),
    )
    out_specs = (P(("gx", "gy")), P(), P(), P(), P(), P(), P(), P(("gx", "gy"), None))
    return jax.shard_map(local, mesh=mesh, in_specs=in_specs, out_specs=out_specs, check_vma=False)
```

```python
import math

import jax
import numpy as np
import jax.numpy as jnp
from jax import lax
from jax.experimental import pallas as pl
from jax.experimental.pallas import tpu as pltpu
from jax.sharding import PartitionSpec as P

EPS = 1e-05


def with_halo(array, sides, width):
    for axis, dim in sides:
        peers, length = (lax.axis_size(axis), array.shape[dim])
        up = [(i, (i + 1) % peers) for i in range(peers - 1)]
        down = [(j, i) for i, j in up]
        last = lax.slice_in_dim(array, length - width, length, axis=dim)
        leading = lax.slice_in_dim(array, 0, width, axis=dim)
        before = lax.ppermute(last, axis, up)
        after = lax.ppermute(leading, axis, down)
        array = jnp.concatenate([before, array, after], axis=dim)
    return array


def activate(hidden, gain_vec):
    inverse_rms = lax.rsqrt(jnp.mean(hidden * hidden, axis=-1, keepdims=True) + EPS)
    return jax.nn.silu(hidden * inverse_rms * gain_vec)


def build_table(features, border_list):
    channels = features.shape[1]
    edge_rows = features[border_list]
    neighbour_rows = with_halo(edge_rows, (("gx", 0), ("gy", 1)), 1)
    zero_row = jnp.zeros((1, channels), features.dtype)
    return jnp.concatenate([features, neighbour_rows.reshape(-1, channels), zero_row], axis=0)


def gather_local(rows, kernel_map):
    voxels = rows.shape[0]
    local_rows = jnp.arange(voxels, dtype=jnp.int32)
    selector = (kernel_map[:, :, None] == local_rows[None, None, :]).astype(rows.dtype)
    picked = jnp.einsum("kvu,uc->kvc", selector, rows, preferred_element_type=jnp.float32)
    return picked.astype(rows.dtype)


def pair_gather_kernel(map_ref, rows_ref, low_ref, high_ref):
    voxels = rows_ref.shape[0]
    pairs = low_ref.shape[0]
    rows = rows_ref[...]
    local_rows = lax.broadcasted_iota(jnp.int32, (voxels, voxels), 1)
    for k in range(pairs):
        selector = (map_ref[:, k:k + 1] == local_rows).astype(rows.dtype)
        low_ref[k] = jnp.dot(selector, rows, preferred_element_type=jnp.float32).astype(low_ref.dtype)
        high_ref[pairs - 1 - k] = lax.dot_general(
            rows, selector, (((0,), (0,)), ((), ())), preferred_element_type=jnp.float32
        ).astype(high_ref.dtype)


def gather_pairs(rows, map_t):
    voxels, channels = rows.shape
    pairs = map_t.shape[1]
    return pl.pallas_call(
        pair_gather_kernel,
        out_shape=(
            jax.ShapeDtypeStruct((pairs, voxels, channels), rows.dtype),
            jax.ShapeDtypeStruct((pairs, channels, voxels), rows.dtype),
        ),
        in_specs=[pl.BlockSpec(memory_space=pltpu.VMEM)] * 2,
        out_specs=(pl.BlockSpec(memory_space=pltpu.VMEM), pl.BlockSpec(memory_space=pltpu.VMEM)),
        compiler_params=pltpu.CompilerParams(vmem_limit_bytes=48 * 1024 * 1024),
        cost_estimate=pl.CostEstimate(
            flops=4 * pairs * voxels * voxels * channels,
            bytes_accessed=2 * (2 * pairs + 2) * voxels * channels + 4 * pairs * voxels,
            transcendentals=0,
        ),
    )(map_t, rows)


def pair_conv(low, rows, high, weight):
    pairs = low.shape[0]
    return (
        jnp.einsum("kvc,kcd->vd", low, weight[:pairs], preferred_element_type=jnp.float32)
        + jnp.dot(rows, weight[pairs], preferred_element_type=jnp.float32)
        + jnp.einsum("kcv,kcd->vd", high, weight[pairs + 1:], preferred_element_type=jnp.float32)
    )


def halo_layout(kernel_map, border_list):
    voxels = kernel_map.shape[1]
    boundary = border_list.shape[2]
    border_flat = border_list.reshape(-1)
    border_hot = (jnp.arange(voxels, dtype=jnp.int32)[:, None] == border_flat[None, :])
    named = jnp.einsum(
        "kv,vb->kb",
        kernel_map.astype(jnp.float32),
        border_hot.astype(jnp.float32),
        precision=lax.Precision.HIGHEST,
    )
    expected = np.zeros((27, 2, 2, boundary), np.int32)
    for k in range(27):
        step_x, step_y = k // 9 - 1, k // 3 % 3 - 1
        for i in range(2):
            for j in range(2):
                cell = (i + 1 + step_x) * 4 + (j + 1 + step_y)
                expected[k, i, j] = cell * boundary + np.arange(boundary)
    expected = jnp.asarray(expected.reshape(27, -1))
    flag = named == (expected + voxels).astype(jnp.float32)
    target = jnp.where(flag, expected, -1)
    return border_hot, target


def halo_hot(target, halo_count):
    return target[:, :, None] == jnp.arange(halo_count, dtype=jnp.int32)[None, None, :]


def halo_pick(halo, target):
    channels = halo.shape[-1]
    flat = halo.reshape(-1, channels)
    picked = jnp.einsum(
        "kbr,rc->kbc",
        halo_hot(target, flat.shape[0]).astype(flat.dtype),
        flat,
        preferred_element_type=jnp.float32,
    )
    return picked.astype(halo.dtype)


def edge_halo(features, border_hot, border_list):
    channels = features.shape[1]
    edge_rows = jnp.einsum(
        "vb,vc->bc", border_hot.astype(features.dtype), features, preferred_element_type=jnp.float32
    ).astype(features.dtype)
    edge_rows = edge_rows.reshape(border_list.shape + (channels,))
    return with_halo(edge_rows, (("gx", 0), ("gy", 1)), 1)


def conv_forward(features, kernel_map, border_list, border_hot, target, weight):
    low, high = gather_pairs(features, jnp.transpose(kernel_map[: kernel_map.shape[0] // 2]))
    halo_rows = halo_pick(edge_halo(features, border_hot, border_list), target)
    local_out = pair_conv(low, features, high, weight)
    border_out = jnp.einsum("kbc,kcd->bd", halo_rows, weight, preferred_element_type=jnp.float32)
    placed = jnp.einsum(
        "vb,bd->vd", border_hot.astype(jnp.float32), border_out, precision=lax.Precision.HIGHEST
    )
    return local_out + placed, (low, features, high), halo_rows


def backward_conv(gathered, halo_rows, kernel_map, weight, grad_rows, border_hot, target, border_list):
    grad_border = jnp.einsum(
        "vb,vd->bd", border_hot.astype(grad_rows.dtype), grad_rows, preferred_element_type=jnp.float32
    ).astype(grad_rows.dtype)
    low, centre, high = gathered
    pairs = low.shape[0]
    weight_grad = jnp.concatenate(
        [
            jnp.einsum("kvc,vd->kcd", low, grad_rows, preferred_element_type=jnp.float32),
            jnp.einsum("vc,vd->cd", centre, grad_rows, preferred_element_type=jnp.float32)[None],
            jnp.einsum("kcv,vd->kcd", high, grad_rows, preferred_element_type=jnp.float32),
        ],
        axis=0,
    ) + jnp.einsum("kbc,bd->kcd", halo_rows, grad_border, preferred_element_type=jnp.float32)
    flipped_weight = jnp.swapaxes(weight[::-1], 1, 2)
    grad_low, grad_high = gather_pairs(grad_rows, jnp.transpose(kernel_map[: kernel_map.shape[0] // 2]))
    local_part = pair_conv(grad_low, grad_rows, grad_high, flipped_weight)
    channels = grad_rows.shape[1]
    boundary = border_list.shape[2]
    spread = jnp.einsum(
        "kbr,bd->rkd",
        halo_hot(target, 16 * boundary).astype(grad_border.dtype),
        grad_border,
        preferred_element_type=jnp.float32,
    ).astype(grad_border.dtype)
    halo_grad = jnp.einsum(
        "rkd,kcd->rc", spread, weight, preferred_element_type=jnp.float32
    ).reshape(4, 4, boundary, channels)
    rows_end = jnp.stack([halo_grad[0], halo_grad[3]], axis=0)
    cols_end = jnp.stack([halo_grad[:, 0], halo_grad[:, 3]], axis=1)
    corner_end = jnp.stack([rows_end[:, 0], rows_end[:, 3]], axis=1)
    payload = jnp.stack([rows_end[:, 1:3], cols_end[1:3], corner_end], axis=2)
    received = with_halo(payload.astype(jnp.bfloat16), (("gx", 0), ("gy", 1)), 1).astype(
        payload.dtype
    )
    from_rows = jnp.stack([received[0, 1:3, 0], received[3, 1:3, 0]], axis=0)
    from_cols = jnp.stack([received[1:3, 0, 1], received[1:3, 3, 1]], axis=1)
    corner_low = jnp.stack([received[0, 0, 2], received[0, 3, 2]], axis=0)
    corner_high = jnp.stack([received[3, 0, 2], received[3, 3, 2]], axis=0)
    from_corner = jnp.stack([corner_low, corner_high], axis=0)
    folded = halo_grad[1:3, 1:3] + from_rows + from_cols + from_corner
    result = local_part + jnp.einsum(
        "vb,bd->vd",
        border_hot.astype(jnp.float32),
        folded.reshape(-1, channels),
        precision=lax.Precision.HIGHEST,
    )
    return (result, weight_grad)


HALVING_STEPS = (("gy", 1), ("gy", 2), ("gx", 1))
DOUBLING_STEPS = (("gx", 4), ("gy", 4), ("gx", 2), ("gx", 8))


def tree_psum(parts):
    flat = jnp.concatenate([jnp.ravel(p).astype(jnp.float32) for p in parts])
    lanes = 128
    rows = -(-flat.shape[0] // lanes)
    rows = -(-rows // (8 * 2 ** len(HALVING_STEPS))) * (8 * 2 ** len(HALVING_STEPS))
    x = jnp.pad(flat, (0, rows * lanes - flat.shape[0])).reshape(rows, lanes)
    bits = []
    for axis, mask in HALVING_STEPS:
        peers = lax.axis_size(axis)
        bit = (lax.axis_index(axis) // mask) % 2
        bits.append(bit)
        half = x.shape[0] // 2
        low, high = x[:half], x[half:]
        send = jnp.where(bit == 1, low, high)
        keep = jnp.where(bit == 1, high, low)
        x = keep + lax.ppermute(send, axis, [(i, i ^ mask) for i in range(peers)])
    for axis, mask in DOUBLING_STEPS:
        peers = lax.axis_size(axis)
        other = lax.ppermute(x, axis, [(i, i ^ mask) for i in range(peers)])
        x = x + other
    for (axis, mask), bit in reversed(list(zip(HALVING_STEPS, bits))):
        peers = lax.axis_size(axis)
        other = lax.ppermute(x, axis, [(i, i ^ mask) for i in range(peers)])
        x = jnp.where(bit == 1, jnp.concatenate([other, x]), jnp.concatenate([x, other]))
    flat = x.reshape(-1)
    out, start = [], 0
    for p in parts:
        size = math.prod(p.shape)
        out.append(flat[start:start + size].reshape(p.shape))
        start += size
    return tuple(out)


def slot_positions(destination, devices, capacity):
    points = destination.shape[0]
    block = math.gcd(points, 128)
    blocks = points // block
    dest_hot = destination[:, None] == jnp.arange(devices, dtype=jnp.int32)[None, :]
    grouped = dest_hot.astype(jnp.bfloat16).reshape(blocks, block, devices)
    lower = (
        jnp.arange(block, dtype=jnp.int32)[:, None] > jnp.arange(block, dtype=jnp.int32)[None, :]
    ).astype(jnp.bfloat16)
    within = jnp.einsum("ij,bjd->bid", lower, grouped, preferred_element_type=jnp.float32)
    totals = jnp.sum(grouped.astype(jnp.float32), axis=1)
    lower_blocks = (
        jnp.arange(blocks, dtype=jnp.int32)[:, None] > jnp.arange(blocks, dtype=jnp.int32)[None, :]
    ).astype(jnp.float32)
    offsets = jnp.einsum("ab,bd->ad", lower_blocks, totals, precision=lax.Precision.HIGHEST)
    earlier = (within + offsets[:, None, :]).reshape(points, devices)
    rank = jnp.sum(jnp.where(dest_hot, earlier, 0.0), axis=1).astype(jnp.int32)
    return destination * capacity + rank


def send_points(send_rows):
    return lax.all_to_all(send_rows, ("gx", "gy"), split_axis=0, concat_axis=0, tiled=True)


def return_grads(slot_grads):
    returned = lax.all_to_all(slot_grads, ("gx", "gy"), split_axis=0, concat_axis=0, tiled=True)
    return returned


def local(
    point_feats,
    point_dest,
    point_voxel,
    kernel_map,
    border_list,
    conv_one,
    conv_two,
    gain_one,
    gain_two,
    decoder_in,
    decoder_bias,
    decoder_out,
    target,
):
    devices = lax.axis_size("gx") * lax.axis_size("gy")
    voxels = kernel_map.shape[1]
    points, channels = point_feats.shape
    capacity = 2 * points // devices
    destination = point_dest[:, 0]
    position = slot_positions(destination, devices, capacity)
    slot_hot = (
        jnp.arange(devices * capacity, dtype=jnp.int32)[:, None] == position[None, :]
    ).astype(jnp.bfloat16)
    id_high = (point_voxel // 32 + 1).astype(jnp.bfloat16)
    id_low = (point_voxel % 32).astype(jnp.bfloat16)
    payload = jnp.concatenate(
        [
            point_feats,
            jnp.ones((points, 1), jnp.bfloat16),
            id_high[:, None],
            id_low[:, None],
        ],
        axis=1,
    )
    send = jnp.einsum(
        "sp,pc->sc", slot_hot, payload, preferred_element_type=jnp.float32
    ).astype(jnp.bfloat16)
    got = send_points(send.reshape(devices, capacity, channels + 3)).reshape(-1, channels + 3)
    flat_ids = ((got[:, channels + 1].astype(jnp.float32) - 1.0) * 32.0 + got[:, channels + 2].astype(jnp.float32)).astype(jnp.int32)
    voxel_rows = jnp.arange(voxels, dtype=jnp.int32)
    slot_match = (flat_ids[:, None] == voxel_rows[None, :]).astype(jnp.bfloat16)
    pooled = jnp.einsum(
        "sv,sc->vc", slot_match, got[:, : channels + 1], preferred_element_type=jnp.float32
    )
    pooled_sum = pooled[:, :channels]
    counts = pooled[:, channels]
    inverse = 1.0 / jnp.maximum(counts, 1.0)
    x_zero = (pooled_sum * inverse[:, None]).astype(jnp.bfloat16)
    border_hot, halo_target = halo_layout(kernel_map, border_list)
    hidden_one, gathered_one, halo_one = conv_forward(
        x_zero, kernel_map, border_list, border_hot, halo_target, conv_one
    )
    act_one = activate(hidden_one, gain_one).astype(jnp.bfloat16)
    hidden_two, gathered_two, halo_two = conv_forward(
        act_one, kernel_map, border_list, border_hot, halo_target, conv_two
    )
    block_out = (x_zero.astype(jnp.float32) + activate(hidden_two, gain_two)).astype(jnp.bfloat16)
    pre_dec = jnp.dot(block_out, decoder_in, preferred_element_type=jnp.float32) + decoder_bias
    dec_hidden = jax.nn.silu(pre_dec)
    sdf_values = jnp.sum(dec_hidden * decoder_out, axis=-1)
    whole_count = voxels * devices
    error_sdf = sdf_values - target
    loss_part = jnp.sum(error_sdf * error_sdf) / (2.0 * whole_count)
    grad_sdf = error_sdf / whole_count
    grad_out_part = jnp.sum(dec_hidden * grad_sdf[:, None], axis=0)
    _, pull_silu = jax.vjp(jax.nn.silu, pre_dec)
    grad_pre = pull_silu(grad_sdf[:, None] * decoder_out)[0]
    grad_bias_part = jnp.sum(grad_pre, axis=0)
    grad_pre_low = grad_pre.astype(jnp.bfloat16)
    grad_in_part = lax.dot_general(
        block_out, grad_pre_low, (((0,), (0,)), ((), ())), preferred_element_type=jnp.float32
    )
    grad_block = lax.dot_general(
        grad_pre_low, decoder_in, (((1,), (1,)), ((), ())), preferred_element_type=jnp.float32
    )
    _, pull_two = jax.vjp(lambda hidden: activate(hidden, gain_two), hidden_two)
    grad_hidden_two = pull_two(grad_block)[0].astype(jnp.bfloat16)
    grad_act_one, weight_grad_two = backward_conv(
        gathered_two, halo_two, kernel_map, conv_two, grad_hidden_two, border_hot, halo_target, border_list
    )
    _, pull_one = jax.vjp(lambda hidden: activate(hidden, gain_one), hidden_one)
    grad_hidden_one = pull_one(grad_act_one)[0].astype(jnp.bfloat16)
    input_part, weight_grad_one = backward_conv(
        gathered_one, halo_one, kernel_map, conv_one, grad_hidden_one, border_hot, halo_target, border_list
    )
    grad_x_zero = grad_block + input_part
    scaled = (grad_x_zero * inverse[:, None]).astype(jnp.bfloat16)
    slot_values = jnp.einsum(
        "sv,vc->sc", slot_match, scaled, preferred_element_type=jnp.float32
    ).astype(jnp.bfloat16)
    returned = return_grads(slot_values.reshape(devices, capacity, channels)).reshape(-1, channels)
    grad_points = jnp.einsum(
        "sp,sc->pc", slot_hot, returned, preferred_element_type=jnp.float32
    ).astype(jnp.bfloat16)
    parts = (weight_grad_one, weight_grad_two, grad_in_part, grad_bias_part, grad_out_part, loss_part)
    summed = tree_psum(parts)
    (
        grad_conv_one,
        grad_conv_two,
        grad_decoder_in,
        grad_decoder_bias,
        grad_decoder_out,
        loss_value,
    ) = summed
    return (
        sdf_values,
        loss_value,
        grad_conv_one,
        grad_conv_two,
        grad_decoder_in,
        grad_decoder_bias,
        grad_decoder_out,
        grad_points,
    )


def solution(mesh):
    in_specs = (
        P(("gx", "gy"), None),
        P(("gx", "gy"), None),
        P(("gx", "gy")),
        P(None, ("gx", "gy")),
        P("gx", "gy", None),
        P(),
        P(),
        P(),
        P(),
        P(),
        P(),
        P(),
        P(("gx", "gy")),
    )
    out_specs = (P(("gx", "gy")), P(), P(), P(), P(), P(), P(), P(("gx", "gy"), None))
    return jax.shard_map(local, mesh=mesh, in_specs=in_specs, out_specs=out_specs, check_vma=False)
```

```python
import math

import jax
import numpy as np
import jax.numpy as jnp
from jax import lax
from jax.experimental import pallas as pl
from jax.experimental.pallas import tpu as pltpu
from jax.sharding import PartitionSpec as P

EPS = 1e-05


def with_halo(array, sides, width):
    for axis, dim in sides:
        peers, length = (lax.axis_size(axis), array.shape[dim])
        up = [(i, (i + 1) % peers) for i in range(peers - 1)]
        down = [(j, i) for i, j in up]
        last = lax.slice_in_dim(array, length - width, length, axis=dim)
        leading = lax.slice_in_dim(array, 0, width, axis=dim)
        before = lax.ppermute(last, axis, up)
        after = lax.ppermute(leading, axis, down)
        array = jnp.concatenate([before, array, after], axis=dim)
    return array


def activate(hidden, gain_vec):
    inverse_rms = lax.rsqrt(jnp.mean(hidden * hidden, axis=-1, keepdims=True) + EPS)
    return jax.nn.silu(hidden * inverse_rms * gain_vec)


def build_table(features, border_list):
    channels = features.shape[1]
    edge_rows = features[border_list]
    neighbour_rows = with_halo(edge_rows, (("gx", 0), ("gy", 1)), 1)
    zero_row = jnp.zeros((1, channels), features.dtype)
    return jnp.concatenate([features, neighbour_rows.reshape(-1, channels), zero_row], axis=0)


def gather_local(rows, kernel_map):
    voxels = rows.shape[0]
    local_rows = jnp.arange(voxels, dtype=jnp.int32)
    selector = (kernel_map[:, :, None] == local_rows[None, None, :]).astype(rows.dtype)
    picked = jnp.einsum("kvu,uc->kvc", selector, rows, preferred_element_type=jnp.float32)
    return picked.astype(rows.dtype)


def pair_gather_kernel(map_ref, rows_ref, rows_t_ref, low_ref, high_ref):
    voxels = rows_ref.shape[0]
    pairs = low_ref.shape[0]
    rows = rows_ref[...]
    rows_t = rows_t_ref[...]
    local_rows = lax.broadcasted_iota(jnp.int32, (voxels, voxels), 1)
    for k in range(pairs):
        selector = (map_ref[:, k:k + 1] == local_rows).astype(rows.dtype)
        low_ref[k] = jnp.dot(selector, rows, preferred_element_type=jnp.float32).astype(low_ref.dtype)
        high_ref[pairs - 1 - k] = jnp.dot(rows_t, selector, preferred_element_type=jnp.float32).astype(high_ref.dtype)


def gather_pairs(rows, map_t):
    voxels, channels = rows.shape
    pairs = map_t.shape[1]
    return pl.pallas_call(
        pair_gather_kernel,
        out_shape=(
            jax.ShapeDtypeStruct((pairs, voxels, channels), rows.dtype),
            jax.ShapeDtypeStruct((pairs, channels, voxels), rows.dtype),
        ),
        in_specs=[pl.BlockSpec(memory_space=pltpu.VMEM)] * 3,
        out_specs=(pl.BlockSpec(memory_space=pltpu.VMEM), pl.BlockSpec(memory_space=pltpu.VMEM)),
        compiler_params=pltpu.CompilerParams(vmem_limit_bytes=48 * 1024 * 1024),
        cost_estimate=pl.CostEstimate(
            flops=4 * pairs * voxels * voxels * channels,
            bytes_accessed=2 * (2 * pairs + 2) * voxels * channels + 4 * pairs * voxels,
            transcendentals=0,
        ),
    )(map_t, rows, jnp.transpose(rows))


def pair_conv(low, rows, high, weight):
    pairs = low.shape[0]
    return (
        jnp.einsum("kvc,kcd->vd", low, weight[:pairs], preferred_element_type=jnp.float32)
        + jnp.dot(rows, weight[pairs], preferred_element_type=jnp.float32)
        + jnp.einsum("kcv,kcd->vd", high, weight[pairs + 1:], preferred_element_type=jnp.float32)
    )


def halo_layout(kernel_map, border_list):
    voxels = kernel_map.shape[1]
    boundary = border_list.shape[2]
    border_flat = border_list.reshape(-1)
    border_hot = (jnp.arange(voxels, dtype=jnp.int32)[:, None] == border_flat[None, :])
    named = jnp.einsum(
        "kv,vb->kb",
        kernel_map.astype(jnp.float32),
        border_hot.astype(jnp.float32),
        precision=lax.Precision.HIGHEST,
    )
    expected = np.zeros((27, 2, 2, boundary), np.int32)
    for k in range(27):
        step_x, step_y = k // 9 - 1, k // 3 % 3 - 1
        for i in range(2):
            for j in range(2):
                cell = (i + 1 + step_x) * 4 + (j + 1 + step_y)
                expected[k, i, j] = cell * boundary + np.arange(boundary)
    expected = jnp.asarray(expected.reshape(27, -1))
    flag = named == (expected + voxels).astype(jnp.float32)
    target = jnp.where(flag, expected, -1)
    return border_hot, target


def halo_hot(target, halo_count):
    return target[:, :, None] == jnp.arange(halo_count, dtype=jnp.int32)[None, None, :]


def halo_pick(halo, target):
    channels = halo.shape[-1]
    flat = halo.reshape(-1, channels)
    picked = jnp.einsum(
        "kbr,rc->kbc",
        halo_hot(target, flat.shape[0]).astype(flat.dtype),
        flat,
        preferred_element_type=jnp.float32,
    )
    return picked.astype(halo.dtype)


def edge_halo(features, border_hot, border_list):
    channels = features.shape[1]
    edge_rows = jnp.einsum(
        "vb,vc->bc", border_hot.astype(features.dtype), features, preferred_element_type=jnp.float32
    ).astype(features.dtype)
    edge_rows = edge_rows.reshape(border_list.shape + (channels,))
    return with_halo(edge_rows, (("gx", 0), ("gy", 1)), 1)


def conv_forward(features, kernel_map, border_list, border_hot, target, weight):
    low, high = gather_pairs(features, jnp.transpose(kernel_map[: kernel_map.shape[0] // 2]))
    halo_rows = halo_pick(edge_halo(features, border_hot, border_list), target)
    local_out = pair_conv(low, features, high, weight)
    border_out = jnp.einsum("kbc,kcd->bd", halo_rows, weight, preferred_element_type=jnp.float32)
    placed = jnp.einsum(
        "vb,bd->vd", border_hot.astype(jnp.float32), border_out, precision=lax.Precision.HIGHEST
    )
    return local_out + placed, (low, features, high), halo_rows


def backward_conv(gathered, halo_rows, kernel_map, weight, grad_rows, border_hot, target, border_list):
    grad_border = jnp.einsum(
        "vb,vd->bd", border_hot.astype(grad_rows.dtype), grad_rows, preferred_element_type=jnp.float32
    ).astype(grad_rows.dtype)
    low, centre, high = gathered
    pairs = low.shape[0]
    weight_grad = jnp.concatenate(
        [
            jnp.einsum("kvc,vd->kcd", low, grad_rows, preferred_element_type=jnp.float32),
            jnp.einsum("vc,vd->cd", centre, grad_rows, preferred_element_type=jnp.float32)[None],
            jnp.einsum("kcv,vd->kcd", high, grad_rows, preferred_element_type=jnp.float32),
        ],
        axis=0,
    ) + jnp.einsum("kbc,bd->kcd", halo_rows, grad_border, preferred_element_type=jnp.float32)
    flipped_weight = jnp.swapaxes(weight[::-1], 1, 2)
    grad_low, grad_high = gather_pairs(grad_rows, jnp.transpose(kernel_map[: kernel_map.shape[0] // 2]))
    local_part = pair_conv(grad_low, grad_rows, grad_high, flipped_weight)
    channels = grad_rows.shape[1]
    boundary = border_list.shape[2]
    spread = jnp.einsum(
        "kbr,bd->rkd",
        halo_hot(target, 16 * boundary).astype(grad_border.dtype),
        grad_border,
        preferred_element_type=jnp.float32,
    ).astype(grad_border.dtype)
    halo_grad = jnp.einsum(
        "rkd,kcd->rc", spread, weight, preferred_element_type=jnp.float32
    ).reshape(4, 4, boundary, channels)
    rows_end = jnp.stack([halo_grad[0], halo_grad[3]], axis=0)
    cols_end = jnp.stack([halo_grad[:, 0], halo_grad[:, 3]], axis=1)
    corner_end = jnp.stack([rows_end[:, 0], rows_end[:, 3]], axis=1)
    payload = jnp.stack([rows_end[:, 1:3], cols_end[1:3], corner_end], axis=2)
    received = with_halo(payload.astype(jnp.bfloat16), (("gx", 0), ("gy", 1)), 1).astype(
        payload.dtype
    )
    from_rows = jnp.stack([received[0, 1:3, 0], received[3, 1:3, 0]], axis=0)
    from_cols = jnp.stack([received[1:3, 0, 1], received[1:3, 3, 1]], axis=1)
    corner_low = jnp.stack([received[0, 0, 2], received[0, 3, 2]], axis=0)
    corner_high = jnp.stack([received[3, 0, 2], received[3, 3, 2]], axis=0)
    from_corner = jnp.stack([corner_low, corner_high], axis=0)
    folded = halo_grad[1:3, 1:3] + from_rows + from_cols + from_corner
    result = local_part + jnp.einsum(
        "vb,bd->vd",
        border_hot.astype(jnp.float32),
        folded.reshape(-1, channels),
        precision=lax.Precision.HIGHEST,
    )
    return (result, weight_grad)


HALVING_STEPS = (("gy", 1), ("gy", 2), ("gx", 1))
DOUBLING_STEPS = (("gx", 4), ("gy", 4), ("gx", 2), ("gx", 8))


def tree_psum(parts, tie):
    flat = jnp.concatenate([jnp.ravel(p).astype(jnp.float32) for p in parts])
    lanes = 128
    rows = -(-flat.shape[0] // lanes)
    rows = -(-rows // (8 * 2 ** len(HALVING_STEPS))) * (8 * 2 ** len(HALVING_STEPS))
    x = jnp.pad(flat, (0, rows * lanes - flat.shape[0])).reshape(rows, lanes)
    bits = []
    for axis, mask in HALVING_STEPS:
        peers = lax.axis_size(axis)
        bit = (lax.axis_index(axis) // mask) % 2
        bits.append(bit)
        half = x.shape[0] // 2
        low, high = x[:half], x[half:]
        send = jnp.where(bit == 1, low, high)
        keep = jnp.where(bit == 1, high, low)
        x = keep + lax.ppermute(send, axis, [(i, i ^ mask) for i in range(peers)])
    for axis, mask in DOUBLING_STEPS:
        peers = lax.axis_size(axis)
        bit = (lax.axis_index(axis) // mask) % 2
        other = lax.ppermute(x, axis, [(i, i ^ mask) for i in range(peers)])
        x = jnp.where(bit == 1, other + x, x + other)
    x, tie = lax.optimization_barrier((x, tie))
    for (axis, mask), bit in reversed(list(zip(HALVING_STEPS, bits))):
        peers = lax.axis_size(axis)
        other = lax.ppermute(x, axis, [(i, i ^ mask) for i in range(peers)])
        x = jnp.where(bit == 1, jnp.concatenate([other, x]), jnp.concatenate([x, other]))
    flat = x.reshape(-1)
    out, start = [], 0
    for p in parts:
        size = math.prod(p.shape)
        out.append(flat[start:start + size].reshape(p.shape))
        start += size
    return tuple(out), tie


def slot_positions(destination, devices, capacity):
    points = destination.shape[0]
    block = math.gcd(points, 128)
    blocks = points // block
    dest_hot = destination[:, None] == jnp.arange(devices, dtype=jnp.int32)[None, :]
    grouped = dest_hot.astype(jnp.bfloat16).reshape(blocks, block, devices)
    lower = (
        jnp.arange(block, dtype=jnp.int32)[:, None] > jnp.arange(block, dtype=jnp.int32)[None, :]
    ).astype(jnp.bfloat16)
    within = jnp.einsum("ij,bjd->bid", lower, grouped, preferred_element_type=jnp.float32)
    totals = jnp.sum(grouped.astype(jnp.float32), axis=1)
    lower_blocks = (
        jnp.arange(blocks, dtype=jnp.int32)[:, None] > jnp.arange(blocks, dtype=jnp.int32)[None, :]
    ).astype(jnp.float32)
    offsets = jnp.einsum("ab,bd->ad", lower_blocks, totals, precision=lax.Precision.HIGHEST)
    earlier = (within + offsets[:, None, :]).reshape(points, devices)
    rank = jnp.sum(jnp.where(dest_hot, earlier, 0.0), axis=1).astype(jnp.int32)
    return destination * capacity + rank


def send_points(send_rows):
    return lax.all_to_all(send_rows, ("gx", "gy"), split_axis=0, concat_axis=0, tiled=True)


def return_grads(slot_grads):
    returned = lax.all_to_all(slot_grads, ("gx", "gy"), split_axis=0, concat_axis=0, tiled=True)
    return returned


def local(
    point_feats,
    point_dest,
    point_voxel,
    kernel_map,
    border_list,
    conv_one,
    conv_two,
    gain_one,
    gain_two,
    decoder_in,
    decoder_bias,
    decoder_out,
    target,
):
    devices = lax.axis_size("gx") * lax.axis_size("gy")
    voxels = kernel_map.shape[1]
    points, channels = point_feats.shape
    capacity = 2 * points // devices
    destination = point_dest[:, 0]
    position = slot_positions(destination, devices, capacity)
    slot_hot = (
        jnp.arange(devices * capacity, dtype=jnp.int32)[:, None] == position[None, :]
    ).astype(jnp.bfloat16)
    id_high = (point_voxel // 32 + 1).astype(jnp.bfloat16)
    id_low = (point_voxel % 32).astype(jnp.bfloat16)
    payload = jnp.concatenate(
        [
            point_feats,
            jnp.ones((points, 1), jnp.bfloat16),
            id_high[:, None],
            id_low[:, None],
        ],
        axis=1,
    )
    send = jnp.einsum(
        "sp,pc->sc", slot_hot, payload, preferred_element_type=jnp.float32
    ).astype(jnp.bfloat16)
    got = send_points(send.reshape(devices, capacity, channels + 3)).reshape(-1, channels + 3)
    flat_ids = ((got[:, channels + 1].astype(jnp.float32) - 1.0) * 32.0 + got[:, channels + 2].astype(jnp.float32)).astype(jnp.int32)
    voxel_rows = jnp.arange(voxels, dtype=jnp.int32)
    slot_match = (flat_ids[:, None] == voxel_rows[None, :]).astype(jnp.bfloat16)
    pooled = jnp.einsum(
        "sv,sc->vc", slot_match, got[:, : channels + 1], preferred_element_type=jnp.float32
    )
    pooled_sum = pooled[:, :channels]
    counts = pooled[:, channels]
    inverse = 1.0 / jnp.maximum(counts, 1.0)
    x_zero = (pooled_sum * inverse[:, None]).astype(jnp.bfloat16)
    border_hot, halo_target = halo_layout(kernel_map, border_list)
    hidden_one, gathered_one, halo_one = conv_forward(
        x_zero, kernel_map, border_list, border_hot, halo_target, conv_one
    )
    act_one = activate(hidden_one, gain_one).astype(jnp.bfloat16)
    hidden_two, gathered_two, halo_two = conv_forward(
        act_one, kernel_map, border_list, border_hot, halo_target, conv_two
    )
    block_out = (x_zero.astype(jnp.float32) + activate(hidden_two, gain_two)).astype(jnp.bfloat16)
    pre_dec = jnp.dot(block_out, decoder_in, preferred_element_type=jnp.float32) + decoder_bias
    dec_hidden = jax.nn.silu(pre_dec)
    sdf_values = jnp.sum(dec_hidden * decoder_out, axis=-1)
    whole_count = voxels * devices
    error_sdf = sdf_values - target
    loss_part = jnp.sum(error_sdf * error_sdf) / (2.0 * whole_count)
    grad_sdf = error_sdf / whole_count
    grad_out_part = jnp.sum(dec_hidden * grad_sdf[:, None], axis=0)
    _, pull_silu = jax.vjp(jax.nn.silu, pre_dec)
    grad_pre = pull_silu(grad_sdf[:, None] * decoder_out)[0]
    grad_bias_part = jnp.sum(grad_pre, axis=0)
    grad_pre_low = grad_pre.astype(jnp.bfloat16)
    grad_in_part = lax.dot_general(
        block_out, grad_pre_low, (((0,), (0,)), ((), ())), preferred_element_type=jnp.float32
    )
    grad_block = lax.dot_general(
        grad_pre_low, decoder_in, (((1,), (1,)), ((), ())), preferred_element_type=jnp.float32
    )
    _, pull_two = jax.vjp(lambda hidden: activate(hidden, gain_two), hidden_two)
    grad_hidden_two = pull_two(grad_block)[0].astype(jnp.bfloat16)
    grad_act_one, weight_grad_two = backward_conv(
        gathered_two, halo_two, kernel_map, conv_two, grad_hidden_two, border_hot, halo_target, border_list
    )
    _, pull_one = jax.vjp(lambda hidden: activate(hidden, gain_one), hidden_one)
    grad_hidden_one = pull_one(grad_act_one)[0].astype(jnp.bfloat16)
    input_part, weight_grad_one = backward_conv(
        gathered_one, halo_one, kernel_map, conv_one, grad_hidden_one, border_hot, halo_target, border_list
    )
    grad_x_zero = grad_block + input_part
    scaled = (grad_x_zero * inverse[:, None]).astype(jnp.bfloat16)
    slot_values = jnp.einsum(
        "sv,vc->sc", slot_match, scaled, preferred_element_type=jnp.float32
    ).astype(jnp.bfloat16)
    returned = return_grads(slot_values.reshape(devices, capacity, channels)).reshape(-1, channels)
    grad_points = jnp.einsum(
        "sp,sc->pc", slot_hot, returned, preferred_element_type=jnp.float32
    ).astype(jnp.bfloat16)
    parts = (weight_grad_one, weight_grad_two, grad_in_part, grad_bias_part, grad_out_part, loss_part)
    summed, grad_points = tree_psum(parts, grad_points)
    (
        grad_conv_one,
        grad_conv_two,
        grad_decoder_in,
        grad_decoder_bias,
        grad_decoder_out,
        loss_value,
    ) = summed
    return (
        sdf_values,
        loss_value,
        grad_conv_one,
        grad_conv_two,
        grad_decoder_in,
        grad_decoder_bias,
        grad_decoder_out,
        grad_points,
    )


def solution(mesh):
    in_specs = (
        P(("gx", "gy"), None),
        P(("gx", "gy"), None),
        P(("gx", "gy")),
        P(None, ("gx", "gy")),
        P("gx", "gy", None),
        P(),
        P(),
        P(),
        P(),
        P(),
        P(),
        P(),
        P(("gx", "gy")),
    )
    out_specs = (P(("gx", "gy")), P(), P(), P(), P(), P(), P(), P(("gx", "gy"), None))
    return jax.shard_map(local, mesh=mesh, in_specs=in_specs, out_specs=out_specs, check_vma=False)
```

```python
import math

import jax
import numpy as np
import jax.numpy as jnp
from jax import lax
from jax.experimental import pallas as pl
from jax.experimental.pallas import tpu as pltpu
from jax.sharding import PartitionSpec as P

EPS = 1e-05


def with_halo(array, sides, width):
    for axis, dim in sides:
        peers, length = (lax.axis_size(axis), array.shape[dim])
        up = [(i, (i + 1) % peers) for i in range(peers - 1)]
        down = [(j, i) for i, j in up]
        last = lax.slice_in_dim(array, length - width, length, axis=dim)
        leading = lax.slice_in_dim(array, 0, width, axis=dim)
        before = lax.ppermute(last, axis, up)
        after = lax.ppermute(leading, axis, down)
        array = jnp.concatenate([before, array, after], axis=dim)
    return array


def activate(hidden, gain_vec):
    inverse_rms = lax.rsqrt(jnp.mean(hidden * hidden, axis=-1, keepdims=True) + EPS)
    return jax.nn.silu(hidden * inverse_rms * gain_vec)


def build_table(features, border_list):
    channels = features.shape[1]
    edge_rows = features[border_list]
    neighbour_rows = with_halo(edge_rows, (("gx", 0), ("gy", 1)), 1)
    zero_row = jnp.zeros((1, channels), features.dtype)
    return jnp.concatenate([features, neighbour_rows.reshape(-1, channels), zero_row], axis=0)


def gather_local(rows, kernel_map):
    voxels = rows.shape[0]
    local_rows = jnp.arange(voxels, dtype=jnp.int32)
    selector = (kernel_map[:, :, None] == local_rows[None, None, :]).astype(rows.dtype)
    picked = jnp.einsum("kvu,uc->kvc", selector, rows, preferred_element_type=jnp.float32)
    return picked.astype(rows.dtype)


def pair_gather_kernel(map_ref, rows_ref, rows_t_ref, low_ref, high_ref):
    voxels = rows_ref.shape[0]
    pairs = low_ref.shape[0]
    rows = rows_ref[...]
    rows_t = rows_t_ref[...]
    local_rows = lax.broadcasted_iota(jnp.int32, (voxels, voxels), 1)
    for k in range(pairs):
        selector = (map_ref[:, k:k + 1] == local_rows).astype(rows.dtype)
        low_ref[k] = jnp.dot(selector, rows, preferred_element_type=jnp.float32).astype(low_ref.dtype)
        high_ref[pairs - 1 - k] = jnp.dot(rows_t, selector, preferred_element_type=jnp.float32).astype(high_ref.dtype)


def gather_pairs(rows, map_t):
    voxels, channels = rows.shape
    pairs = map_t.shape[1]
    return pl.pallas_call(
        pair_gather_kernel,
        out_shape=(
            jax.ShapeDtypeStruct((pairs, voxels, channels), rows.dtype),
            jax.ShapeDtypeStruct((pairs, channels, voxels), rows.dtype),
        ),
        in_specs=[pl.BlockSpec(memory_space=pltpu.VMEM)] * 3,
        out_specs=(pl.BlockSpec(memory_space=pltpu.VMEM), pl.BlockSpec(memory_space=pltpu.VMEM)),
        compiler_params=pltpu.CompilerParams(vmem_limit_bytes=48 * 1024 * 1024),
        cost_estimate=pl.CostEstimate(
            flops=4 * pairs * voxels * voxels * channels,
            bytes_accessed=2 * (2 * pairs + 2) * voxels * channels + 4 * pairs * voxels,
            transcendentals=0,
        ),
    )(map_t, rows, jnp.transpose(rows))


def pair_conv(low, rows, high, weight):
    pairs = low.shape[0]
    return (
        jnp.einsum("kvc,kcd->vd", low, weight[:pairs], preferred_element_type=jnp.float32)
        + jnp.dot(rows, weight[pairs], preferred_element_type=jnp.float32)
        + jnp.einsum("kcv,kcd->vd", high, weight[pairs + 1:], preferred_element_type=jnp.float32)
    )


def halo_layout(kernel_map, border_list):
    voxels = kernel_map.shape[1]
    boundary = border_list.shape[2]
    border_flat = border_list.reshape(-1)
    border_hot = (jnp.arange(voxels, dtype=jnp.int32)[:, None] == border_flat[None, :])
    named = jnp.einsum(
        "kv,vb->kb",
        kernel_map.astype(jnp.float32),
        border_hot.astype(jnp.float32),
        precision=lax.Precision.HIGHEST,
    )
    expected = np.zeros((27, 2, 2, boundary), np.int32)
    for k in range(27):
        step_x, step_y = k // 9 - 1, k // 3 % 3 - 1
        for i in range(2):
            for j in range(2):
                cell = (i + 1 + step_x) * 4 + (j + 1 + step_y)
                expected[k, i, j] = cell * boundary + np.arange(boundary)
    expected = jnp.asarray(expected.reshape(27, -1))
    flag = named == (expected + voxels).astype(jnp.float32)
    target = jnp.where(flag, expected, -1)
    return border_hot, target


def halo_hot(target, halo_count):
    return target[:, :, None] == jnp.arange(halo_count, dtype=jnp.int32)[None, None, :]


def halo_pick(halo, target):
    channels = halo.shape[-1]
    flat = halo.reshape(-1, channels)
    picked = jnp.einsum(
        "kbr,rc->kbc",
        halo_hot(target, flat.shape[0]).astype(flat.dtype),
        flat,
        preferred_element_type=jnp.float32,
    )
    return picked.astype(halo.dtype)


def edge_halo(features, border_hot, border_list):
    channels = features.shape[1]
    edge_rows = jnp.einsum(
        "vb,vc->bc", border_hot.astype(features.dtype), features, preferred_element_type=jnp.float32
    ).astype(features.dtype)
    edge_rows = edge_rows.reshape(border_list.shape + (channels,))
    return with_halo(edge_rows, (("gx", 0), ("gy", 1)), 1)


def conv_forward(features, kernel_map, border_list, border_hot, target, weight):
    low, high = gather_pairs(features, jnp.transpose(kernel_map[: kernel_map.shape[0] // 2]))
    halo_rows = halo_pick(edge_halo(features, border_hot, border_list), target)
    local_out = pair_conv(low, features, high, weight)
    border_out = jnp.einsum("kbc,kcd->bd", halo_rows, weight, preferred_element_type=jnp.float32)
    placed = jnp.einsum(
        "vb,bd->vd", border_hot.astype(jnp.float32), border_out, precision=lax.Precision.HIGHEST
    )
    return local_out + placed, (low, features, high), halo_rows


def backward_conv(gathered, halo_rows, kernel_map, weight, grad_rows, border_hot, target, border_list):
    grad_border = jnp.einsum(
        "vb,vd->bd", border_hot.astype(grad_rows.dtype), grad_rows, preferred_element_type=jnp.float32
    ).astype(grad_rows.dtype)
    low, centre, high = gathered
    pairs = low.shape[0]
    weight_grad = jnp.concatenate(
        [
            jnp.einsum("kvc,vd->kcd", low, grad_rows, preferred_element_type=jnp.float32),
            jnp.einsum("vc,vd->cd", centre, grad_rows, preferred_element_type=jnp.float32)[None],
            jnp.einsum("kcv,vd->kcd", high, grad_rows, preferred_element_type=jnp.float32),
        ],
        axis=0,
    ) + jnp.einsum("kbc,bd->kcd", halo_rows, grad_border, preferred_element_type=jnp.float32)
    flipped_weight = jnp.swapaxes(weight[::-1], 1, 2)
    grad_low, grad_high = gather_pairs(grad_rows, jnp.transpose(kernel_map[: kernel_map.shape[0] // 2]))
    local_part = pair_conv(grad_low, grad_rows, grad_high, flipped_weight)
    channels = grad_rows.shape[1]
    boundary = border_list.shape[2]
    spread = jnp.einsum(
        "kbr,bd->rkd",
        halo_hot(target, 16 * boundary).astype(grad_border.dtype),
        grad_border,
        preferred_element_type=jnp.float32,
    ).astype(grad_border.dtype)
    halo_grad = jnp.einsum(
        "rkd,kcd->rc", spread, weight, preferred_element_type=jnp.float32
    ).reshape(4, 4, boundary, channels)
    rows_end = jnp.stack([halo_grad[0], halo_grad[3]], axis=0)
    cols_end = jnp.stack([halo_grad[:, 0], halo_grad[:, 3]], axis=1)
    corner_end = jnp.stack([rows_end[:, 0], rows_end[:, 3]], axis=1)
    payload = jnp.stack([rows_end[:, 1:3], cols_end[1:3], corner_end], axis=2)
    received = with_halo(payload.astype(jnp.bfloat16), (("gx", 0), ("gy", 1)), 1).astype(
        payload.dtype
    )
    from_rows = jnp.stack([received[0, 1:3, 0], received[3, 1:3, 0]], axis=0)
    from_cols = jnp.stack([received[1:3, 0, 1], received[1:3, 3, 1]], axis=1)
    corner_low = jnp.stack([received[0, 0, 2], received[0, 3, 2]], axis=0)
    corner_high = jnp.stack([received[3, 0, 2], received[3, 3, 2]], axis=0)
    from_corner = jnp.stack([corner_low, corner_high], axis=0)
    folded = halo_grad[1:3, 1:3] + from_rows + from_cols + from_corner
    result = local_part + jnp.einsum(
        "vb,bd->vd",
        border_hot.astype(jnp.float32),
        folded.reshape(-1, channels),
        precision=lax.Precision.HIGHEST,
    )
    return (result, weight_grad)


HALVING_STEPS = (("gy", 1), ("gy", 2), ("gx", 1))
DOUBLING_STEPS = (("gx", 4), ("gy", 4), ("gx", 2), ("gx", 8))


def tree_psum(parts, tie):
    one, two, grad_in, grad_bias, grad_out, loss = parts
    lanes = grad_in.shape[1]
    kernels = jnp.concatenate([one, two], axis=2).reshape(-1, lanes)
    small = jnp.stack([grad_bias, grad_out, jnp.full((lanes,), loss)], axis=0)
    stacked = jnp.concatenate([kernels, grad_in, small], axis=0)
    rows = -(-stacked.shape[0] // (8 * 2 ** len(HALVING_STEPS))) * (8 * 2 ** len(HALVING_STEPS))
    x = jnp.pad(stacked, ((0, rows - stacked.shape[0]), (0, 0)))
    bits = []
    for axis, mask in HALVING_STEPS:
        peers = lax.axis_size(axis)
        bit = (lax.axis_index(axis) // mask) % 2
        bits.append(bit)
        half = x.shape[0] // 2
        low, high = x[:half], x[half:]
        send = jnp.where(bit == 1, low, high)
        keep = jnp.where(bit == 1, high, low)
        x = keep + lax.ppermute(send, axis, [(i, i ^ mask) for i in range(peers)])
    for axis, mask in DOUBLING_STEPS:
        peers = lax.axis_size(axis)
        bit = (lax.axis_index(axis) // mask) % 2
        other = lax.ppermute(x, axis, [(i, i ^ mask) for i in range(peers)])
        x = jnp.where(bit == 1, other + x, x + other)
    x, tie = lax.optimization_barrier((x, tie))
    for (axis, mask), bit in reversed(list(zip(HALVING_STEPS, bits))):
        peers = lax.axis_size(axis)
        other = lax.ppermute(x, axis, [(i, i ^ mask) for i in range(peers)])
        x = jnp.where(bit == 1, jnp.concatenate([other, x]), jnp.concatenate([x, other]))
    kernel_rows = kernels.shape[0]
    summed_kernels = x[:kernel_rows].reshape(one.shape[0], one.shape[1], 2 * one.shape[2])
    out = [
        summed_kernels[:, :, : one.shape[2]],
        summed_kernels[:, :, one.shape[2]:],
        x[kernel_rows:kernel_rows + grad_in.shape[0]],
        x[kernel_rows + grad_in.shape[0]],
        x[kernel_rows + grad_in.shape[0] + 1],
        x[kernel_rows + grad_in.shape[0] + 2, 0],
    ]
    return tuple(out), tie


def slot_positions(destination, devices, capacity):
    points = destination.shape[0]
    block = math.gcd(points, 128)
    blocks = points // block
    dest_hot = destination[:, None] == jnp.arange(devices, dtype=jnp.int32)[None, :]
    grouped = dest_hot.astype(jnp.bfloat16).reshape(blocks, block, devices)
    lower = (
        jnp.arange(block, dtype=jnp.int32)[:, None] > jnp.arange(block, dtype=jnp.int32)[None, :]
    ).astype(jnp.bfloat16)
    within = jnp.einsum("ij,bjd->bid", lower, grouped, preferred_element_type=jnp.float32)
    totals = jnp.sum(grouped.astype(jnp.float32), axis=1)
    lower_blocks = (
        jnp.arange(blocks, dtype=jnp.int32)[:, None] > jnp.arange(blocks, dtype=jnp.int32)[None, :]
    ).astype(jnp.float32)
    offsets = jnp.einsum("ab,bd->ad", lower_blocks, totals, precision=lax.Precision.HIGHEST)
    earlier = (within + offsets[:, None, :]).reshape(points, devices)
    rank = jnp.sum(jnp.where(dest_hot, earlier, 0.0), axis=1).astype(jnp.int32)
    return destination * capacity + rank


def send_points(send_rows):
    return lax.all_to_all(send_rows, ("gx", "gy"), split_axis=0, concat_axis=0, tiled=True)


def return_grads(slot_grads):
    returned = lax.all_to_all(slot_grads, ("gx", "gy"), split_axis=0, concat_axis=0, tiled=True)
    return returned


def local(
    point_feats,
    point_dest,
    point_voxel,
    kernel_map,
    border_list,
    conv_one,
    conv_two,
    gain_one,
    gain_two,
    decoder_in,
    decoder_bias,
    decoder_out,
    target,
):
    devices = lax.axis_size("gx") * lax.axis_size("gy")
    voxels = kernel_map.shape[1]
    points, channels = point_feats.shape
    capacity = 2 * points // devices
    destination = point_dest[:, 0]
    position = slot_positions(destination, devices, capacity)
    slot_hot = (
        jnp.arange(devices * capacity, dtype=jnp.int32)[:, None] == position[None, :]
    ).astype(jnp.bfloat16)
    id_high = (point_voxel // 32 + 1).astype(jnp.bfloat16)
    id_low = (point_voxel % 32).astype(jnp.bfloat16)
    payload = jnp.concatenate(
        [
            point_feats,
            jnp.ones((points, 1), jnp.bfloat16),
            id_high[:, None],
            id_low[:, None],
        ],
        axis=1,
    )
    send = jnp.einsum(
        "sp,pc->sc", slot_hot, payload, preferred_element_type=jnp.float32
    ).astype(jnp.bfloat16)
    got = send_points(send.reshape(devices, capacity, channels + 3)).reshape(-1, channels + 3)
    flat_ids = ((got[:, channels + 1].astype(jnp.float32) - 1.0) * 32.0 + got[:, channels + 2].astype(jnp.float32)).astype(jnp.int32)
    voxel_rows = jnp.arange(voxels, dtype=jnp.int32)
    slot_match = (flat_ids[:, None] == voxel_rows[None, :]).astype(jnp.bfloat16)
    pooled = jnp.einsum(
        "sv,sc->vc", slot_match, got[:, : channels + 1], preferred_element_type=jnp.float32
    )
    pooled_sum = pooled[:, :channels]
    counts = pooled[:, channels]
    inverse = 1.0 / jnp.maximum(counts, 1.0)
    x_zero = (pooled_sum * inverse[:, None]).astype(jnp.bfloat16)
    border_hot, halo_target = halo_layout(kernel_map, border_list)
    hidden_one, gathered_one, halo_one = conv_forward(
        x_zero, kernel_map, border_list, border_hot, halo_target, conv_one
    )
    act_one = activate(hidden_one, gain_one).astype(jnp.bfloat16)
    hidden_two, gathered_two, halo_two = conv_forward(
        act_one, kernel_map, border_list, border_hot, halo_target, conv_two
    )
    block_out = (x_zero.astype(jnp.float32) + activate(hidden_two, gain_two)).astype(jnp.bfloat16)
    pre_dec = jnp.dot(block_out, decoder_in, preferred_element_type=jnp.float32) + decoder_bias
    dec_hidden = jax.nn.silu(pre_dec)
    sdf_values = jnp.sum(dec_hidden * decoder_out, axis=-1)
    whole_count = voxels * devices
    error_sdf = sdf_values - target
    loss_part = jnp.sum(error_sdf * error_sdf) / (2.0 * whole_count)
    grad_sdf = error_sdf / whole_count
    grad_out_part = jnp.sum(dec_hidden * grad_sdf[:, None], axis=0)
    _, pull_silu = jax.vjp(jax.nn.silu, pre_dec)
    grad_pre = pull_silu(grad_sdf[:, None] * decoder_out)[0]
    grad_bias_part = jnp.sum(grad_pre, axis=0)
    grad_pre_low = grad_pre.astype(jnp.bfloat16)
    grad_in_part = lax.dot_general(
        block_out, grad_pre_low, (((0,), (0,)), ((), ())), preferred_element_type=jnp.float32
    )
    grad_block = lax.dot_general(
        grad_pre_low, decoder_in, (((1,), (1,)), ((), ())), preferred_element_type=jnp.float32
    )
    _, pull_two = jax.vjp(lambda hidden: activate(hidden, gain_two), hidden_two)
    grad_hidden_two = pull_two(grad_block)[0].astype(jnp.bfloat16)
    grad_act_one, weight_grad_two = backward_conv(
        gathered_two, halo_two, kernel_map, conv_two, grad_hidden_two, border_hot, halo_target, border_list
    )
    _, pull_one = jax.vjp(lambda hidden: activate(hidden, gain_one), hidden_one)
    grad_hidden_one = pull_one(grad_act_one)[0].astype(jnp.bfloat16)
    input_part, weight_grad_one = backward_conv(
        gathered_one, halo_one, kernel_map, conv_one, grad_hidden_one, border_hot, halo_target, border_list
    )
    grad_x_zero = grad_block + input_part
    scaled = (grad_x_zero * inverse[:, None]).astype(jnp.bfloat16)
    slot_values = jnp.einsum(
        "sv,vc->sc", slot_match, scaled, preferred_element_type=jnp.float32
    ).astype(jnp.bfloat16)
    returned = return_grads(slot_values.reshape(devices, capacity, channels)).reshape(-1, channels)
    grad_points = jnp.einsum(
        "sp,sc->pc", slot_hot, returned, preferred_element_type=jnp.float32
    ).astype(jnp.bfloat16)
    parts = (weight_grad_one, weight_grad_two, grad_in_part, grad_bias_part, grad_out_part, loss_part)
    summed, grad_points = tree_psum(parts, grad_points)
    (
        grad_conv_one,
        grad_conv_two,
        grad_decoder_in,
        grad_decoder_bias,
        grad_decoder_out,
        loss_value,
    ) = summed
    return (
        sdf_values,
        loss_value,
        grad_conv_one,
        grad_conv_two,
        grad_decoder_in,
        grad_decoder_bias,
        grad_decoder_out,
        grad_points,
    )


def solution(mesh):
    in_specs = (
        P(("gx", "gy"), None),
        P(("gx", "gy"), None),
        P(("gx", "gy")),
        P(None, ("gx", "gy")),
        P("gx", "gy", None),
        P(),
        P(),
        P(),
        P(),
        P(),
        P(),
        P(),
        P(("gx", "gy")),
    )
    out_specs = (P(("gx", "gy")), P(), P(), P(), P(), P(), P(), P(("gx", "gy"), None))
    return jax.shard_map(local, mesh=mesh, in_specs=in_specs, out_specs=out_specs, check_vma=False)
```

```python
import math

import jax
import numpy as np
import jax.numpy as jnp
from jax import lax
from jax.experimental import pallas as pl
from jax.experimental.pallas import tpu as pltpu
from jax.sharding import PartitionSpec as P

EPS = 1e-05


def with_halo(array, sides, width):
    for axis, dim in sides:
        peers, length = (lax.axis_size(axis), array.shape[dim])
        up = [(i, (i + 1) % peers) for i in range(peers - 1)]
        down = [(j, i) for i, j in up]
        last = lax.slice_in_dim(array, length - width, length, axis=dim)
        leading = lax.slice_in_dim(array, 0, width, axis=dim)
        before = lax.ppermute(last, axis, up)
        after = lax.ppermute(leading, axis, down)
        array = jnp.concatenate([before, array, after], axis=dim)
    return array


def activate(hidden, gain_vec):
    inverse_rms = lax.rsqrt(jnp.mean(hidden * hidden, axis=-1, keepdims=True) + EPS)
    return jax.nn.silu(hidden * inverse_rms * gain_vec)


def build_table(features, border_list):
    channels = features.shape[1]
    edge_rows = features[border_list]
    neighbour_rows = with_halo(edge_rows, (("gx", 0), ("gy", 1)), 1)
    zero_row = jnp.zeros((1, channels), features.dtype)
    return jnp.concatenate([features, neighbour_rows.reshape(-1, channels), zero_row], axis=0)


def gather_local(rows, kernel_map):
    voxels = rows.shape[0]
    local_rows = jnp.arange(voxels, dtype=jnp.int32)
    selector = (kernel_map[:, :, None] == local_rows[None, None, :]).astype(rows.dtype)
    picked = jnp.einsum("kvu,uc->kvc", selector, rows, preferred_element_type=jnp.float32)
    return picked.astype(rows.dtype)


def pair_gather_kernel(map_ref, rows_ref, rows_t_ref, low_ref, high_ref):
    voxels = rows_ref.shape[0]
    pairs = low_ref.shape[0]
    rows = rows_ref[...]
    rows_t = rows_t_ref[...]
    local_rows = lax.broadcasted_iota(jnp.int32, (voxels, voxels), 1)
    for k in range(pairs):
        selector = (map_ref[:, k:k + 1] == local_rows).astype(rows.dtype)
        low_ref[k] = jnp.dot(selector, rows, preferred_element_type=jnp.float32).astype(low_ref.dtype)
        high_ref[pairs - 1 - k] = jnp.dot(rows_t, selector, preferred_element_type=jnp.float32).astype(high_ref.dtype)


def gather_pairs(rows, map_t):
    voxels, channels = rows.shape
    pairs = map_t.shape[1]
    return pl.pallas_call(
        pair_gather_kernel,
        out_shape=(
            jax.ShapeDtypeStruct((pairs, voxels, channels), rows.dtype),
            jax.ShapeDtypeStruct((pairs, channels, voxels), rows.dtype),
        ),
        in_specs=[pl.BlockSpec(memory_space=pltpu.VMEM)] * 3,
        out_specs=(pl.BlockSpec(memory_space=pltpu.VMEM), pl.BlockSpec(memory_space=pltpu.VMEM)),
        compiler_params=pltpu.CompilerParams(vmem_limit_bytes=48 * 1024 * 1024),
        cost_estimate=pl.CostEstimate(
            flops=4 * pairs * voxels * voxels * channels,
            bytes_accessed=2 * (2 * pairs + 2) * voxels * channels + 4 * pairs * voxels,
            transcendentals=0,
        ),
    )(map_t, rows, jnp.transpose(rows))


def pair_conv(low, rows, high, weight):
    pairs = low.shape[0]
    return (
        jnp.einsum("kvc,kcd->vd", low, weight[:pairs], preferred_element_type=jnp.float32)
        + jnp.dot(rows, weight[pairs], preferred_element_type=jnp.float32)
        + jnp.einsum("kcv,kcd->vd", high, weight[pairs + 1:], preferred_element_type=jnp.float32)
    )


def halo_layout(kernel_map, border_list):
    voxels = kernel_map.shape[1]
    boundary = border_list.shape[2]
    border_flat = border_list.reshape(-1)
    border_hot = (jnp.arange(voxels, dtype=jnp.int32)[:, None] == border_flat[None, :])
    named = jnp.einsum(
        "kv,vb->kb",
        kernel_map.astype(jnp.float32),
        border_hot.astype(jnp.float32),
        precision=lax.Precision.HIGHEST,
    )
    expected = np.zeros((27, 2, 2, boundary), np.int32)
    for k in range(27):
        step_x, step_y = k // 9 - 1, k // 3 % 3 - 1
        for i in range(2):
            for j in range(2):
                cell = (i + 1 + step_x) * 4 + (j + 1 + step_y)
                expected[k, i, j] = cell * boundary + np.arange(boundary)
    expected = jnp.asarray(expected.reshape(27, -1))
    flag = named == (expected + voxels).astype(jnp.float32)
    target = jnp.where(flag, expected, -1)
    return border_hot, target


def halo_hot(target, halo_count):
    return target[:, :, None] == jnp.arange(halo_count, dtype=jnp.int32)[None, None, :]


def halo_pick(halo, target):
    channels = halo.shape[-1]
    flat = halo.reshape(-1, channels)
    picked = jnp.einsum(
        "kbr,rc->kbc",
        halo_hot(target, flat.shape[0]).astype(flat.dtype),
        flat,
        preferred_element_type=jnp.float32,
    )
    return picked.astype(halo.dtype)


def edge_halo(features, border_hot, border_list):
    channels = features.shape[1]
    edge_rows = jnp.einsum(
        "vb,vc->bc", border_hot.astype(features.dtype), features, preferred_element_type=jnp.float32
    ).astype(features.dtype)
    edge_rows = edge_rows.reshape(border_list.shape + (channels,))
    return with_halo(edge_rows, (("gx", 0), ("gy", 1)), 1)


def conv_forward(features, kernel_map, border_list, border_hot, target, weight):
    low, high = gather_pairs(features, jnp.transpose(kernel_map[: kernel_map.shape[0] // 2]))
    halo_rows = halo_pick(edge_halo(features, border_hot, border_list), target)
    local_out = pair_conv(low, features, high, weight)
    border_out = jnp.einsum("kbc,kcd->bd", halo_rows, weight, preferred_element_type=jnp.float32)
    placed = jnp.einsum(
        "vb,bd->vd", border_hot.astype(jnp.float32), border_out, precision=lax.Precision.HIGHEST
    )
    return local_out + placed, (low, features, high), halo_rows


def backward_conv(gathered, halo_rows, kernel_map, weight, grad_rows, border_hot, target, border_list):
    grad_border = jnp.einsum(
        "vb,vd->bd", border_hot.astype(grad_rows.dtype), grad_rows, preferred_element_type=jnp.float32
    ).astype(grad_rows.dtype)
    low, centre, high = gathered
    pairs = low.shape[0]
    weight_grad = jnp.concatenate(
        [
            jnp.einsum("kvc,vd->kcd", low, grad_rows, preferred_element_type=jnp.float32),
            jnp.einsum("vc,vd->cd", centre, grad_rows, preferred_element_type=jnp.float32)[None],
            jnp.einsum("kcv,vd->kcd", high, grad_rows, preferred_element_type=jnp.float32),
        ],
        axis=0,
    ) + jnp.einsum("kbc,bd->kcd", halo_rows, grad_border, preferred_element_type=jnp.float32)
    flipped_weight = jnp.swapaxes(weight[::-1], 1, 2)
    grad_low, grad_high = gather_pairs(grad_rows, jnp.transpose(kernel_map[: kernel_map.shape[0] // 2]))
    local_part = pair_conv(grad_low, grad_rows, grad_high, flipped_weight)
    channels = grad_rows.shape[1]
    boundary = border_list.shape[2]
    spread = jnp.einsum(
        "kbr,bd->rkd",
        halo_hot(target, 16 * boundary).astype(grad_border.dtype),
        grad_border,
        preferred_element_type=jnp.float32,
    ).astype(grad_border.dtype)
    halo_grad = jnp.einsum(
        "rkd,kcd->rc", spread, weight, preferred_element_type=jnp.float32
    ).reshape(4, 4, boundary, channels)
    rows_end = jnp.stack([halo_grad[0], halo_grad[3]], axis=0)
    cols_end = jnp.stack([halo_grad[:, 0], halo_grad[:, 3]], axis=1)
    corner_end = jnp.stack([rows_end[:, 0], rows_end[:, 3]], axis=1)
    payload = jnp.stack([rows_end[:, 1:3], cols_end[1:3], corner_end], axis=2)
    received = with_halo(payload.astype(jnp.bfloat16), (("gx", 0), ("gy", 1)), 1).astype(
        payload.dtype
    )
    from_rows = jnp.stack([received[0, 1:3, 0], received[3, 1:3, 0]], axis=0)
    from_cols = jnp.stack([received[1:3, 0, 1], received[1:3, 3, 1]], axis=1)
    corner_low = jnp.stack([received[0, 0, 2], received[0, 3, 2]], axis=0)
    corner_high = jnp.stack([received[3, 0, 2], received[3, 3, 2]], axis=0)
    from_corner = jnp.stack([corner_low, corner_high], axis=0)
    folded = halo_grad[1:3, 1:3] + from_rows + from_cols + from_corner
    result = local_part + jnp.einsum(
        "vb,bd->vd",
        border_hot.astype(jnp.float32),
        folded.reshape(-1, channels),
        precision=lax.Precision.HIGHEST,
    )
    return (result, weight_grad)


HALVING_STEPS = (("gy", 1), ("gy", 2), ("gx", 1))
DOUBLING_STEPS = (("gx", 4), ("gy", 4), ("gx", 2), ("gx", 8))


def tree_psum(parts, tie):
    flat = jnp.concatenate([jnp.ravel(p).astype(jnp.float32) for p in parts])
    lanes = 128
    rows = -(-flat.shape[0] // lanes)
    rows = -(-rows // (8 * 2 ** len(HALVING_STEPS))) * (8 * 2 ** len(HALVING_STEPS))
    x = jnp.pad(flat, (0, rows * lanes - flat.shape[0])).reshape(rows, lanes)
    bits = []
    for axis, mask in HALVING_STEPS:
        peers = lax.axis_size(axis)
        bit = (lax.axis_index(axis) // mask) % 2
        bits.append(bit)
        half = x.shape[0] // 2
        send = lax.dynamic_slice_in_dim(x, (1 - bit) * half, half, axis=0)
        keep = lax.dynamic_slice_in_dim(x, bit * half, half, axis=0)
        x = keep + lax.ppermute(send, axis, [(i, i ^ mask) for i in range(peers)])
    for axis, mask in DOUBLING_STEPS:
        peers = lax.axis_size(axis)
        other = lax.ppermute(x, axis, [(i, i ^ mask) for i in range(peers)])
        x = x + other
    x, tie = lax.optimization_barrier((x, tie))
    for (axis, mask), bit in reversed(list(zip(HALVING_STEPS, bits))):
        peers = lax.axis_size(axis)
        other = lax.ppermute(x, axis, [(i, i ^ mask) for i in range(peers)])
        half = x.shape[0]
        both = lax.dynamic_update_slice_in_dim(jnp.concatenate([other, other]), x, bit * half, axis=0)
        x = both
    flat = x.reshape(-1)
    out, start = [], 0
    for p in parts:
        size = math.prod(p.shape)
        out.append(flat[start:start + size].reshape(p.shape))
        start += size
    return tuple(out), tie


def slot_positions(destination, devices, capacity):
    points = destination.shape[0]
    block = math.gcd(points, 128)
    blocks = points // block
    dest_hot = destination[:, None] == jnp.arange(devices, dtype=jnp.int32)[None, :]
    grouped = dest_hot.astype(jnp.bfloat16).reshape(blocks, block, devices)
    lower = (
        jnp.arange(block, dtype=jnp.int32)[:, None] > jnp.arange(block, dtype=jnp.int32)[None, :]
    ).astype(jnp.bfloat16)
    within = jnp.einsum("ij,bjd->bid", lower, grouped, preferred_element_type=jnp.float32)
    totals = jnp.sum(grouped.astype(jnp.float32), axis=1)
    lower_blocks = (
        jnp.arange(blocks, dtype=jnp.int32)[:, None] > jnp.arange(blocks, dtype=jnp.int32)[None, :]
    ).astype(jnp.float32)
    offsets = jnp.einsum("ab,bd->ad", lower_blocks, totals, precision=lax.Precision.HIGHEST)
    earlier = (within + offsets[:, None, :]).reshape(points, devices)
    rank = jnp.sum(jnp.where(dest_hot, earlier, 0.0), axis=1).astype(jnp.int32)
    return destination * capacity + rank


def send_points(send_rows):
    return lax.all_to_all(send_rows, ("gx", "gy"), split_axis=0, concat_axis=0, tiled=True)


def return_grads(slot_grads):
    returned = lax.all_to_all(slot_grads, ("gx", "gy"), split_axis=0, concat_axis=0, tiled=True)
    return returned


def local(
    point_feats,
    point_dest,
    point_voxel,
    kernel_map,
    border_list,
    conv_one,
    conv_two,
    gain_one,
    gain_two,
    decoder_in,
    decoder_bias,
    decoder_out,
    target,
):
    devices = lax.axis_size("gx") * lax.axis_size("gy")
    voxels = kernel_map.shape[1]
    points, channels = point_feats.shape
    capacity = 2 * points // devices
    destination = point_dest[:, 0]
    position = slot_positions(destination, devices, capacity)
    slot_hot = (
        jnp.arange(devices * capacity, dtype=jnp.int32)[:, None] == position[None, :]
    ).astype(jnp.bfloat16)
    id_high = (point_voxel // 32 + 1).astype(jnp.bfloat16)
    id_low = (point_voxel % 32).astype(jnp.bfloat16)
    payload = jnp.concatenate(
        [
            point_feats,
            jnp.ones((points, 1), jnp.bfloat16),
            id_high[:, None],
            id_low[:, None],
        ],
        axis=1,
    )
    send = jnp.einsum(
        "sp,pc->sc", slot_hot, payload, preferred_element_type=jnp.float32
    ).astype(jnp.bfloat16)
    got = send_points(send.reshape(devices, capacity, channels + 3)).reshape(-1, channels + 3)
    flat_ids = ((got[:, channels + 1].astype(jnp.float32) - 1.0) * 32.0 + got[:, channels + 2].astype(jnp.float32)).astype(jnp.int32)
    voxel_rows = jnp.arange(voxels, dtype=jnp.int32)
    slot_match = (flat_ids[:, None] == voxel_rows[None, :]).astype(jnp.bfloat16)
    pooled = jnp.einsum(
        "sv,sc->vc", slot_match, got[:, : channels + 1], preferred_element_type=jnp.float32
    )
    pooled_sum = pooled[:, :channels]
    counts = pooled[:, channels]
    inverse = 1.0 / jnp.maximum(counts, 1.0)
    x_zero = (pooled_sum * inverse[:, None]).astype(jnp.bfloat16)
    border_hot, halo_target = halo_layout(kernel_map, border_list)
    hidden_one, gathered_one, halo_one = conv_forward(
        x_zero, kernel_map, border_list, border_hot, halo_target, conv_one
    )
    act_one = activate(hidden_one, gain_one).astype(jnp.bfloat16)
    hidden_two, gathered_two, halo_two = conv_forward(
        act_one, kernel_map, border_list, border_hot, halo_target, conv_two
    )
    block_out = (x_zero.astype(jnp.float32) + activate(hidden_two, gain_two)).astype(jnp.bfloat16)
    pre_dec = jnp.dot(block_out, decoder_in, preferred_element_type=jnp.float32) + decoder_bias
    dec_hidden = jax.nn.silu(pre_dec)
    sdf_values = jnp.sum(dec_hidden * decoder_out, axis=-1)
    whole_count = voxels * devices
    error_sdf = sdf_values - target
    loss_part = jnp.sum(error_sdf * error_sdf) / (2.0 * whole_count)
    grad_sdf = error_sdf / whole_count
    grad_out_part = jnp.sum(dec_hidden * grad_sdf[:, None], axis=0)
    _, pull_silu = jax.vjp(jax.nn.silu, pre_dec)
    grad_pre = pull_silu(grad_sdf[:, None] * decoder_out)[0]
    grad_bias_part = jnp.sum(grad_pre, axis=0)
    grad_pre_low = grad_pre.astype(jnp.bfloat16)
    grad_in_part = lax.dot_general(
        block_out, grad_pre_low, (((0,), (0,)), ((), ())), preferred_element_type=jnp.float32
    )
    grad_block = lax.dot_general(
        grad_pre_low, decoder_in, (((1,), (1,)), ((), ())), preferred_element_type=jnp.float32
    )
    _, pull_two = jax.vjp(lambda hidden: activate(hidden, gain_two), hidden_two)
    grad_hidden_two = pull_two(grad_block)[0].astype(jnp.bfloat16)
    grad_act_one, weight_grad_two = backward_conv(
        gathered_two, halo_two, kernel_map, conv_two, grad_hidden_two, border_hot, halo_target, border_list
    )
    _, pull_one = jax.vjp(lambda hidden: activate(hidden, gain_one), hidden_one)
    grad_hidden_one = pull_one(grad_act_one)[0].astype(jnp.bfloat16)
    input_part, weight_grad_one = backward_conv(
        gathered_one, halo_one, kernel_map, conv_one, grad_hidden_one, border_hot, halo_target, border_list
    )
    grad_x_zero = grad_block + input_part
    scaled = (grad_x_zero * inverse[:, None]).astype(jnp.bfloat16)
    slot_values = jnp.einsum(
        "sv,vc->sc", slot_match, scaled, preferred_element_type=jnp.float32
    ).astype(jnp.bfloat16)
    returned = return_grads(slot_values.reshape(devices, capacity, channels)).reshape(-1, channels)
    grad_points = jnp.einsum(
        "sp,sc->pc", slot_hot, returned, preferred_element_type=jnp.float32
    ).astype(jnp.bfloat16)
    parts = (weight_grad_one, weight_grad_two, grad_in_part, grad_bias_part, grad_out_part, loss_part)
    summed, grad_points = tree_psum(parts, grad_points)
    (
        grad_conv_one,
        grad_conv_two,
        grad_decoder_in,
        grad_decoder_bias,
        grad_decoder_out,
        loss_value,
    ) = summed
    return (
        sdf_values,
        loss_value,
        grad_conv_one,
        grad_conv_two,
        grad_decoder_in,
        grad_decoder_bias,
        grad_decoder_out,
        grad_points,
    )


def solution(mesh):
    in_specs = (
        P(("gx", "gy"), None),
        P(("gx", "gy"), None),
        P(("gx", "gy")),
        P(None, ("gx", "gy")),
        P("gx", "gy", None),
        P(),
        P(),
        P(),
        P(),
        P(),
        P(),
        P(),
        P(("gx", "gy")),
    )
    out_specs = (P(("gx", "gy")), P(), P(), P(), P(), P(), P(), P(("gx", "gy"), None))
    return jax.shard_map(local, mesh=mesh, in_specs=in_specs, out_specs=out_specs, check_vma=False)
```

```python
import math

import jax
import numpy as np
import jax.numpy as jnp
from jax import lax
from jax.experimental import pallas as pl
from jax.experimental.pallas import tpu as pltpu
from jax.sharding import PartitionSpec as P

EPS = 1e-05


def with_halo(array, sides, width):
    for axis, dim in sides:
        peers, length = (lax.axis_size(axis), array.shape[dim])
        up = [(i, (i + 1) % peers) for i in range(peers - 1)]
        down = [(j, i) for i, j in up]
        last = lax.slice_in_dim(array, length - width, length, axis=dim)
        leading = lax.slice_in_dim(array, 0, width, axis=dim)
        before = lax.ppermute(last, axis, up)
        after = lax.ppermute(leading, axis, down)
        array = jnp.concatenate([before, array, after], axis=dim)
    return array


def activate(hidden, gain_vec):
    inverse_rms = lax.rsqrt(jnp.mean(hidden * hidden, axis=-1, keepdims=True) + EPS)
    return jax.nn.silu(hidden * inverse_rms * gain_vec)


def build_table(features, border_list):
    channels = features.shape[1]
    edge_rows = features[border_list]
    neighbour_rows = with_halo(edge_rows, (("gx", 0), ("gy", 1)), 1)
    zero_row = jnp.zeros((1, channels), features.dtype)
    return jnp.concatenate([features, neighbour_rows.reshape(-1, channels), zero_row], axis=0)


def gather_local(rows, kernel_map):
    voxels = rows.shape[0]
    local_rows = jnp.arange(voxels, dtype=jnp.int32)
    selector = (kernel_map[:, :, None] == local_rows[None, None, :]).astype(rows.dtype)
    picked = jnp.einsum("kvu,uc->kvc", selector, rows, preferred_element_type=jnp.float32)
    return picked.astype(rows.dtype)


def pair_gather_kernel(map_ref, rows_ref, rows_t_ref, low_ref, high_ref):
    voxels = rows_ref.shape[0]
    pairs = low_ref.shape[0]
    rows = rows_ref[...]
    rows_t = rows_t_ref[...]
    local_rows = lax.broadcasted_iota(jnp.int32, (voxels, voxels), 1)
    for k in range(pairs):
        selector = (map_ref[:, k:k + 1] == local_rows).astype(rows.dtype)
        low_ref[k] = jnp.dot(selector, rows, preferred_element_type=jnp.float32).astype(low_ref.dtype)
        high_ref[pairs - 1 - k] = jnp.dot(rows_t, selector, preferred_element_type=jnp.float32).astype(high_ref.dtype)


def gather_pairs(rows, map_t):
    voxels, channels = rows.shape
    pairs = map_t.shape[1]
    return pl.pallas_call(
        pair_gather_kernel,
        out_shape=(
            jax.ShapeDtypeStruct((pairs, voxels, channels), rows.dtype),
            jax.ShapeDtypeStruct((pairs, channels, voxels), rows.dtype),
        ),
        in_specs=[pl.BlockSpec(memory_space=pltpu.VMEM)] * 3,
        out_specs=(pl.BlockSpec(memory_space=pltpu.VMEM), pl.BlockSpec(memory_space=pltpu.VMEM)),
        compiler_params=pltpu.CompilerParams(vmem_limit_bytes=48 * 1024 * 1024),
        cost_estimate=pl.CostEstimate(
            flops=4 * pairs * voxels * voxels * channels,
            bytes_accessed=2 * (2 * pairs + 2) * voxels * channels + 4 * pairs * voxels,
            transcendentals=0,
        ),
    )(map_t, rows, jnp.transpose(rows))


def pair_conv(low, rows, high, weight):
    pairs = low.shape[0]
    return (
        jnp.einsum("kvc,kcd->vd", low, weight[:pairs], preferred_element_type=jnp.float32)
        + jnp.dot(rows, weight[pairs], preferred_element_type=jnp.float32)
        + jnp.einsum("kcv,kcd->vd", high, weight[pairs + 1:], preferred_element_type=jnp.float32)
    )


def halo_layout(kernel_map, border_list):
    voxels = kernel_map.shape[1]
    boundary = border_list.shape[2]
    border_flat = border_list.reshape(-1)
    border_hot = (jnp.arange(voxels, dtype=jnp.int32)[:, None] == border_flat[None, :])
    named = jnp.einsum(
        "kv,vb->kb",
        kernel_map.astype(jnp.float32),
        border_hot.astype(jnp.float32),
        precision=lax.Precision.HIGHEST,
    )
    expected = np.zeros((27, 2, 2, boundary), np.int32)
    for k in range(27):
        step_x, step_y = k // 9 - 1, k // 3 % 3 - 1
        for i in range(2):
            for j in range(2):
                cell = (i + 1 + step_x) * 4 + (j + 1 + step_y)
                expected[k, i, j] = cell * boundary + np.arange(boundary)
    expected = jnp.asarray(expected.reshape(27, -1))
    flag = named == (expected + voxels).astype(jnp.float32)
    target = jnp.where(flag, expected, -1)
    return border_hot, target


def halo_hot(target, halo_count):
    return target[:, :, None] == jnp.arange(halo_count, dtype=jnp.int32)[None, None, :]


def halo_pick(halo, target):
    channels = halo.shape[-1]
    flat = halo.reshape(-1, channels)
    picked = jnp.einsum(
        "kbr,rc->kbc",
        halo_hot(target, flat.shape[0]).astype(flat.dtype),
        flat,
        preferred_element_type=jnp.float32,
    )
    return picked.astype(halo.dtype)


def edge_halo(features, border_hot, border_list):
    channels = features.shape[1]
    edge_rows = jnp.einsum(
        "vb,vc->bc", border_hot.astype(features.dtype), features, preferred_element_type=jnp.float32
    ).astype(features.dtype)
    edge_rows = edge_rows.reshape(border_list.shape + (channels,))
    return with_halo(edge_rows, (("gx", 0), ("gy", 1)), 1)


def place_rows(border_hot, values):
    hot = border_hot.astype(jnp.bfloat16)
    high = values.astype(jnp.bfloat16)
    rest = values - high.astype(jnp.float32)
    middle = rest.astype(jnp.bfloat16)
    low = (rest - middle.astype(jnp.float32)).astype(jnp.bfloat16)
    total = jnp.einsum("vb,bd->vd", hot, high, preferred_element_type=jnp.float32)
    total = total + jnp.einsum("vb,bd->vd", hot, middle, preferred_element_type=jnp.float32)
    return total + jnp.einsum("vb,bd->vd", hot, low, preferred_element_type=jnp.float32)


def conv_forward(features, kernel_map, border_list, border_hot, target, weight):
    low, high = gather_pairs(features, jnp.transpose(kernel_map[: kernel_map.shape[0] // 2]))
    halo_rows = halo_pick(edge_halo(features, border_hot, border_list), target)
    local_out = pair_conv(low, features, high, weight)
    border_out = jnp.einsum("kbc,kcd->bd", halo_rows, weight, preferred_element_type=jnp.float32)
    placed = place_rows(border_hot, border_out)
    return local_out + placed, (low, features, high), halo_rows


def backward_conv(gathered, halo_rows, kernel_map, weight, grad_rows, border_hot, target, border_list):
    grad_border = jnp.einsum(
        "vb,vd->bd", border_hot.astype(grad_rows.dtype), grad_rows, preferred_element_type=jnp.float32
    ).astype(grad_rows.dtype)
    low, centre, high = gathered
    pairs = low.shape[0]
    weight_grad = jnp.concatenate(
        [
            jnp.einsum("kvc,vd->kcd", low, grad_rows, preferred_element_type=jnp.float32),
            jnp.einsum("vc,vd->cd", centre, grad_rows, preferred_element_type=jnp.float32)[None],
            jnp.einsum("kcv,vd->kcd", high, grad_rows, preferred_element_type=jnp.float32),
        ],
        axis=0,
    ) + jnp.einsum("kbc,bd->kcd", halo_rows, grad_border, preferred_element_type=jnp.float32)
    flipped_weight = jnp.swapaxes(weight[::-1], 1, 2)
    grad_low, grad_high = gather_pairs(grad_rows, jnp.transpose(kernel_map[: kernel_map.shape[0] // 2]))
    local_part = pair_conv(grad_low, grad_rows, grad_high, flipped_weight)
    channels = grad_rows.shape[1]
    boundary = border_list.shape[2]
    spread = jnp.einsum(
        "kbr,bd->rkd",
        halo_hot(target, 16 * boundary).astype(grad_border.dtype),
        grad_border,
        preferred_element_type=jnp.float32,
    ).astype(grad_border.dtype)
    halo_grad = jnp.einsum(
        "rkd,kcd->rc", spread, weight, preferred_element_type=jnp.float32
    ).reshape(4, 4, boundary, channels)
    rows_end = jnp.stack([halo_grad[0], halo_grad[3]], axis=0)
    cols_end = jnp.stack([halo_grad[:, 0], halo_grad[:, 3]], axis=1)
    corner_end = jnp.stack([rows_end[:, 0], rows_end[:, 3]], axis=1)
    payload = jnp.stack([rows_end[:, 1:3], cols_end[1:3], corner_end], axis=2)
    received = with_halo(payload.astype(jnp.bfloat16), (("gx", 0), ("gy", 1)), 1).astype(
        payload.dtype
    )
    from_rows = jnp.stack([received[0, 1:3, 0], received[3, 1:3, 0]], axis=0)
    from_cols = jnp.stack([received[1:3, 0, 1], received[1:3, 3, 1]], axis=1)
    corner_low = jnp.stack([received[0, 0, 2], received[0, 3, 2]], axis=0)
    corner_high = jnp.stack([received[3, 0, 2], received[3, 3, 2]], axis=0)
    from_corner = jnp.stack([corner_low, corner_high], axis=0)
    folded = halo_grad[1:3, 1:3] + from_rows + from_cols + from_corner
    result = local_part + place_rows(border_hot, folded.reshape(-1, channels))
    return (result, weight_grad)


HALVING_STEPS = (("gy", 1), ("gy", 2), ("gx", 1))
DOUBLING_STEPS = (("gx", 4), ("gy", 4), ("gx", 2), ("gx", 8))


def tree_psum(parts, tie):
    flat = jnp.concatenate([jnp.ravel(p).astype(jnp.float32) for p in parts])
    lanes = 128
    rows = -(-flat.shape[0] // lanes)
    rows = -(-rows // (8 * 2 ** len(HALVING_STEPS))) * (8 * 2 ** len(HALVING_STEPS))
    x = jnp.pad(flat, (0, rows * lanes - flat.shape[0])).reshape(rows, lanes)
    bits = []
    for axis, mask in HALVING_STEPS:
        peers = lax.axis_size(axis)
        bit = (lax.axis_index(axis) // mask) % 2
        bits.append(bit)
        half = x.shape[0] // 2
        send = lax.dynamic_slice_in_dim(x, (1 - bit) * half, half, axis=0)
        keep = lax.dynamic_slice_in_dim(x, bit * half, half, axis=0)
        x = keep + lax.ppermute(send, axis, [(i, i ^ mask) for i in range(peers)])
    for axis, mask in DOUBLING_STEPS:
        peers = lax.axis_size(axis)
        other = lax.ppermute(x, axis, [(i, i ^ mask) for i in range(peers)])
        x = x + other
    x, tie = lax.optimization_barrier((x, tie))
    for (axis, mask), bit in reversed(list(zip(HALVING_STEPS, bits))):
        peers = lax.axis_size(axis)
        other = lax.ppermute(x, axis, [(i, i ^ mask) for i in range(peers)])
        half = x.shape[0]
        both = lax.dynamic_update_slice_in_dim(jnp.concatenate([other, other]), x, bit * half, axis=0)
        x = both
    flat = x.reshape(-1)
    out, start = [], 0
    for p in parts:
        size = math.prod(p.shape)
        out.append(flat[start:start + size].reshape(p.shape))
        start += size
    return tuple(out), tie


def slot_positions(destination, devices, capacity):
    points = destination.shape[0]
    block = math.gcd(points, 128)
    blocks = points // block
    dest_hot = destination[:, None] == jnp.arange(devices, dtype=jnp.int32)[None, :]
    grouped = dest_hot.astype(jnp.bfloat16).reshape(blocks, block, devices)
    lower = (
        jnp.arange(block, dtype=jnp.int32)[:, None] > jnp.arange(block, dtype=jnp.int32)[None, :]
    ).astype(jnp.bfloat16)
    within = jnp.einsum("ij,bjd->bid", lower, grouped, preferred_element_type=jnp.float32)
    totals = jnp.sum(grouped.astype(jnp.float32), axis=1)
    lower_blocks = (
        jnp.arange(blocks, dtype=jnp.int32)[:, None] > jnp.arange(blocks, dtype=jnp.int32)[None, :]
    ).astype(jnp.float32)
    offsets = jnp.einsum("ab,bd->ad", lower_blocks, totals, precision=lax.Precision.HIGHEST)
    earlier = (within + offsets[:, None, :]).reshape(points, devices)
    rank = jnp.sum(jnp.where(dest_hot, earlier, 0.0), axis=1).astype(jnp.int32)
    return destination * capacity + rank


def send_points(send_rows):
    return lax.all_to_all(send_rows, ("gx", "gy"), split_axis=0, concat_axis=0, tiled=True)


def return_grads(slot_grads):
    returned = lax.all_to_all(slot_grads, ("gx", "gy"), split_axis=0, concat_axis=0, tiled=True)
    return returned


def local(
    point_feats,
    point_dest,
    point_voxel,
    kernel_map,
    border_list,
    conv_one,
    conv_two,
    gain_one,
    gain_two,
    decoder_in,
    decoder_bias,
    decoder_out,
    target,
):
    devices = lax.axis_size("gx") * lax.axis_size("gy")
    voxels = kernel_map.shape[1]
    points, channels = point_feats.shape
    capacity = 2 * points // devices
    destination = point_dest[:, 0]
    position = slot_positions(destination, devices, capacity)
    slot_hot = (
        jnp.arange(devices * capacity, dtype=jnp.int32)[:, None] == position[None, :]
    ).astype(jnp.bfloat16)
    id_high = (point_voxel // 32 + 1).astype(jnp.bfloat16)
    id_low = (point_voxel % 32).astype(jnp.bfloat16)
    payload = jnp.concatenate(
        [
            point_feats,
            jnp.ones((points, 1), jnp.bfloat16),
            id_high[:, None],
            id_low[:, None],
        ],
        axis=1,
    )
    send = jnp.einsum(
        "sp,pc->sc", slot_hot, payload, preferred_element_type=jnp.float32
    ).astype(jnp.bfloat16)
    got = send_points(send.reshape(devices, capacity, channels + 3)).reshape(-1, channels + 3)
    flat_ids = ((got[:, channels + 1].astype(jnp.float32) - 1.0) * 32.0 + got[:, channels + 2].astype(jnp.float32)).astype(jnp.int32)
    voxel_rows = jnp.arange(voxels, dtype=jnp.int32)
    slot_match = (flat_ids[:, None] == voxel_rows[None, :]).astype(jnp.bfloat16)
    pooled = jnp.einsum(
        "sv,sc->vc", slot_match, got[:, : channels + 1], preferred_element_type=jnp.float32
    )
    pooled_sum = pooled[:, :channels]
    counts = pooled[:, channels]
    inverse = 1.0 / jnp.maximum(counts, 1.0)
    x_zero = (pooled_sum * inverse[:, None]).astype(jnp.bfloat16)
    border_hot, halo_target = halo_layout(kernel_map, border_list)
    hidden_one, gathered_one, halo_one = conv_forward(
        x_zero, kernel_map, border_list, border_hot, halo_target, conv_one
    )
    act_one = activate(hidden_one, gain_one).astype(jnp.bfloat16)
    hidden_two, gathered_two, halo_two = conv_forward(
        act_one, kernel_map, border_list, border_hot, halo_target, conv_two
    )
    block_out = (x_zero.astype(jnp.float32) + activate(hidden_two, gain_two)).astype(jnp.bfloat16)
    pre_dec = jnp.dot(block_out, decoder_in, preferred_element_type=jnp.float32) + decoder_bias
    dec_hidden = jax.nn.silu(pre_dec)
    sdf_values = jnp.sum(dec_hidden * decoder_out, axis=-1)
    whole_count = voxels * devices
    error_sdf = sdf_values - target
    loss_part = jnp.sum(error_sdf * error_sdf) / (2.0 * whole_count)
    grad_sdf = error_sdf / whole_count
    grad_out_part = jnp.sum(dec_hidden * grad_sdf[:, None], axis=0)
    _, pull_silu = jax.vjp(jax.nn.silu, pre_dec)
    grad_pre = pull_silu(grad_sdf[:, None] * decoder_out)[0]
    grad_bias_part = jnp.sum(grad_pre, axis=0)
    grad_pre_low = grad_pre.astype(jnp.bfloat16)
    grad_in_part = lax.dot_general(
        block_out, grad_pre_low, (((0,), (0,)), ((), ())), preferred_element_type=jnp.float32
    )
    grad_block = lax.dot_general(
        grad_pre_low, decoder_in, (((1,), (1,)), ((), ())), preferred_element_type=jnp.float32
    )
    _, pull_two = jax.vjp(lambda hidden: activate(hidden, gain_two), hidden_two)
    grad_hidden_two = pull_two(grad_block)[0].astype(jnp.bfloat16)
    grad_act_one, weight_grad_two = backward_conv(
        gathered_two, halo_two, kernel_map, conv_two, grad_hidden_two, border_hot, halo_target, border_list
    )
    _, pull_one = jax.vjp(lambda hidden: activate(hidden, gain_one), hidden_one)
    grad_hidden_one = pull_one(grad_act_one)[0].astype(jnp.bfloat16)
    input_part, weight_grad_one = backward_conv(
        gathered_one, halo_one, kernel_map, conv_one, grad_hidden_one, border_hot, halo_target, border_list
    )
    grad_x_zero = grad_block + input_part
    scaled = (grad_x_zero * inverse[:, None]).astype(jnp.bfloat16)
    slot_values = jnp.einsum(
        "sv,vc->sc", slot_match, scaled, preferred_element_type=jnp.float32
    ).astype(jnp.bfloat16)
    returned = return_grads(slot_values.reshape(devices, capacity, channels)).reshape(-1, channels)
    grad_points = jnp.einsum(
        "sp,sc->pc", slot_hot, returned, preferred_element_type=jnp.float32
    ).astype(jnp.bfloat16)
    parts = (weight_grad_one, weight_grad_two, grad_in_part, grad_bias_part, grad_out_part, loss_part)
    summed, grad_points = tree_psum(parts, grad_points)
    (
        grad_conv_one,
        grad_conv_two,
        grad_decoder_in,
        grad_decoder_bias,
        grad_decoder_out,
        loss_value,
    ) = summed
    return (
        sdf_values,
        loss_value,
        grad_conv_one,
        grad_conv_two,
        grad_decoder_in,
        grad_decoder_bias,
        grad_decoder_out,
        grad_points,
    )


def solution(mesh):
    in_specs = (
        P(("gx", "gy"), None),
        P(("gx", "gy"), None),
        P(("gx", "gy")),
        P(None, ("gx", "gy")),
        P("gx", "gy", None),
        P(),
        P(),
        P(),
        P(),
        P(),
        P(),
        P(),
        P(("gx", "gy")),
    )
    out_specs = (P(("gx", "gy")), P(), P(), P(), P(), P(), P(), P(("gx", "gy"), None))
    return jax.shard_map(local, mesh=mesh, in_specs=in_specs, out_specs=out_specs, check_vma=False)
```
